32 devices in a mesh: leaf: 8 (over z, y), coef: 4 (over x, core).
Axes of the slice: x: 2, y: 2, z: 4, core: 2. Of those that a mesh axis runs over, the one named last changes fastest.
Arguments:
- vectors: float32 [16, 16384], P(None, ('leaf', 'coef')), may hold values from -6 to 6
- sigma_point: float32 [1], replicated, may hold values from 0.5 to 1.5
- leaf_basis: bfloat16 [128, 64, 128], P(('leaf', 'coef')), may hold values from -0.5 to 0.5
- near_blocks: bfloat16 [3, 128, 8, 128, 128], P(None, ('leaf', 'coef')), may hold values from -0.109375 to 0.109375
- near_list: int32 [128, 8], P(('leaf', 'coef')), may hold values from 0 to 127, as said below
- coupling: bfloat16 [3, 128, 16, 4096], P(None, 'leaf', 'coef'), may hold values from -0.1875 to 0.1875
- far_list: int32 [128, 16], P('leaf', 'coef'), may hold values from 0 to 127, as said below
- far_rank: int32 [128, 16], P('leaf', 'coef'), may hold values from 0 to 64, as said below
- krylov: float32 [64, 16384], P(None, ('leaf', 'coef')), as said below
Outputs:
- new_block: float32 [16, 16384], P(None, ('leaf', 'coef'))
- coeffs: float32 [64, 16], replicated
- chol_factor: float32 [16, 16], replicated
The draws below stay inside these ranges and needn't reach their ends.
Inputs may be any that keep to these rules, and one draw needn't show every extreme that they name: near_list[c, 0] = c, and every entry names a cluster held by the same device as c or by the device just before or after it in the order of leaf+coef, 4 consecutive clusters a device. `far_list`: every entry of cluster c names a cluster whose group (clusters taken 16 at a time) is at most 2 groups from the group of c. `far_rank`: 0 marks a padded slot. The rows of krylov are orthonormal.
All inputs are finite; a program needn't handle non-finite values.
Results may differ from the reference program's by a relative error of at most 0.008.
Values may be sent and summed in bfloat16 or wider, within the bound.
No kernel may reach another device: no remote copies, remote signals or barrier semaphores. Data moves between devices by JAX's collectives and lax.ppermute only.
A program may use at most 64 MiB of HBM per device.

```python
import jax
import jax.numpy as jnp
from jax import lax

LEAF = 128
RANK = 64
NV = 16
BASIS = 64
NEAR = 8
FAR = 16
CL_DEV = 4
CLG = 16
CLUSTERS = 128
NPTS = 16384
REACH = 2


def draw_near_list(key, part):
    device_count = CLUSTERS // CL_DEV
    cluster_ids = jnp.arange(CLUSTERS, dtype=jnp.int32)
    device_pos = cluster_ids // CL_DEV
    low_bound = jnp.maximum(device_pos - 1, 0) * CL_DEV
    high_bound = jnp.minimum(device_pos + 2, device_count) * CL_DEV
    next_low = jnp.minimum(device_pos + 1, device_count - 1) * CL_DEV
    key_one, key_two, key_three = jax.random.split(jax.random.fold_in(key, 11), 3)
    before = jax.random.randint(key_one, (CLUSTERS,), low_bound, low_bound + CL_DEV)
    after = jax.random.randint(key_two, (CLUSTERS,), next_low, next_low + CL_DEV)
    others = jax.random.randint(key_three, (CLUSTERS, NEAR - 3), low_bound[:, None], high_bound[:, None])
    return jnp.concatenate([cluster_ids[:, None], before[:, None], after[:, None], others], axis=1).astype(jnp.int32)


def draw_far_list(key, part):
    group_count = CLUSTERS // CLG
    cluster_ids = jnp.arange(CLUSTERS, dtype=jnp.int32)
    group_pos = cluster_ids // CLG
    low_group = jnp.maximum(group_pos - REACH, 0)
    high_group = jnp.minimum(group_pos + REACH, group_count - 1)
    key_one, key_two, key_three = jax.random.split(jax.random.fold_in(key, 23), 3)
    anywhere = jax.random.randint(key_one, (CLUSTERS, FAR), (low_group * CLG)[:, None], ((high_group + 1) * CLG)[:, None])
    lowest = jax.random.randint(key_two, (CLUSTERS,), low_group * CLG, (low_group + 1) * CLG)
    highest_pick = jax.random.randint(key_three, (CLUSTERS,), high_group * CLG, (high_group + 1) * CLG)
    anywhere = anywhere.at[:, 1].set(lowest).at[:, 2].set(highest_pick)
    return anywhere.astype(jnp.int32)


def draw_far_rank(key, part):
    key_one, key_two = jax.random.split(jax.random.fold_in(key, 37), 2)
    ranks = jax.random.randint(key_one, (CLUSTERS, FAR), 1, RANK + 1)
    padded = jax.random.randint(key_two, (CLUSTERS, FAR), 0, 4) == 0
    ranks = jnp.where(padded, 0, ranks)
    ranks = ranks.at[:, 0].set(RANK)
    return ranks.astype(jnp.int32)


def draw_krylov(key, part):
    key_one, key_two = jax.random.split(jax.random.fold_in(key, 41), 2)
    freqs = jax.random.permutation(key_one, NPTS)[:BASIS].astype(jnp.int32)
    point_signs = (jax.random.randint(key_two, (NPTS,), 0, 2) * 2 - 1).astype(jnp.int32)
    point_ids = jnp.arange(NPTS, dtype=jnp.int32)
    shared = jnp.bitwise_and(freqs[:, None], point_ids[None, :])
    parity = jnp.zeros((BASIS, NPTS), jnp.int32)
    bit_count = NPTS.bit_length() - 1
    for bit_pos in range(bit_count):
        parity = parity + jnp.bitwise_and(jnp.right_shift(shared, bit_pos), 1)
    walsh_sign = 1 - 2 * (parity % 2)
    values = (walsh_sign * point_signs[None, :]).astype(jnp.float32) / jnp.sqrt(jnp.float32(NPTS))
    return values.astype(jnp.float32)


def block_scale(stream_key, dims, cuts, low, largest):
    level, own = 1.0, jax.random.fold_in(stream_key, 6)
    for position, shards_of in cuts:
        steps = jnp.exp(jax.random.uniform(jax.random.fold_in(own, position), (shards_of,), jnp.float32, low / len(cuts), largest / len(cuts)))
        level = level * jnp.repeat(steps, dims[position] // shards_of).reshape([-1 if axis == position else 1 for axis in range(len(dims))])
    return level


def scatter_about(key, shape, deviation, most, cuts=(), held_as=jnp.bfloat16):
    level = block_scale(key, shape, cuts, -0.22, 0.18) if cuts else 1.0
    drawn = jax.random.normal(key, shape, jnp.float32) * deviation * level
    return jnp.minimum(jnp.maximum(drawn, -most), most).astype(held_as)


def setup_inputs(seed: int = 0) -> dict:
    streams_of = jax.random.split(jax.random.key(seed), 10)
    return {
        "vectors": scatter_about(streams_of[0], (NV, NPTS), 1.0, 6.0, ((1, 32),), jnp.float32),
        "sigma_point": jnp.clip(jax.random.uniform(streams_of[1], (1,), jnp.float32, 0.5, 1.5), 0.5, 1.5),
        "leaf_basis": scatter_about(streams_of[2], (CLUSTERS, RANK, LEAF), LEAF ** -0.5, 0.5, ((0, 32),)),
        "near_blocks": scatter_about(streams_of[3], (3, CLUSTERS, NEAR, LEAF, LEAF), (3 * NEAR * LEAF) ** -0.5, 0.109375, ((1, 32),)),
        "near_list": draw_near_list(jax.random.fold_in(streams_of[9], 71), 0),
        "coupling": scatter_about(streams_of[5], (3, CLUSTERS, FAR, RANK * RANK), (FAR * RANK) ** -0.5, 0.1875, ((1, 8), (2, 4))),
        "far_list": draw_far_list(jax.random.fold_in(streams_of[9], 71), 0),
        "far_rank": draw_far_rank(jax.random.fold_in(streams_of[9], 71), 0),
        "krylov": draw_krylov(jax.random.fold_in(streams_of[9], 71), 0),
    }


def reference(vectors, sigma_point, leaf_basis, near_blocks, near_list, coupling, far_list, far_rank, krylov):
    highest = lax.Precision.HIGHEST
    sigma_val = sigma_point[0].astype(jnp.float32)
    powers = jnp.stack([jnp.ones((), jnp.float32), sigma_val, sigma_val * sigma_val])
    rounded = vectors.astype(jnp.bfloat16)
    by_cluster = rounded.reshape(NV, CLUSTERS, LEAF)
    coarse = jnp.einsum('cki,vci->cvk', leaf_basis.astype(jnp.float32), by_cluster.astype(jnp.float32), precision=highest).astype(jnp.bfloat16)
    lane_ids = jnp.arange(RANK, dtype=jnp.int32)

    def one_group(group_idx):
        first_row = (group_idx * CLG).astype(jnp.int32)
        far_ids = lax.dynamic_slice_in_dim(far_list, first_row, CLG, 0)
        block_ranks = lax.dynamic_slice_in_dim(far_rank, first_row, CLG, 0)
        keep_mask = (lane_ids[None, None, :] < block_ranks[:, :, None]).astype(jnp.float32)
        sources = coarse[far_ids].astype(jnp.float32) * keep_mask[:, :, None, :]
        couple = lax.dynamic_slice_in_dim(coupling, first_row, CLG, 1).astype(jnp.float32).reshape(3, CLG, FAR, RANK, RANK)
        far_terms = jnp.einsum('jcfkl,cfvl->jcfvk', couple, sources, precision=highest)
        combined = jnp.tensordot(powers, far_terms, 1) * keep_mask[:, :, None, :]
        far_hat = jnp.sum(combined, axis=1)
        near_ids = lax.dynamic_slice_in_dim(near_list, first_row, CLG, 0)
        near_src = jnp.take(by_cluster, near_ids, axis=1).astype(jnp.float32)
        blocks = lax.dynamic_slice_in_dim(near_blocks, first_row, CLG, 1).astype(jnp.float32)
        near_terms = jnp.einsum('jcnil,vcnl->jvci', blocks, near_src, precision=highest)
        return (far_hat, jnp.tensordot(powers, near_terms, 1))
    groups = CLUSTERS // CLG
    far_hat, near_part = lax.map(one_group, jnp.arange(groups, dtype=jnp.int32))
    far_round = far_hat.reshape(CLUSTERS, NV, RANK).astype(jnp.bfloat16)
    near_part = jnp.transpose(near_part, (1, 0, 2, 3)).reshape(NV, CLUSTERS, LEAF)
    far_part = jnp.einsum('cki,cvk->vci', leaf_basis.astype(jnp.float32), far_round.astype(jnp.float32), precision=highest)
    applied = (far_part + near_part).reshape(NV, NPTS)
    coeffs = jnp.dot(krylov, applied.T, precision=highest)
    residue = applied - jnp.dot(coeffs.T, krylov, precision=highest)
    gram_matrix = jnp.dot(residue, residue.T, precision=highest) / NPTS
    chol_factor = jnp.linalg.cholesky(gram_matrix)
    new_block = jax.scipy.linalg.solve_triangular(chol_factor, residue, lower=True)
    return (new_block, coeffs, chol_factor)
```

```python
import jax
import jax.numpy as jnp
from jax import lax
from jax.sharding import PartitionSpec as P


def shifted(block, axis, distance):
    devices = range(lax.axis_size(axis))
    route = [(i - distance, i) for i in devices if i - distance in devices]
    return lax.ppermute(block, axis, route)


def extended_2(block, sides, width):
    for axis, dim in sides:
        count = lax.axis_size(axis)
        forward = [(i, i + 1) for i in range(count - 1)]
        backward = [(target, source) for source, target in forward]
        low = lax.ppermute(
            lax.slice_in_dim(block, block.shape[dim] - width, None, axis=dim), axis, forward
        )
        high = lax.ppermute(lax.slice_in_dim(block, 0, width, axis=dim), axis, backward)
        block = jnp.concatenate([low, block, high], axis=dim)
    return block


def is_power_of_two(count):
    return count > 0 and count & (count - 1) == 0


def butterfly_sum(block, axes):
    total = 1
    for axis in axes:
        total *= lax.axis_size(axis)
    if not is_power_of_two(total):
        return lax.psum(block, axes)
    distance = 1
    while distance < total:
        route = [(i, i ^ distance) for i in range(total)]
        block = block + lax.ppermute(block, axes, route)
        distance *= 2
    return block


def butterfly_scatter(block, axis):
    count = lax.axis_size(axis)
    if not is_power_of_two(count):
        return lax.psum_scatter(block, axis, scatter_dimension=0, tiled=True)
    me = lax.axis_index(axis)
    parts = block.reshape(count, -1, *block.shape[1:])
    distance = 1
    while distance < count:
        bit = (me // distance) % 2
        pairs = parts.reshape(parts.shape[0] // 2, 2, *parts.shape[1:])
        keep = lax.dynamic_index_in_dim(pairs, bit, axis=1, keepdims=False)
        give = lax.dynamic_index_in_dim(pairs, 1 - bit, axis=1, keepdims=False)
        route = [(i, i ^ distance) for i in range(count)]
        parts = keep + lax.ppermute(give, axis, route)
        distance *= 2
    return parts.reshape(-1, *block.shape[1:])


def group_reach(grouped, offsets):
    pieces = []
    for offset in offsets:
        if offset == 0:
            pieces.append(grouped)
        else:
            pieces.append(shifted(grouped, "leaf", -offset))
    return jnp.concatenate(pieces, axis=0)


def on_device(
    vectors, sigma_point, leaf_basis, near_blocks, near_list, coupling, far_list, far_rank, krylov
):
    highest = lax.Precision.HIGHEST
    local_count, rank_width, leaf_size = leaf_basis.shape
    vec_count = vectors.shape[0]
    near_count = near_list.shape[1]
    slot_count = far_list.shape[1]
    coef_count = lax.axis_size("coef")
    leaf_count = lax.axis_size("leaf")
    group_size = local_count * coef_count
    reach_groups = min(8, leaf_count // 4)
    total_points = local_count * leaf_size * coef_count * leaf_count
    sigma_val = sigma_point[0]
    powers = jnp.stack([jnp.ones((), jnp.float32), sigma_val, sigma_val * sigma_val])
    rounded = vectors.astype(jnp.bfloat16)
    by_cluster = rounded.reshape(vec_count, local_count, leaf_size)
    coarse = jnp.einsum(
        "cki,vci->cvk", leaf_basis, by_cluster, preferred_element_type=jnp.float32
    ).astype(jnp.bfloat16)
    own_rows = coarse.reshape(1, local_count, vec_count * rank_width)
    offsets = list(range(-reach_groups, reach_groups + 1))
    grouped = lax.all_gather(own_rows, "coef", axis=1, tiled=True)
    window = group_reach(grouped, offsets)
    flat_rows = window.reshape(-1, vec_count * rank_width)
    group_pos = lax.axis_index("leaf")
    local_ids = (far_list - (group_pos - reach_groups) * group_size).reshape(-1)
    sources = jnp.take(flat_rows, local_ids, axis=0).reshape(
        group_size, slot_count, vec_count, rank_width
    )
    lane_ids = jnp.arange(rank_width, dtype=jnp.int32)
    keep_mask = lane_ids[None, None, :] < far_rank[:, :, None]
    sources = jnp.where(keep_mask[:, :, None, :], sources, jnp.zeros((), jnp.bfloat16))
    couple = coupling.reshape(3, group_size, slot_count, rank_width, rank_width)
    far_terms = jnp.einsum("jcfkl,cfvl->jcfvk", couple, sources, preferred_element_type=jnp.float32)
    combined = jnp.tensordot(powers, far_terms, 1) * keep_mask[:, :, None, :].astype(jnp.float32)
    partial_far = jnp.sum(combined, axis=1).reshape(group_size, vec_count * rank_width)
    far_hat = butterfly_scatter(partial_far, "coef")
    far_round = far_hat.astype(jnp.bfloat16).reshape(local_count, vec_count, rank_width)
    far_part = jnp.einsum("cki,cvk->vci", leaf_basis, far_round, preferred_element_type=jnp.float32)
    extended = extended_2(rounded, ((("leaf", "coef"), 1),), local_count * leaf_size)
    extended = extended.reshape(vec_count, 3 * local_count, leaf_size)
    device_pos = lax.axis_index("leaf") * coef_count + lax.axis_index("coef")
    near_ids = (near_list - (device_pos - 1) * local_count).reshape(-1)
    near_src = jnp.take(extended, near_ids, axis=1).reshape(
        vec_count, local_count, near_count, leaf_size
    )
    near_terms = jnp.einsum(
        "jcnil,vcnl->jvci", near_blocks, near_src, preferred_element_type=jnp.float32
    )
    near_part = jnp.tensordot(powers, near_terms, 1)
    applied = (far_part + near_part).reshape(vec_count, local_count * leaf_size)
    basis_count = krylov.shape[0]
    both_axes = ("leaf", "coef")
    proj_part = jnp.dot(krylov, applied.T, precision=highest)
    self_part = jnp.dot(applied, applied.T, precision=highest)
    summed = butterfly_sum(jnp.concatenate([proj_part, self_part], axis=0), both_axes)
    coeffs = summed[:basis_count]
    outer = summed[basis_count:]
    residue = applied - jnp.dot(coeffs.T, krylov, precision=highest)
    short_gram = (outer - jnp.dot(coeffs.T, coeffs, precision=highest)) / total_points
    kept = jnp.diagonal(short_gram) * (64 * total_points) >= jnp.diagonal(outer)
    def exact_gram():
        part = jnp.dot(residue, residue.T, precision=highest)
        return butterfly_sum(part, both_axes) / total_points
    gram_matrix = lax.cond(jnp.all(kept), lambda: short_gram, exact_gram)
    chol_factor = jnp.linalg.cholesky(gram_matrix)
    new_block = jax.scipy.linalg.solve_triangular(chol_factor, residue, lower=True)
    return (new_block, coeffs, chol_factor)


def solution(mesh):
    in_specs = (
        P(None, ("leaf", "coef")),
        P(),
        P(("leaf", "coef"), None, None),
        P(None, ("leaf", "coef"), None, None, None),
        P(("leaf", "coef"), None),
        P(None, "leaf", "coef", None),
        P("leaf", "coef"),
        P("leaf", "coef"),
        P(None, ("leaf", "coef")),
    )
    out_specs = (P(None, ("leaf", "coef")), P(), P())
    return jax.shard_map(
        on_device, mesh=mesh, in_specs=in_specs, out_specs=out_specs, check_vma=False
    )
```

```python
import jax
import jax.numpy as jnp
from jax import lax
from jax.sharding import PartitionSpec as P


def shifted(block, axis, distance):
    devices = range(lax.axis_size(axis))
    route = [(i - distance, i) for i in devices if i - distance in devices]
    return lax.ppermute(block, axis, route)


def extended_2(block, sides, width):
    for axis, dim in sides:
        count = lax.axis_size(axis)
        forward = [(i, i + 1) for i in range(count - 1)]
        backward = [(target, source) for source, target in forward]
        low = lax.ppermute(
            lax.slice_in_dim(block, block.shape[dim] - width, None, axis=dim), axis, forward
        )
        high = lax.ppermute(lax.slice_in_dim(block, 0, width, axis=dim), axis, backward)
        block = jnp.concatenate([low, block, high], axis=dim)
    return block


def is_power_of_two(count):
    return count > 0 and count & (count - 1) == 0


def butterfly_sum(block, axes):
    total = 1
    for axis in axes:
        total *= lax.axis_size(axis)
    if not is_power_of_two(total):
        return lax.psum(block, axes)
    distance = 1
    while distance < total:
        route = [(i, i ^ distance) for i in range(total)]
        block = block + lax.ppermute(block, axes, route)
        distance *= 2
    return block


def butterfly_gather(block, axes):
    total = 1
    for axis in axes:
        total *= lax.axis_size(axis)
    if not is_power_of_two(total):
        return lax.all_gather(block, axes, axis=0, tiled=True)
    me = lax.axis_index(axes[0])
    for axis in axes[1:]:
        me = me * lax.axis_size(axis) + lax.axis_index(axis)
    distance = 1
    while distance < total:
        route = [(i, i ^ distance) for i in range(total)]
        other = lax.ppermute(block, axes, route)
        upper = (me // distance) % 2 == 1
        block = jnp.where(
            upper, jnp.concatenate([other, block], axis=0), jnp.concatenate([block, other], axis=0)
        )
        distance *= 2
    return block


def butterfly_scatter(block, axis):
    count = lax.axis_size(axis)
    if not is_power_of_two(count):
        return lax.psum_scatter(block, axis, scatter_dimension=0, tiled=True)
    me = lax.axis_index(axis)
    parts = block.reshape(count, -1, *block.shape[1:])
    distance = 1
    while distance < count:
        bit = (me // distance) % 2
        pairs = parts.reshape(parts.shape[0] // 2, 2, *parts.shape[1:])
        keep = lax.dynamic_index_in_dim(pairs, bit, axis=1, keepdims=False)
        give = lax.dynamic_index_in_dim(pairs, 1 - bit, axis=1, keepdims=False)
        route = [(i, i ^ distance) for i in range(count)]
        parts = keep + lax.ppermute(give, axis, route)
        distance *= 2
    return parts.reshape(-1, *block.shape[1:])


def group_reach(grouped, offsets):
    pieces = []
    for offset in offsets:
        if offset == 0:
            pieces.append(grouped)
        else:
            pieces.append(shifted(grouped, "leaf", -offset))
    return jnp.concatenate(pieces, axis=0)


def on_device(
    vectors, sigma_point, leaf_basis, near_blocks, near_list, coupling, far_list, far_rank, krylov
):
    highest = lax.Precision.HIGHEST
    local_count, rank_width, leaf_size = leaf_basis.shape
    vec_count = vectors.shape[0]
    near_count = near_list.shape[1]
    slot_count = far_list.shape[1]
    coef_count = lax.axis_size("coef")
    leaf_count = lax.axis_size("leaf")
    group_size = local_count * coef_count
    reach_groups = min(8, leaf_count // 4)
    total_points = local_count * leaf_size * coef_count * leaf_count
    sigma_val = sigma_point[0]
    powers = jnp.stack([jnp.ones((), jnp.float32), sigma_val, sigma_val * sigma_val])
    rounded = vectors.astype(jnp.bfloat16)
    by_cluster = rounded.reshape(vec_count, local_count, leaf_size)
    coarse = jnp.einsum(
        "cki,vci->cvk", leaf_basis, by_cluster, preferred_element_type=jnp.float32
    ).astype(jnp.bfloat16)
    all_rows = butterfly_gather(coarse.reshape(local_count, vec_count * rank_width), ("leaf", "coef"))
    sources = jnp.take(all_rows, far_list.reshape(-1), axis=0).reshape(
        group_size, slot_count, vec_count, rank_width
    )
    lane_ids = jnp.arange(rank_width, dtype=jnp.int32)
    keep_mask = lane_ids[None, None, :] < far_rank[:, :, None]
    sources = jnp.where(keep_mask[:, :, None, :], sources, jnp.zeros((), jnp.bfloat16))
    lane_width = 128
    halves = lane_width // rank_width
    tiles = rank_width * rank_width // lane_width
    wide_lanes = jnp.arange(lane_width, dtype=jnp.int32)
    spread = jnp.tile(jnp.swapaxes(sources, 2, 3), (1, 1, halves, 1))
    half_of_lane = (wide_lanes // rank_width)[:, None] == jnp.arange(halves, dtype=jnp.int32)[None, :]
    slot_eye = jnp.eye(slot_count, dtype=jnp.bool_)
    spread = jnp.where(
        slot_eye[None, :, None, :, None, None] & half_of_lane[None, None, :, None, :, None],
        spread[:, :, :, None, None, :],
        jnp.zeros((), jnp.bfloat16),
    ).reshape(group_size, slot_count, lane_width, slot_count * halves * vec_count)
    couple = jnp.swapaxes(coupling.reshape(3, group_size, slot_count, tiles, lane_width), 2, 3)
    far_terms = jnp.einsum("jchfL,cfLw->jchw", couple, spread, preferred_element_type=jnp.float32)
    far_terms = jnp.swapaxes(
        far_terms.reshape(3, group_size, tiles, slot_count, halves, vec_count), 2, 3
    ).reshape(3, group_size, slot_count, rank_width, vec_count)
    row_mask = keep_mask[:, :, :, None].astype(jnp.float32)
    combined = jnp.tensordot(powers, far_terms, 1) * row_mask
    partial_far = jnp.swapaxes(jnp.sum(combined, axis=1), 1, 2).reshape(
        group_size, vec_count * rank_width
    )
    far_hat = butterfly_scatter(partial_far, "coef")
    far_round = far_hat.astype(jnp.bfloat16).reshape(local_count, vec_count, rank_width)
    far_part = jnp.einsum("cki,cvk->vci", leaf_basis, far_round, preferred_element_type=jnp.float32)
    extended = extended_2(rounded, ((("leaf", "coef"), 1),), local_count * leaf_size)
    extended = extended.reshape(vec_count, 3 * local_count, leaf_size)
    device_pos = lax.axis_index("leaf") * coef_count + lax.axis_index("coef")
    near_ids = (near_list - (device_pos - 1) * local_count).reshape(-1)
    near_src = jnp.take(extended, near_ids, axis=1).reshape(
        vec_count, local_count, near_count, leaf_size
    )
    near_terms = jnp.einsum(
        "jcnil,vcnl->jvci", near_blocks, near_src, preferred_element_type=jnp.float32
    )
    near_part = jnp.tensordot(powers, near_terms, 1)
    applied = (far_part + near_part).reshape(vec_count, local_count * leaf_size)
    basis_count = krylov.shape[0]
    both_axes = ("leaf", "coef")
    proj_part = jnp.dot(krylov, applied.T, precision=highest)
    self_part = jnp.dot(applied, applied.T, precision=highest)
    summed = butterfly_sum(jnp.concatenate([proj_part, self_part], axis=0), both_axes)
    coeffs = summed[:basis_count]
    outer = summed[basis_count:]
    residue = applied - jnp.dot(coeffs.T, krylov, precision=highest)
    short_gram = (outer - jnp.dot(coeffs.T, coeffs, precision=highest)) / total_points
    kept = jnp.diagonal(short_gram) * (64 * total_points) >= jnp.diagonal(outer)
    def exact_gram():
        part = jnp.dot(residue, residue.T, precision=highest)
        return butterfly_sum(part, both_axes) / total_points
    gram_matrix = lax.cond(jnp.all(kept), lambda: short_gram, exact_gram)
    chol_factor = jnp.linalg.cholesky(gram_matrix)
    new_block = jax.scipy.linalg.solve_triangular(chol_factor, residue, lower=True)
    return (new_block, coeffs, chol_factor)


def solution(mesh):
    in_specs = (
        P(None, ("leaf", "coef")),
        P(),
        P(("leaf", "coef"), None, None),
        P(None, ("leaf", "coef"), None, None, None),
        P(("leaf", "coef"), None),
        P(None, "leaf", "coef", None),
        P("leaf", "coef"),
        P("leaf", "coef"),
        P(None, ("leaf", "coef")),
    )
    out_specs = (P(None, ("leaf", "coef")), P(), P())
    return jax.shard_map(
        on_device, mesh=mesh, in_specs=in_specs, out_specs=out_specs, check_vma=False
    )
```

```python
import jax
import jax.numpy as jnp
from jax import lax
from jax.sharding import PartitionSpec as P


def shifted(block, axis, distance):
    devices = range(lax.axis_size(axis))
    route = [(i - distance, i) for i in devices if i - distance in devices]
    return lax.ppermute(block, axis, route)


def extended_2(block, sides, width):
    for axis, dim in sides:
        count = lax.axis_size(axis)
        forward = [(i, i + 1) for i in range(count - 1)]
        backward = [(target, source) for source, target in forward]
        low = lax.ppermute(
            lax.slice_in_dim(block, block.shape[dim] - width, None, axis=dim), axis, forward
        )
        high = lax.ppermute(lax.slice_in_dim(block, 0, width, axis=dim), axis, backward)
        block = jnp.concatenate([low, block, high], axis=dim)
    return block


def is_power_of_two(count):
    return count > 0 and count & (count - 1) == 0


def butterfly_sum(block, axes):
    total = 1
    for axis in axes:
        total *= lax.axis_size(axis)
    if not is_power_of_two(total):
        return lax.psum(block, axes)
    distance = 1
    while distance < total:
        route = [(i, i ^ distance) for i in range(total)]
        block = block + lax.ppermute(block, axes, route)
        distance *= 2
    return block


def butterfly_scatter(block, axis):
    count = lax.axis_size(axis)
    if not is_power_of_two(count):
        return lax.psum_scatter(block, axis, scatter_dimension=0, tiled=True)
    me = lax.axis_index(axis)
    parts = block.reshape(count, -1, *block.shape[1:])
    distance = 1
    while distance < count:
        bit = (me // distance) % 2
        pairs = parts.reshape(parts.shape[0] // 2, 2, *parts.shape[1:])
        keep = lax.dynamic_index_in_dim(pairs, bit, axis=1, keepdims=False)
        give = lax.dynamic_index_in_dim(pairs, 1 - bit, axis=1, keepdims=False)
        route = [(i, i ^ distance) for i in range(count)]
        parts = keep + lax.ppermute(give, axis, route)
        distance *= 2
    return parts.reshape(-1, *block.shape[1:])


def group_reach(grouped, offsets):
    pieces = []
    for offset in offsets:
        if offset == 0:
            pieces.append(grouped)
        else:
            pieces.append(shifted(grouped, "leaf", -offset))
    return jnp.concatenate(pieces, axis=0)


def on_device(
    vectors, sigma_point, leaf_basis, near_blocks, near_list, coupling, far_list, far_rank, krylov
):
    highest = lax.Precision.HIGHEST
    local_count, rank_width, leaf_size = leaf_basis.shape
    vec_count = vectors.shape[0]
    near_count = near_list.shape[1]
    slot_count = far_list.shape[1]
    coef_count = lax.axis_size("coef")
    leaf_count = lax.axis_size("leaf")
    group_size = local_count * coef_count
    reach_groups = min(8, leaf_count // 4)
    total_points = local_count * leaf_size * coef_count * leaf_count
    sigma_val = sigma_point[0]
    powers = jnp.stack([jnp.ones((), jnp.float32), sigma_val, sigma_val * sigma_val])
    rounded = vectors.astype(jnp.bfloat16)
    by_cluster = rounded.reshape(vec_count, local_count, leaf_size)
    coarse = jnp.einsum(
        "cki,vci->cvk", leaf_basis, by_cluster, preferred_element_type=jnp.float32
    ).astype(jnp.bfloat16)
    own_rows = coarse.reshape(1, local_count, vec_count * rank_width)
    offsets = list(range(-reach_groups, reach_groups + 1))
    reached = group_reach(own_rows, offsets)
    window = lax.all_gather(reached, "coef", axis=1, tiled=True)
    flat_rows = window.reshape(-1, vec_count * rank_width)
    group_pos = lax.axis_index("leaf")
    local_ids = (far_list - (group_pos - reach_groups) * group_size).reshape(-1)
    sources = jnp.take(flat_rows, local_ids, axis=0).reshape(
        group_size, slot_count, vec_count, rank_width
    )
    lane_ids = jnp.arange(rank_width, dtype=jnp.int32)
    keep_mask = lane_ids[None, None, :] < far_rank[:, :, None]
    sources = jnp.where(keep_mask[:, :, None, :], sources, jnp.zeros((), jnp.bfloat16))
    couple = coupling.reshape(3, group_size, slot_count, rank_width, rank_width)
    far_terms = jnp.einsum("jcfkl,cfvl->jcfvk", couple, sources, preferred_element_type=jnp.float32)
    combined = jnp.tensordot(powers, far_terms, 1) * keep_mask[:, :, None, :].astype(jnp.float32)
    partial_far = jnp.sum(combined, axis=1).reshape(group_size, vec_count * rank_width)
    far_hat = butterfly_scatter(partial_far, "coef")
    far_round = far_hat.astype(jnp.bfloat16).reshape(local_count, vec_count, rank_width)
    far_part = jnp.einsum("cki,cvk->vci", leaf_basis, far_round, preferred_element_type=jnp.float32)
    extended = extended_2(rounded, ((("leaf", "coef"), 1),), local_count * leaf_size)
    extended = extended.reshape(vec_count, 3 * local_count, leaf_size)
    device_pos = lax.axis_index("leaf") * coef_count + lax.axis_index("coef")
    near_ids = (near_list - (device_pos - 1) * local_count).reshape(-1)
    near_src = jnp.take(extended, near_ids, axis=1).reshape(
        vec_count, local_count, near_count, leaf_size
    )
    near_terms = jnp.einsum(
        "jcnil,vcnl->jvci", near_blocks, near_src, preferred_element_type=jnp.float32
    )
    near_part = jnp.tensordot(powers, near_terms, 1)
    applied = (far_part + near_part).reshape(vec_count, local_count * leaf_size)
    basis_count = krylov.shape[0]
    both_axes = ("leaf", "coef")
    proj_part = jnp.dot(krylov, applied.T, precision=highest)
    self_part = jnp.dot(applied, applied.T, precision=highest)
    summed = butterfly_sum(jnp.concatenate([proj_part, self_part], axis=0), both_axes)
    coeffs = summed[:basis_count]
    outer = summed[basis_count:]
    residue = applied - jnp.dot(coeffs.T, krylov, precision=highest)
    short_gram = (outer - jnp.dot(coeffs.T, coeffs, precision=highest)) / total_points
    eye = jnp.eye(vec_count, dtype=jnp.bool_)
    short_diag = jnp.sum(jnp.where(eye, short_gram, 0.0), axis=0)
    outer_diag = jnp.sum(jnp.where(eye, outer, 0.0), axis=0)
    kept = short_diag * (64 * total_points) >= outer_diag
    def exact_gram():
        part = jnp.dot(residue, residue.T, precision=highest)
        return butterfly_sum(part, both_axes) / total_points
    gram_matrix = lax.cond(jnp.all(kept), lambda: short_gram, exact_gram)
    chol_factor = jnp.linalg.cholesky(gram_matrix)
    new_block = jax.scipy.linalg.solve_triangular(chol_factor, residue, lower=True)
    return (new_block, coeffs, chol_factor)


def solution(mesh):
    in_specs = (
        P(None, ("leaf", "coef")),
        P(),
        P(("leaf", "coef"), None, None),
        P(None, ("leaf", "coef"), None, None, None),
        P(("leaf", "coef"), None),
        P(None, "leaf", "coef", None),
        P("leaf", "coef"),
        P("leaf", "coef"),
        P(None, ("leaf", "coef")),
    )
    out_specs = (P(None, ("leaf", "coef")), P(), P())
    return jax.shard_map(
        on_device, mesh=mesh, in_specs=in_specs, out_specs=out_specs, check_vma=False
    )
```

```python
import jax
import jax.numpy as jnp
from jax import lax
from jax.experimental import pallas as pl
from jax.experimental.pallas import tpu as pltpu
from jax.sharding import PartitionSpec as P


def shifted(block, axis, distance):
    devices = range(lax.axis_size(axis))
    route = [(i - distance, i) for i in devices if i - distance in devices]
    return lax.ppermute(block, axis, route)


def extended_2(block, sides, width):
    for axis, dim in sides:
        count = lax.axis_size(axis)
        forward = [(i, i + 1) for i in range(count - 1)]
        backward = [(target, source) for source, target in forward]
        low = lax.ppermute(
            lax.slice_in_dim(block, block.shape[dim] - width, None, axis=dim), axis, forward
        )
        high = lax.ppermute(lax.slice_in_dim(block, 0, width, axis=dim), axis, backward)
        block = jnp.concatenate([low, block, high], axis=dim)
    return block


def is_power_of_two(count):
    return count > 0 and count & (count - 1) == 0


def butterfly_sum(block, axes):
    total = 1
    for axis in axes:
        total *= lax.axis_size(axis)
    if not is_power_of_two(total):
        return lax.psum(block, axes)
    distance = 1
    while distance < total:
        route = [(i, i ^ distance) for i in range(total)]
        block = block + lax.ppermute(block, axes, route)
        distance *= 2
    return block


def butterfly_scatter(block, axis):
    count = lax.axis_size(axis)
    if not is_power_of_two(count):
        return lax.psum_scatter(block, axis, scatter_dimension=0, tiled=True)
    me = lax.axis_index(axis)
    parts = block.reshape(count, -1, *block.shape[1:])
    distance = 1
    while distance < count:
        bit = (me // distance) % 2
        pairs = parts.reshape(parts.shape[0] // 2, 2, *parts.shape[1:])
        keep = lax.dynamic_index_in_dim(pairs, bit, axis=1, keepdims=False)
        give = lax.dynamic_index_in_dim(pairs, 1 - bit, axis=1, keepdims=False)
        route = [(i, i ^ distance) for i in range(count)]
        parts = keep + lax.ppermute(give, axis, route)
        distance *= 2
    return parts.reshape(-1, *block.shape[1:])


def group_reach(grouped, offsets):
    pieces = []
    for offset in offsets:
        if offset == 0:
            pieces.append(grouped)
        else:
            pieces.append(shifted(grouped, "leaf", -offset))
    return jnp.concatenate(pieces, axis=0)


def chol_solve_kernel(gram_ref, residue_ref, chol_ref, block_ref):
    left = gram_ref[...]
    size = left.shape[0]
    rows = lax.broadcasted_iota(jnp.int32, left.shape, 0)
    cols = lax.broadcasted_iota(jnp.int32, left.shape, 1)
    row_ids = lax.broadcasted_iota(jnp.int32, (size, 1), 0)
    col_ids = lax.broadcasted_iota(jnp.int32, (1, size), 1)
    low = jnp.zeros_like(left)
    for step in range(size):
        column = jnp.sum(jnp.where(cols == step, left, 0.0), axis=1, keepdims=True)
        row = jnp.sum(jnp.where(rows == step, left, 0.0), axis=0, keepdims=True)
        pivot = jnp.sum(jnp.where(row_ids == step, column, 0.0), axis=0, keepdims=True)
        root = jnp.sqrt(pivot)
        low_column = jnp.where(row_ids >= step, column / root, 0.0)
        low_row = jnp.where(col_ids >= step, row / root, 0.0)
        low = jnp.where(cols == step, low_column, low)
        left = left - low_column * low_row
    chol_ref[...] = low
    block = residue_ref[...]
    for step in range(size):
        low_column = jnp.sum(jnp.where(cols == step, low, 0.0), axis=1, keepdims=True)
        diagonal = jnp.sum(jnp.where(row_ids == step, low_column, 0.0), axis=0, keepdims=True)
        solved = jnp.sum(jnp.where(row_ids == step, block, 0.0), axis=0, keepdims=True) / diagonal
        block = jnp.where(
            row_ids == step, solved, jnp.where(row_ids > step, block - low_column * solved, block)
        )
    block_ref[...] = block


def chol_solve(gram_matrix, residue):
    size, width = residue.shape
    return pl.pallas_call(
        chol_solve_kernel,
        out_shape=(
            jax.ShapeDtypeStruct((size, size), jnp.float32),
            jax.ShapeDtypeStruct((size, width), jnp.float32),
        ),
        in_specs=[pl.BlockSpec(memory_space=pltpu.VMEM)] * 2,
        out_specs=(pl.BlockSpec(memory_space=pltpu.VMEM), pl.BlockSpec(memory_space=pltpu.VMEM)),
        cost_estimate=pl.CostEstimate(
            flops=4 * size * size * (size + width), bytes_accessed=8 * size * (size + width), transcendentals=size
        ),
    )(gram_matrix, residue)


def on_device(
    vectors, sigma_point, leaf_basis, near_blocks, near_list, coupling, far_list, far_rank, krylov
):
    highest = lax.Precision.HIGHEST
    local_count, rank_width, leaf_size = leaf_basis.shape
    vec_count = vectors.shape[0]
    near_count = near_list.shape[1]
    slot_count = far_list.shape[1]
    coef_count = lax.axis_size("coef")
    leaf_count = lax.axis_size("leaf")
    group_size = local_count * coef_count
    reach_groups = min(8, leaf_count // 4)
    total_points = local_count * leaf_size * coef_count * leaf_count
    sigma_val = sigma_point[0]
    powers = jnp.stack([jnp.ones((), jnp.float32), sigma_val, sigma_val * sigma_val])
    rounded = vectors.astype(jnp.bfloat16)
    by_cluster = rounded.reshape(vec_count, local_count, leaf_size)
    coarse = jnp.einsum(
        "cki,vci->cvk", leaf_basis, by_cluster, preferred_element_type=jnp.float32
    ).astype(jnp.bfloat16)
    own_rows = coarse.reshape(1, local_count, vec_count * rank_width)
    offsets = list(range(-reach_groups, reach_groups + 1))
    reached = group_reach(own_rows, offsets)
    window = lax.all_gather(reached, "coef", axis=1, tiled=True)
    flat_rows = window.reshape(-1, vec_count * rank_width)
    group_pos = lax.axis_index("leaf")
    local_ids = (far_list - (group_pos - reach_groups) * group_size).reshape(-1)
    sources = flat_rows.at[local_ids].get(mode="promise_in_bounds").reshape(
        group_size, slot_count, vec_count, rank_width
    )
    lane_ids = jnp.arange(rank_width, dtype=jnp.int32)
    keep_mask = lane_ids[None, None, :] < far_rank[:, :, None]
    sources = jnp.where(keep_mask[:, :, None, :], sources, jnp.zeros((), jnp.bfloat16))
    couple = coupling.reshape(3, group_size, slot_count, rank_width, rank_width)
    far_terms = jnp.einsum("jcfkl,cfvl->jcfvk", couple, sources, preferred_element_type=jnp.float32)
    combined = jnp.tensordot(powers, far_terms, 1) * keep_mask[:, :, None, :].astype(jnp.float32)
    partial_far = jnp.sum(combined, axis=1).reshape(group_size, vec_count * rank_width)
    far_hat = butterfly_scatter(partial_far, "coef")
    far_round = far_hat.astype(jnp.bfloat16).reshape(local_count, vec_count, rank_width)
    far_part = jnp.einsum("cki,cvk->vci", leaf_basis, far_round, preferred_element_type=jnp.float32)
    extended = extended_2(rounded, ((("leaf", "coef"), 1),), local_count * leaf_size)
    extended = extended.reshape(vec_count, 3 * local_count, leaf_size)
    device_pos = lax.axis_index("leaf") * coef_count + lax.axis_index("coef")
    near_ids = (near_list - (device_pos - 1) * local_count).reshape(-1)
    near_src = extended.at[:, near_ids].get(mode="promise_in_bounds").reshape(
        vec_count, local_count, near_count, leaf_size
    )
    near_terms = jnp.einsum(
        "jcnil,vcnl->jvci", near_blocks, near_src, preferred_element_type=jnp.float32
    )
    near_part = jnp.tensordot(powers, near_terms, 1)
    applied = (far_part + near_part).reshape(vec_count, local_count * leaf_size)
    basis_count = krylov.shape[0]
    both_axes = ("leaf", "coef")
    proj_part = jnp.dot(krylov, applied.T, precision=highest)
    self_part = jnp.dot(applied, applied.T, precision=highest)
    summed = butterfly_sum(jnp.concatenate([proj_part, self_part], axis=0), both_axes)
    coeffs = summed[:basis_count]
    outer = summed[basis_count:]
    residue = applied - jnp.dot(coeffs.T, krylov, precision=highest)
    short_gram = (outer - jnp.dot(coeffs.T, coeffs, precision=highest)) / total_points
    eye = jnp.eye(vec_count, dtype=jnp.bool_)
    short_diag = jnp.sum(jnp.where(eye, short_gram, 0.0), axis=0)
    outer_diag = jnp.sum(jnp.where(eye, outer, 0.0), axis=0)
    kept = short_diag * (64 * total_points) >= outer_diag
    def exact_gram():
        part = jnp.dot(residue, residue.T, precision=highest)
        return butterfly_sum(part, both_axes) / total_points
    gram_matrix = lax.cond(jnp.all(kept), lambda: short_gram, exact_gram)
    chol_factor, new_block = chol_solve(gram_matrix, residue)
    return (new_block, coeffs, chol_factor)


def solution(mesh):
    in_specs = (
        P(None, ("leaf", "coef")),
        P(),
        P(("leaf", "coef"), None, None),
        P(None, ("leaf", "coef"), None, None, None),
        P(("leaf", "coef"), None),
        P(None, "leaf", "coef", None),
        P("leaf", "coef"),
        P("leaf", "coef"),
        P(None, ("leaf", "coef")),
    )
    out_specs = (P(None, ("leaf", "coef")), P(), P())
    return jax.shard_map(
        on_device, mesh=mesh, in_specs=in_specs, out_specs=out_specs, check_vma=False
    )
```

```python
import jax
import jax.numpy as jnp
from jax import lax
from jax.experimental import pallas as pl
from jax.experimental.pallas import tpu as pltpu
from jax.sharding import PartitionSpec as P


def shifted(block, axis, distance):
    devices = range(lax.axis_size(axis))
    route = [(i - distance, i) for i in devices if i - distance in devices]
    return lax.ppermute(block, axis, route)


def extended_2(block, sides, width):
    for axis, dim in sides:
        count = lax.axis_size(axis)
        forward = [(i, i + 1) for i in range(count - 1)]
        backward = [(target, source) for source, target in forward]
        low = lax.ppermute(
            lax.slice_in_dim(block, block.shape[dim] - width, None, axis=dim), axis, forward
        )
        high = lax.ppermute(lax.slice_in_dim(block, 0, width, axis=dim), axis, backward)
        block = jnp.concatenate([low, block, high], axis=dim)
    return block


def is_power_of_two(count):
    return count > 0 and count & (count - 1) == 0


def butterfly_sum(block, axes):
    total = 1
    for axis in axes:
        total *= lax.axis_size(axis)
    if not is_power_of_two(total):
        return lax.psum(block, axes)
    distance = 1
    while distance < total:
        route = [(i, i ^ distance) for i in range(total)]
        block = block + lax.ppermute(block, axes, route)
        distance *= 2
    return block


def butterfly_scatter(block, axis):
    count = lax.axis_size(axis)
    if not is_power_of_two(count):
        return lax.psum_scatter(block, axis, scatter_dimension=0, tiled=True)
    me = lax.axis_index(axis)
    parts = block.reshape(count, -1, *block.shape[1:])
    distance = 1
    while distance < count:
        bit = (me // distance) % 2
        pairs = parts.reshape(parts.shape[0] // 2, 2, *parts.shape[1:])
        keep = lax.dynamic_index_in_dim(pairs, bit, axis=1, keepdims=False)
        give = lax.dynamic_index_in_dim(pairs, 1 - bit, axis=1, keepdims=False)
        route = [(i, i ^ distance) for i in range(count)]
        parts = keep + lax.ppermute(give, axis, route)
        distance *= 2
    return parts.reshape(-1, *block.shape[1:])


def group_reach(grouped, offsets):
    pieces = []
    for offset in offsets:
        if offset == 0:
            pieces.append(grouped)
        else:
            pieces.append(shifted(grouped, "leaf", -offset))
    return jnp.concatenate(pieces, axis=0)


def chol_solve_kernel(gram_ref, residue_ref, chol_ref, block_ref):
    left = gram_ref[...]
    size = left.shape[0]
    rows = lax.broadcasted_iota(jnp.int32, left.shape, 0)
    cols = lax.broadcasted_iota(jnp.int32, left.shape, 1)
    row_ids = lax.broadcasted_iota(jnp.int32, (size, 1), 0)
    col_ids = lax.broadcasted_iota(jnp.int32, (1, size), 1)
    low = jnp.zeros_like(left)
    for step in range(size):
        column = jnp.sum(jnp.where(cols == step, left, 0.0), axis=1, keepdims=True)
        row = jnp.sum(jnp.where(rows == step, left, 0.0), axis=0, keepdims=True)
        pivot = jnp.sum(jnp.where(row_ids == step, column, 0.0), axis=0, keepdims=True)
        root = jnp.sqrt(pivot)
        low_column = jnp.where(row_ids >= step, column / root, 0.0)
        low_row = jnp.where(col_ids >= step, row / root, 0.0)
        low = jnp.where(cols == step, low_column, low)
        left = left - low_column * low_row
    chol_ref[...] = low
    block = residue_ref[...]
    for step in range(size):
        low_column = jnp.sum(jnp.where(cols == step, low, 0.0), axis=1, keepdims=True)
        diagonal = jnp.sum(jnp.where(row_ids == step, low_column, 0.0), axis=0, keepdims=True)
        solved = jnp.sum(jnp.where(row_ids == step, block, 0.0), axis=0, keepdims=True) / diagonal
        block = jnp.where(
            row_ids == step, solved, jnp.where(row_ids > step, block - low_column * solved, block)
        )
    block_ref[...] = block


def chol_solve(gram_matrix, residue):
    size, width = residue.shape
    return pl.pallas_call(
        chol_solve_kernel,
        out_shape=(
            jax.ShapeDtypeStruct((size, size), jnp.float32),
            jax.ShapeDtypeStruct((size, width), jnp.float32),
        ),
        in_specs=[pl.BlockSpec(memory_space=pltpu.VMEM)] * 2,
        out_specs=(pl.BlockSpec(memory_space=pltpu.VMEM), pl.BlockSpec(memory_space=pltpu.VMEM)),
        cost_estimate=pl.CostEstimate(
            flops=4 * size * size * (size + width), bytes_accessed=8 * size * (size + width), transcendentals=size
        ),
    )(gram_matrix, residue)


def on_device(
    vectors, sigma_point, leaf_basis, near_blocks, near_list, coupling, far_list, far_rank, krylov
):
    highest = lax.Precision.HIGHEST
    local_count, rank_width, leaf_size = leaf_basis.shape
    vec_count = vectors.shape[0]
    near_count = near_list.shape[1]
    slot_count = far_list.shape[1]
    coef_count = lax.axis_size("coef")
    leaf_count = lax.axis_size("leaf")
    group_size = local_count * coef_count
    reach_groups = min(8, leaf_count // 4)
    total_points = local_count * leaf_size * coef_count * leaf_count
    sigma_val = sigma_point[0]
    powers = jnp.stack([jnp.ones((), jnp.float32), sigma_val, sigma_val * sigma_val])
    rounded = vectors.astype(jnp.bfloat16)
    by_cluster = rounded.reshape(vec_count, local_count, leaf_size)
    coarse = jnp.einsum(
        "cki,vci->cvk", leaf_basis, by_cluster, preferred_element_type=jnp.float32
    ).astype(jnp.bfloat16)
    own_rows = coarse.reshape(1, local_count, vec_count * rank_width)
    offsets = list(range(-reach_groups, reach_groups + 1))
    reached = group_reach(own_rows, offsets)
    reach_width = len(offsets) * vec_count * rank_width
    own_vectors = jnp.swapaxes(by_cluster, 0, 1).reshape(local_count, vec_count * leaf_size)
    packed = jnp.concatenate(
        [jnp.swapaxes(reached, 0, 1).reshape(local_count, reach_width), own_vectors], axis=1
    )
    gathered = lax.all_gather(packed, "coef", axis=0, tiled=True)
    flat_rows = gathered[:, :reach_width].reshape(group_size * len(offsets), vec_count * rank_width)
    group_pos = lax.axis_index("leaf")
    source_group = far_list // group_size - (group_pos - reach_groups)
    local_ids = ((far_list % group_size) * len(offsets) + source_group).reshape(-1)
    picks = (local_ids[:, None] == jnp.arange(flat_rows.shape[0], dtype=jnp.int32)[None, :])
    sources = jnp.dot(
        picks.astype(jnp.bfloat16), flat_rows, preferred_element_type=jnp.float32
    ).astype(jnp.bfloat16).reshape(group_size, slot_count, vec_count, rank_width)
    lane_ids = jnp.arange(rank_width, dtype=jnp.int32)
    keep_mask = lane_ids[None, None, :] < far_rank[:, :, None]
    sources = jnp.where(keep_mask[:, :, None, :], sources, jnp.zeros((), jnp.bfloat16))
    couple = coupling.reshape(3, group_size, slot_count, rank_width, rank_width)
    far_terms = jnp.einsum("jcfkl,cfvl->jcfvk", couple, sources, preferred_element_type=jnp.float32)
    combined = jnp.tensordot(powers, far_terms, 1) * keep_mask[:, :, None, :].astype(jnp.float32)
    partial_far = jnp.sum(combined, axis=1).reshape(group_size, vec_count * rank_width)
    far_hat = butterfly_scatter(partial_far, "coef")
    far_round = far_hat.astype(jnp.bfloat16).reshape(local_count, vec_count, rank_width)
    far_part = jnp.einsum("cki,cvk->vci", leaf_basis, far_round, preferred_element_type=jnp.float32)
    edge_route = []
    for group in range(leaf_count - 1):
        last = group * coef_count + coef_count - 1
        edge_route += [(last, last + 1), (last + 1, last)]
    edge_rows = lax.ppermute(own_vectors, ("leaf", "coef"), edge_route)
    table = jnp.concatenate([edge_rows, gathered[:, reach_width:]], axis=0).reshape(
        local_count + group_size, vec_count, leaf_size
    )
    coef_pos = lax.axis_index("coef")
    group_first = group_pos * group_size
    edge_first = jnp.where(coef_pos == 0, group_first - local_count, group_first + group_size)
    in_group = near_list // group_size == group_pos
    near_ids = jnp.where(in_group, local_count + near_list - group_first, near_list - edge_first)
    near_picks = (near_ids[:, :, None] == jnp.arange(table.shape[0], dtype=jnp.int32)[None, None, :])
    near_src = jnp.einsum(
        "cnr,rvl->vcnl", near_picks.astype(jnp.bfloat16), table, preferred_element_type=jnp.float32
    ).astype(jnp.bfloat16)
    near_terms = jnp.einsum(
        "jcnil,vcnl->jvci", near_blocks, near_src, preferred_element_type=jnp.float32
    )
    near_part = jnp.tensordot(powers, near_terms, 1)
    applied = (far_part + near_part).reshape(vec_count, local_count * leaf_size)
    basis_count = krylov.shape[0]
    both_axes = ("leaf", "coef")
    proj_part = jnp.dot(krylov, applied.T, precision=highest)
    self_part = jnp.dot(applied, applied.T, precision=highest)
    summed = butterfly_sum(jnp.concatenate([proj_part, self_part], axis=0), both_axes)
    coeffs = summed[:basis_count]
    outer = summed[basis_count:]
    residue = applied - jnp.dot(coeffs.T, krylov, precision=highest)
    short_gram = (outer - jnp.dot(coeffs.T, coeffs, precision=highest)) / total_points
    eye = jnp.eye(vec_count, dtype=jnp.bool_)
    short_diag = jnp.sum(jnp.where(eye, short_gram, 0.0), axis=0)
    outer_diag = jnp.sum(jnp.where(eye, outer, 0.0), axis=0)
    kept = short_diag * (64 * total_points) >= outer_diag
    def exact_gram():
        part = jnp.dot(residue, residue.T, precision=highest)
        return butterfly_sum(part, both_axes) / total_points
    gram_matrix = lax.cond(jnp.all(kept), lambda: short_gram, exact_gram)
    chol_factor, new_block = chol_solve(gram_matrix, residue)
    return (new_block, coeffs, chol_factor)


def solution(mesh):
    in_specs = (
        P(None, ("leaf", "coef")),
        P(),
        P(("leaf", "coef"), None, None),
        P(None, ("leaf", "coef"), None, None, None),
        P(("leaf", "coef"), None),
        P(None, "leaf", "coef", None),
        P("leaf", "coef"),
        P("leaf", "coef"),
        P(None, ("leaf", "coef")),
    )
    out_specs = (P(None, ("leaf", "coef")), P(), P())
    return jax.shard_map(
        on_device, mesh=mesh, in_specs=in_specs, out_specs=out_specs, check_vma=False
    )
```

```python
import jax
import jax.numpy as jnp
from jax import lax
from jax.experimental import pallas as pl
from jax.experimental.pallas import tpu as pltpu
from jax.sharding import PartitionSpec as P


def shifted(block, axis, distance):
    devices = range(lax.axis_size(axis))
    route = [(i - distance, i) for i in devices if i - distance in devices]
    return lax.ppermute(block, axis, route)


def extended_2(block, sides, width):
    for axis, dim in sides:
        count = lax.axis_size(axis)
        forward = [(i, i + 1) for i in range(count - 1)]
        backward = [(target, source) for source, target in forward]
        low = lax.ppermute(
            lax.slice_in_dim(block, block.shape[dim] - width, None, axis=dim), axis, forward
        )
        high = lax.ppermute(lax.slice_in_dim(block, 0, width, axis=dim), axis, backward)
        block = jnp.concatenate([low, block, high], axis=dim)
    return block


def is_power_of_two(count):
    return count > 0 and count & (count - 1) == 0


def butterfly_sum(block, axes):
    total = 1
    for axis in axes:
        total *= lax.axis_size(axis)
    if not is_power_of_two(total):
        return lax.psum(block, axes)
    distance = 1
    while distance < total:
        route = [(i, i ^ distance) for i in range(total)]
        block = block + lax.ppermute(block, axes, route)
        distance *= 2
    return block


def xor_gather(block, axis, dim):
    count = lax.axis_size(axis)
    if not is_power_of_two(count):
        return lax.all_gather(block, axis, axis=dim, tiled=True), False
    distance = 1
    while distance < count:
        route = [(i, i ^ distance) for i in range(count)]
        block = jnp.concatenate([block, lax.ppermute(block, axis, route)], axis=dim)
        distance *= 2
    return block, True


def butterfly_scatter(block, axis):
    count = lax.axis_size(axis)
    if not is_power_of_two(count):
        return lax.psum_scatter(block, axis, scatter_dimension=0, tiled=True)
    me = lax.axis_index(axis)
    parts = block.reshape(count, -1, *block.shape[1:])
    distance = 1
    while distance < count:
        bit = (me // distance) % 2
        pairs = parts.reshape(parts.shape[0] // 2, 2, *parts.shape[1:])
        keep = lax.dynamic_index_in_dim(pairs, bit, axis=1, keepdims=False)
        give = lax.dynamic_index_in_dim(pairs, 1 - bit, axis=1, keepdims=False)
        route = [(i, i ^ distance) for i in range(count)]
        parts = keep + lax.ppermute(give, axis, route)
        distance *= 2
    return parts.reshape(-1, *block.shape[1:])


def group_reach(grouped, offsets):
    pieces = []
    for offset in offsets:
        if offset == 0:
            pieces.append(grouped)
        else:
            pieces.append(shifted(grouped, "leaf", -offset))
    return jnp.concatenate(pieces, axis=0)


def chol_solve_kernel(gram_ref, residue_ref, chol_ref, block_ref):
    left = gram_ref[...]
    size = left.shape[0]
    rows = lax.broadcasted_iota(jnp.int32, left.shape, 0)
    cols = lax.broadcasted_iota(jnp.int32, left.shape, 1)
    row_ids = lax.broadcasted_iota(jnp.int32, (size, 1), 0)
    col_ids = lax.broadcasted_iota(jnp.int32, (1, size), 1)
    low = jnp.zeros_like(left)
    for step in range(size):
        column = jnp.sum(jnp.where(cols == step, left, 0.0), axis=1, keepdims=True)
        row = jnp.sum(jnp.where(rows == step, left, 0.0), axis=0, keepdims=True)
        pivot = jnp.sum(jnp.where(row_ids == step, column, 0.0), axis=0, keepdims=True)
        root = jnp.sqrt(pivot)
        low_column = jnp.where(row_ids >= step, column / root, 0.0)
        low_row = jnp.where(col_ids >= step, row / root, 0.0)
        low = jnp.where(cols == step, low_column, low)
        left = left - low_column * low_row
    chol_ref[...] = low
    block = residue_ref[...]
    for step in range(size):
        low_column = jnp.sum(jnp.where(cols == step, low, 0.0), axis=1, keepdims=True)
        diagonal = jnp.sum(jnp.where(row_ids == step, low_column, 0.0), axis=0, keepdims=True)
        solved = jnp.sum(jnp.where(row_ids == step, block, 0.0), axis=0, keepdims=True) / diagonal
        block = jnp.where(
            row_ids == step, solved, jnp.where(row_ids > step, block - low_column * solved, block)
        )
    block_ref[...] = block


def chol_solve(gram_matrix, residue):
    size, width = residue.shape
    return pl.pallas_call(
        chol_solve_kernel,
        out_shape=(
            jax.ShapeDtypeStruct((size, size), jnp.float32),
            jax.ShapeDtypeStruct((size, width), jnp.float32),
        ),
        in_specs=[pl.BlockSpec(memory_space=pltpu.VMEM)] * 2,
        out_specs=(pl.BlockSpec(memory_space=pltpu.VMEM), pl.BlockSpec(memory_space=pltpu.VMEM)),
        cost_estimate=pl.CostEstimate(
            flops=4 * size * size * (size + width), bytes_accessed=8 * size * (size + width), transcendentals=size
        ),
    )(gram_matrix, residue)


def on_device(
    vectors, sigma_point, leaf_basis, near_blocks, near_list, coupling, far_list, far_rank, krylov
):
    highest = lax.Precision.HIGHEST
    local_count, rank_width, leaf_size = leaf_basis.shape
    vec_count = vectors.shape[0]
    near_count = near_list.shape[1]
    slot_count = far_list.shape[1]
    coef_count = lax.axis_size("coef")
    leaf_count = lax.axis_size("leaf")
    group_size = local_count * coef_count
    reach_groups = min(8, leaf_count // 4)
    total_points = local_count * leaf_size * coef_count * leaf_count
    sigma_val = sigma_point[0]
    powers = jnp.stack([jnp.ones((), jnp.float32), sigma_val, sigma_val * sigma_val])
    rounded = vectors.astype(jnp.bfloat16)
    by_cluster = rounded.reshape(vec_count, local_count, leaf_size)
    coarse = jnp.einsum(
        "cki,vci->cvk", leaf_basis, by_cluster, preferred_element_type=jnp.float32
    ).astype(jnp.bfloat16)
    own_rows = coarse.reshape(1, local_count, vec_count * rank_width)
    offsets = list(range(-reach_groups, reach_groups + 1))
    reached = group_reach(own_rows, offsets)
    window, xor_order = xor_gather(reached, "coef", 1)
    flat_rows = window.reshape(-1, vec_count * rank_width)
    group_pos = lax.axis_index("leaf")
    local_ids = far_list - (group_pos - reach_groups) * group_size
    if xor_order:
        in_group = local_ids % group_size
        holder = (in_group // local_count) ^ lax.axis_index("coef")
        local_ids = local_ids - in_group + holder * local_count + in_group % local_count
    local_ids = local_ids.reshape(-1)
    sources = flat_rows.at[local_ids].get(mode="promise_in_bounds").reshape(
        group_size, slot_count, vec_count, rank_width
    )
    lane_ids = jnp.arange(rank_width, dtype=jnp.int32)
    keep_mask = lane_ids[None, None, :] < far_rank[:, :, None]
    sources = jnp.where(keep_mask[:, :, None, :], sources, jnp.zeros((), jnp.bfloat16))
    couple = coupling.reshape(3, group_size, slot_count, rank_width, rank_width)
    far_terms = jnp.einsum("jcfkl,cfvl->jcfvk", couple, sources, preferred_element_type=jnp.float32)
    combined = jnp.tensordot(powers, far_terms, 1) * keep_mask[:, :, None, :].astype(jnp.float32)
    partial_far = jnp.sum(combined, axis=1).reshape(group_size, vec_count * rank_width)
    far_hat = butterfly_scatter(partial_far, "coef")
    far_round = far_hat.astype(jnp.bfloat16).reshape(local_count, vec_count, rank_width)
    far_part = jnp.einsum("cki,cvk->vci", leaf_basis, far_round, preferred_element_type=jnp.float32)
    extended = extended_2(rounded, ((("leaf", "coef"), 1),), local_count * leaf_size)
    extended = extended.reshape(vec_count, 3 * local_count, leaf_size)
    device_pos = lax.axis_index("leaf") * coef_count + lax.axis_index("coef")
    near_ids = (near_list - (device_pos - 1) * local_count).reshape(-1)
    near_src = extended.at[:, near_ids].get(mode="promise_in_bounds").reshape(
        vec_count, local_count, near_count, leaf_size
    )
    near_terms = jnp.einsum(
        "jcnil,vcnl->jvci", near_blocks, near_src, preferred_element_type=jnp.float32
    )
    near_part = jnp.tensordot(powers, near_terms, 1)
    applied = (far_part + near_part).reshape(vec_count, local_count * leaf_size)
    basis_count = krylov.shape[0]
    both_axes = ("leaf", "coef")
    proj_part = jnp.dot(krylov, applied.T, precision=highest)
    self_part = jnp.dot(applied, applied.T, precision=highest)
    summed = butterfly_sum(jnp.concatenate([proj_part, self_part], axis=0), both_axes)
    coeffs = summed[:basis_count]
    outer = summed[basis_count:]
    residue = applied - jnp.dot(coeffs.T, krylov, precision=highest)
    short_gram = (outer - jnp.dot(coeffs.T, coeffs, precision=highest)) / total_points
    eye = jnp.eye(vec_count, dtype=jnp.bool_)
    short_diag = jnp.sum(jnp.where(eye, short_gram, 0.0), axis=0)
    outer_diag = jnp.sum(jnp.where(eye, outer, 0.0), axis=0)
    kept = short_diag * (64 * total_points) >= outer_diag
    def exact_gram():
        part = jnp.dot(residue, residue.T, precision=highest)
        return butterfly_sum(part, both_axes) / total_points
    gram_matrix = lax.cond(jnp.all(kept), lambda: short_gram, exact_gram)
    chol_factor, new_block = chol_solve(gram_matrix, residue)
    return (new_block, coeffs, chol_factor)


def solution(mesh):
    in_specs = (
        P(None, ("leaf", "coef")),
        P(),
        P(("leaf", "coef"), None, None),
        P(None, ("leaf", "coef"), None, None, None),
        P(("leaf", "coef"), None),
        P(None, "leaf", "coef", None),
        P("leaf", "coef"),
        P("leaf", "coef"),
        P(None, ("leaf", "coef")),
    )
    out_specs = (P(None, ("leaf", "coef")), P(), P())
    return jax.shard_map(
        on_device, mesh=mesh, in_specs=in_specs, out_specs=out_specs, check_vma=False
    )
```

```python
import jax
import jax.numpy as jnp
from jax import lax
from jax.experimental import pallas as pl
from jax.experimental.pallas import tpu as pltpu
from jax.sharding import PartitionSpec as P


def shifted(block, axis, distance):
    devices = range(lax.axis_size(axis))
    route = [(i - distance, i) for i in devices if i - distance in devices]
    return lax.ppermute(block, axis, route)


def extended_2(block, sides, width):
    for axis, dim in sides:
        count = lax.axis_size(axis)
        forward = [(i, i + 1) for i in range(count - 1)]
        backward = [(target, source) for source, target in forward]
        low = lax.ppermute(
            lax.slice_in_dim(block, block.shape[dim] - width, None, axis=dim), axis, forward
        )
        high = lax.ppermute(lax.slice_in_dim(block, 0, width, axis=dim), axis, backward)
        block = jnp.concatenate([low, block, high], axis=dim)
    return block


def is_power_of_two(count):
    return count > 0 and count & (count - 1) == 0


def butterfly_sum(block, axes):
    total = 1
    for axis in axes:
        total *= lax.axis_size(axis)
    if not is_power_of_two(total):
        return lax.psum(block, axes)
    distance = 1
    while distance < total:
        route = [(i, i ^ distance) for i in range(total)]
        block = block + lax.ppermute(block, axes, route)
        distance *= 2
    return block


def xor_gather(block, axis, dim):
    count = lax.axis_size(axis)
    if not is_power_of_two(count):
        return lax.all_gather(block, axis, axis=dim, tiled=True), False
    distance = 1
    while distance < count:
        route = [(i, i ^ distance) for i in range(count)]
        block = jnp.concatenate([block, lax.ppermute(block, axis, route)], axis=dim)
        distance *= 2
    return block, True


def butterfly_scatter(block, axis):
    count = lax.axis_size(axis)
    if not is_power_of_two(count):
        return lax.psum_scatter(block, axis, scatter_dimension=0, tiled=True)
    me = lax.axis_index(axis)
    parts = block.reshape(count, -1, *block.shape[1:])
    distance = 1
    while distance < count:
        bit = (me // distance) % 2
        pairs = parts.reshape(parts.shape[0] // 2, 2, *parts.shape[1:])
        keep = lax.dynamic_index_in_dim(pairs, bit, axis=1, keepdims=False)
        give = lax.dynamic_index_in_dim(pairs, 1 - bit, axis=1, keepdims=False)
        route = [(i, i ^ distance) for i in range(count)]
        parts = keep + lax.ppermute(give, axis, route)
        distance *= 2
    return parts.reshape(-1, *block.shape[1:])


def group_reach(grouped, offsets):
    pieces = []
    for offset in offsets:
        if offset == 0:
            pieces.append(grouped)
        else:
            pieces.append(shifted(grouped, "leaf", -offset))
    return jnp.concatenate(pieces, axis=0)


def chol_solve_kernel(gram_ref, residue_ref, chol_ref, block_ref):
    left = gram_ref[...]
    size = left.shape[0]
    rows = lax.broadcasted_iota(jnp.int32, left.shape, 0)
    cols = lax.broadcasted_iota(jnp.int32, left.shape, 1)
    row_ids = lax.broadcasted_iota(jnp.int32, (size, 1), 0)
    col_ids = lax.broadcasted_iota(jnp.int32, (1, size), 1)
    low = jnp.zeros_like(left)
    for step in range(size):
        column = jnp.sum(jnp.where(cols == step, left, 0.0), axis=1, keepdims=True)
        row = jnp.sum(jnp.where(rows == step, left, 0.0), axis=0, keepdims=True)
        pivot = jnp.sum(jnp.where(row_ids == step, column, 0.0), axis=0, keepdims=True)
        root = jnp.sqrt(pivot)
        low_column = jnp.where(row_ids >= step, column / root, 0.0)
        low_row = jnp.where(col_ids >= step, row / root, 0.0)
        low = jnp.where(cols == step, low_column, low)
        left = left - low_column * low_row
    chol_ref[...] = low
    block = residue_ref[...]
    for step in range(size):
        low_column = jnp.sum(jnp.where(cols == step, low, 0.0), axis=1, keepdims=True)
        diagonal = jnp.sum(jnp.where(row_ids == step, low_column, 0.0), axis=0, keepdims=True)
        solved = jnp.sum(jnp.where(row_ids == step, block, 0.0), axis=0, keepdims=True) / diagonal
        block = jnp.where(
            row_ids == step, solved, jnp.where(row_ids > step, block - low_column * solved, block)
        )
    block_ref[...] = block


def chol_solve(gram_matrix, residue):
    size, width = residue.shape
    return pl.pallas_call(
        chol_solve_kernel,
        out_shape=(
            jax.ShapeDtypeStruct((size, size), jnp.float32),
            jax.ShapeDtypeStruct((size, width), jnp.float32),
        ),
        in_specs=[pl.BlockSpec(memory_space=pltpu.VMEM)] * 2,
        out_specs=(pl.BlockSpec(memory_space=pltpu.VMEM), pl.BlockSpec(memory_space=pltpu.VMEM)),
        cost_estimate=pl.CostEstimate(
            flops=4 * size * size * (size + width), bytes_accessed=8 * size * (size + width), transcendentals=size
        ),
    )(gram_matrix, residue)


def on_device(
    vectors, sigma_point, leaf_basis, near_blocks, near_list, coupling, far_list, far_rank, krylov
):
    highest = lax.Precision.HIGHEST
    local_count, rank_width, leaf_size = leaf_basis.shape
    vec_count = vectors.shape[0]
    near_count = near_list.shape[1]
    slot_count = far_list.shape[1]
    coef_count = lax.axis_size("coef")
    leaf_count = lax.axis_size("leaf")
    group_size = local_count * coef_count
    reach_groups = min(8, leaf_count // 4)
    total_points = local_count * leaf_size * coef_count * leaf_count
    sigma_val = sigma_point[0]
    powers = jnp.stack([jnp.ones((), jnp.float32), sigma_val, sigma_val * sigma_val])
    rounded = vectors.astype(jnp.bfloat16)
    by_cluster = rounded.reshape(vec_count, local_count, leaf_size)
    coarse = jnp.einsum(
        "cki,vci->cvk", leaf_basis, by_cluster, preferred_element_type=jnp.float32
    ).astype(jnp.bfloat16)
    own_rows = coarse.reshape(1, local_count, vec_count * rank_width)
    offsets = list(range(-reach_groups, reach_groups + 1))
    reached = group_reach(own_rows, offsets)
    window, xor_order = xor_gather(reached, "coef", 1)
    flat_rows = window.reshape(-1, vec_count * rank_width)
    group_pos = lax.axis_index("leaf")
    local_ids = far_list - (group_pos - reach_groups) * group_size
    if xor_order:
        in_group = local_ids % group_size
        holder = (in_group // local_count) ^ lax.axis_index("coef")
        local_ids = local_ids - in_group + holder * local_count + in_group % local_count
    local_ids = local_ids.reshape(-1)
    sources = flat_rows.at[local_ids].get(mode="promise_in_bounds").reshape(
        group_size, slot_count, vec_count, rank_width
    )
    lane_ids = jnp.arange(rank_width, dtype=jnp.int32)
    keep_mask = lane_ids[None, None, :] < far_rank[:, :, None]
    sources = jnp.where(keep_mask[:, :, None, :], sources, jnp.zeros((), jnp.bfloat16))
    couple = coupling.reshape(3, group_size, slot_count, rank_width, rank_width)
    far_terms = jnp.einsum("jcfkl,cfvl->jcfvk", couple, sources, preferred_element_type=jnp.float32)
    combined = jnp.tensordot(powers, far_terms, 1) * keep_mask[:, :, None, :].astype(jnp.float32)
    partial_far = jnp.sum(combined, axis=1).reshape(group_size, vec_count * rank_width)
    far_hat = butterfly_scatter(partial_far, "coef")
    far_round = far_hat.astype(jnp.bfloat16).reshape(local_count, vec_count, rank_width)
    far_part = jnp.einsum("cki,cvk->vci", leaf_basis, far_round, preferred_element_type=jnp.float32)
    after_far = (partial_far[0, 0] * 0).astype(jnp.bfloat16)
    extended = extended_2(rounded + after_far, ((("leaf", "coef"), 1),), local_count * leaf_size)
    extended = extended.reshape(vec_count, 3 * local_count, leaf_size)
    device_pos = lax.axis_index("leaf") * coef_count + lax.axis_index("coef")
    near_ids = (near_list - (device_pos - 1) * local_count).reshape(-1)
    near_src = extended.at[:, near_ids].get(mode="promise_in_bounds").reshape(
        vec_count, local_count, near_count, leaf_size
    )
    near_terms = jnp.einsum(
        "jcnil,vcnl->jvci", near_blocks, near_src, preferred_element_type=jnp.float32
    )
    near_part = jnp.tensordot(powers, near_terms, 1)
    applied = (far_part + near_part).reshape(vec_count, local_count * leaf_size)
    basis_count = krylov.shape[0]
    both_axes = ("leaf", "coef")
    proj_part = jnp.dot(krylov, applied.T, precision=highest)
    self_part = jnp.dot(applied, applied.T, precision=highest)
    summed = butterfly_sum(jnp.concatenate([proj_part, self_part], axis=0), both_axes)
    coeffs = summed[:basis_count]
    outer = summed[basis_count:]
    residue = applied - jnp.dot(coeffs.T, krylov, precision=highest)
    short_gram = (outer - jnp.dot(coeffs.T, coeffs, precision=highest)) / total_points
    eye = jnp.eye(vec_count, dtype=jnp.bool_)
    short_diag = jnp.sum(jnp.where(eye, short_gram, 0.0), axis=0)
    outer_diag = jnp.sum(jnp.where(eye, outer, 0.0), axis=0)
    kept = short_diag * (64 * total_points) >= outer_diag
    def exact_gram():
        part = jnp.dot(residue, residue.T, precision=highest)
        return butterfly_sum(part, both_axes) / total_points
    gram_matrix = lax.cond(jnp.all(kept), lambda: short_gram, exact_gram)
    chol_factor, new_block = chol_solve(gram_matrix, residue)
    return (new_block, coeffs, chol_factor)


def solution(mesh):
    in_specs = (
        P(None, ("leaf", "coef")),
        P(),
        P(("leaf", "coef"), None, None),
        P(None, ("leaf", "coef"), None, None, None),
        P(("leaf", "coef"), None),
        P(None, "leaf", "coef", None),
        P("leaf", "coef"),
        P("leaf", "coef"),
        P(None, ("leaf", "coef")),
    )
    out_specs = (P(None, ("leaf", "coef")), P(), P())
    return jax.shard_map(
        on_device, mesh=mesh, in_specs=in_specs, out_specs=out_specs, check_vma=False
    )
```

```python
import jax
import jax.numpy as jnp
from jax import lax
from jax.experimental import pallas as pl
from jax.experimental.pallas import tpu as pltpu
from jax.sharding import PartitionSpec as P


def shifted(block, axis, distance):
    devices = range(lax.axis_size(axis))
    route = [(i - distance, i) for i in devices if i - distance in devices]
    return lax.ppermute(block, axis, route)


def extended_2(block, sides, width):
    for axis, dim in sides:
        count = lax.axis_size(axis)
        forward = [(i, i + 1) for i in range(count - 1)]
        backward = [(target, source) for source, target in forward]
        low = lax.ppermute(
            lax.slice_in_dim(block, block.shape[dim] - width, None, axis=dim), axis, forward
        )
        high = lax.ppermute(lax.slice_in_dim(block, 0, width, axis=dim), axis, backward)
        block = jnp.concatenate([low, block, high], axis=dim)
    return block


def is_power_of_two(count):
    return count > 0 and count & (count - 1) == 0


def butterfly_sum(block, axes):
    total = 1
    for axis in axes:
        total *= lax.axis_size(axis)
    if not is_power_of_two(total):
        return lax.psum(block, axes)
    distance = 1
    while distance < total:
        route = [(i, i ^ distance) for i in range(total)]
        block = block + lax.ppermute(block, axes, route)
        distance *= 2
    return block


def xor_gather(block, axis, dim):
    count = lax.axis_size(axis)
    if not is_power_of_two(count):
        return lax.all_gather(block, axis, axis=dim, tiled=True), False
    distance = 1
    while distance < count:
        route = [(i, i ^ distance) for i in range(count)]
        block = jnp.concatenate([block, lax.ppermute(block, axis, route)], axis=dim)
        distance *= 2
    return block, True


def butterfly_scatter(block, axis):
    count = lax.axis_size(axis)
    if not is_power_of_two(count):
        return lax.psum_scatter(block, axis, scatter_dimension=0, tiled=True)
    me = lax.axis_index(axis)
    parts = block.reshape(count, -1, *block.shape[1:])
    distance = 1
    while distance < count:
        bit = (me // distance) % 2
        pairs = parts.reshape(parts.shape[0] // 2, 2, *parts.shape[1:])
        keep = lax.dynamic_index_in_dim(pairs, bit, axis=1, keepdims=False)
        give = lax.dynamic_index_in_dim(pairs, 1 - bit, axis=1, keepdims=False)
        route = [(i, i ^ distance) for i in range(count)]
        parts = keep + lax.ppermute(give, axis, route)
        distance *= 2
    return parts.reshape(-1, *block.shape[1:])


def group_reach(grouped, offsets):
    pieces = []
    for offset in offsets:
        if offset == 0:
            pieces.append(grouped)
        else:
            pieces.append(shifted(grouped, "leaf", -offset))
    return jnp.concatenate(pieces, axis=0)


def chol_solve_kernel(gram_ref, residue_ref, chol_ref, block_ref):
    left = gram_ref[...]
    size = left.shape[0]
    rows = lax.broadcasted_iota(jnp.int32, left.shape, 0)
    cols = lax.broadcasted_iota(jnp.int32, left.shape, 1)
    row_ids = lax.broadcasted_iota(jnp.int32, (size, 1), 0)
    col_ids = lax.broadcasted_iota(jnp.int32, (1, size), 1)
    low = jnp.zeros_like(left)
    for step in range(size):
        column = jnp.sum(jnp.where(cols == step, left, 0.0), axis=1, keepdims=True)
        row = jnp.sum(jnp.where(rows == step, left, 0.0), axis=0, keepdims=True)
        pivot = jnp.sum(jnp.where(row_ids == step, column, 0.0), axis=0, keepdims=True)
        root = jnp.sqrt(pivot)
        low_column = jnp.where(row_ids >= step, column / root, 0.0)
        low_row = jnp.where(col_ids >= step, row / root, 0.0)
        low = jnp.where(cols == step, low_column, low)
        left = left - low_column * low_row
    chol_ref[...] = low
    block = residue_ref[...]
    for step in range(size):
        low_column = jnp.sum(jnp.where(cols == step, low, 0.0), axis=1, keepdims=True)
        diagonal = jnp.sum(jnp.where(row_ids == step, low_column, 0.0), axis=0, keepdims=True)
        solved = jnp.sum(jnp.where(row_ids == step, block, 0.0), axis=0, keepdims=True) / diagonal
        block = jnp.where(
            row_ids == step, solved, jnp.where(row_ids > step, block - low_column * solved, block)
        )
    block_ref[...] = block


def chol_solve(gram_matrix, residue):
    size, width = residue.shape
    return pl.pallas_call(
        chol_solve_kernel,
        out_shape=(
            jax.ShapeDtypeStruct((size, size), jnp.float32),
            jax.ShapeDtypeStruct((size, width), jnp.float32),
        ),
        in_specs=[pl.BlockSpec(memory_space=pltpu.VMEM)] * 2,
        out_specs=(pl.BlockSpec(memory_space=pltpu.VMEM), pl.BlockSpec(memory_space=pltpu.VMEM)),
        cost_estimate=pl.CostEstimate(
            flops=4 * size * size * (size + width), bytes_accessed=8 * size * (size + width), transcendentals=size
        ),
    )(gram_matrix, residue)


def on_device(
    vectors, sigma_point, leaf_basis, near_blocks, near_list, coupling, far_list, far_rank, krylov
):
    highest = lax.Precision.HIGHEST
    local_count, rank_width, leaf_size = leaf_basis.shape
    vec_count = vectors.shape[0]
    near_count = near_list.shape[1]
    slot_count = far_list.shape[1]
    coef_count = lax.axis_size("coef")
    leaf_count = lax.axis_size("leaf")
    group_size = local_count * coef_count
    reach_groups = min(8, leaf_count // 4)
    total_points = local_count * leaf_size * coef_count * leaf_count
    sigma_val = sigma_point[0]
    powers = jnp.stack([jnp.ones((), jnp.float32), sigma_val, sigma_val * sigma_val])
    rounded = vectors.astype(jnp.bfloat16)
    by_cluster = rounded.reshape(vec_count, local_count, leaf_size)
    coarse = jnp.einsum(
        "cki,vci->cvk", leaf_basis, by_cluster, preferred_element_type=jnp.float32
    ).astype(jnp.bfloat16)
    own_rows = coarse.reshape(1, local_count, vec_count * rank_width)
    offsets = list(range(-reach_groups, reach_groups + 1))
    reached = group_reach(own_rows, offsets)
    window, xor_order = xor_gather(reached, "coef", 1)
    flat_rows = window.reshape(-1, vec_count * rank_width)
    group_pos = lax.axis_index("leaf")
    local_ids = far_list - (group_pos - reach_groups) * group_size
    if xor_order:
        in_group = local_ids % group_size
        holder = (in_group // local_count) ^ lax.axis_index("coef")
        local_ids = local_ids - in_group + holder * local_count + in_group % local_count
    local_ids = local_ids.reshape(-1)
    sources = flat_rows.at[local_ids].get(mode="promise_in_bounds").reshape(
        group_size, slot_count, vec_count, rank_width
    )
    lane_ids = jnp.arange(rank_width, dtype=jnp.int32)
    keep_mask = lane_ids[None, None, :] < far_rank[:, :, None]
    sources = jnp.where(keep_mask[:, :, None, :], sources, jnp.zeros((), jnp.bfloat16))
    row_keep = keep_mask[None, :, :, :, None].astype(jnp.float32)
    scaled = coupling.reshape(3, group_size, slot_count, rank_width, rank_width).astype(jnp.float32)
    scaled = scaled * powers[:, None, None, None, None] * row_keep
    high = scaled.astype(jnp.bfloat16)
    low = (scaled - high.astype(jnp.float32)).astype(jnp.bfloat16)
    split_count = 2 * 3 * slot_count * rank_width
    lhs = jnp.transpose(jnp.stack([high, low]), (2, 4, 0, 1, 3, 5)).reshape(
        group_size, rank_width, split_count
    )
    rhs = jnp.broadcast_to(
        jnp.swapaxes(sources, 2, 3)[:, None, None], (group_size, 2, 3, slot_count, rank_width, vec_count)
    ).reshape(group_size, split_count, vec_count)
    far_sum = jnp.einsum("ckK,cKv->cvk", lhs, rhs, preferred_element_type=jnp.float32)
    partial_far = far_sum.reshape(group_size, vec_count * rank_width)
    far_hat = butterfly_scatter(partial_far, "coef")
    far_round = far_hat.astype(jnp.bfloat16).reshape(local_count, vec_count, rank_width)
    far_part = jnp.einsum("cki,cvk->vci", leaf_basis, far_round, preferred_element_type=jnp.float32)
    extended = extended_2(rounded, ((("leaf", "coef"), 1),), local_count * leaf_size)
    extended = extended.reshape(vec_count, 3 * local_count, leaf_size)
    device_pos = lax.axis_index("leaf") * coef_count + lax.axis_index("coef")
    near_ids = (near_list - (device_pos - 1) * local_count).reshape(-1)
    near_src = extended.at[:, near_ids].get(mode="promise_in_bounds").reshape(
        vec_count, local_count, near_count, leaf_size
    )
    near_terms = jnp.einsum(
        "jcnil,vcnl->jvci", near_blocks, near_src, preferred_element_type=jnp.float32
    )
    near_part = jnp.tensordot(powers, near_terms, 1)
    applied = (far_part + near_part).reshape(vec_count, local_count * leaf_size)
    basis_count = krylov.shape[0]
    both_axes = ("leaf", "coef")
    proj_part = jnp.dot(krylov, applied.T, precision=highest)
    self_part = jnp.dot(applied, applied.T, precision=highest)
    summed = butterfly_sum(jnp.concatenate([proj_part, self_part], axis=0), both_axes)
    coeffs = summed[:basis_count]
    outer = summed[basis_count:]
    residue = applied - jnp.dot(coeffs.T, krylov, precision=highest)
    short_gram = (outer - jnp.dot(coeffs.T, coeffs, precision=highest)) / total_points
    eye = jnp.eye(vec_count, dtype=jnp.bool_)
    short_diag = jnp.sum(jnp.where(eye, short_gram, 0.0), axis=0)
    outer_diag = jnp.sum(jnp.where(eye, outer, 0.0), axis=0)
    kept = short_diag * (64 * total_points) >= outer_diag
    def exact_gram():
        part = jnp.dot(residue, residue.T, precision=highest)
        return butterfly_sum(part, both_axes) / total_points
    gram_matrix = lax.cond(jnp.all(kept), lambda: short_gram, exact_gram)
    chol_factor, new_block = chol_solve(gram_matrix, residue)
    return (new_block, coeffs, chol_factor)


def solution(mesh):
    in_specs = (
        P(None, ("leaf", "coef")),
        P(),
        P(("leaf", "coef"), None, None),
        P(None, ("leaf", "coef"), None, None, None),
        P(("leaf", "coef"), None),
        P(None, "leaf", "coef", None),
        P("leaf", "coef"),
        P("leaf", "coef"),
        P(None, ("leaf", "coef")),
    )
    out_specs = (P(None, ("leaf", "coef")), P(), P())
    return jax.shard_map(
        on_device, mesh=mesh, in_specs=in_specs, out_specs=out_specs, check_vma=False
    )
```

```python
import jax
import jax.numpy as jnp
from jax import lax
from jax.experimental import pallas as pl
from jax.experimental.pallas import tpu as pltpu
from jax.sharding import PartitionSpec as P


def shifted(block, axis, distance):
    devices = range(lax.axis_size(axis))
    route = [(i - distance, i) for i in devices if i - distance in devices]
    return lax.ppermute(block, axis, route)


def extended_2(block, sides, width):
    for axis, dim in sides:
        count = lax.axis_size(axis)
        forward = [(i, i + 1) for i in range(count - 1)]
        backward = [(target, source) for source, target in forward]
        low = lax.ppermute(
            lax.slice_in_dim(block, block.shape[dim] - width, None, axis=dim), axis, forward
        )
        high = lax.ppermute(lax.slice_in_dim(block, 0, width, axis=dim), axis, backward)
        block = jnp.concatenate([low, block, high], axis=dim)
    return block


def is_power_of_two(count):
    return count > 0 and count & (count - 1) == 0


def butterfly_sum(block, axes):
    total = 1
    for axis in axes:
        total *= lax.axis_size(axis)
    if not is_power_of_two(total):
        return lax.psum(block, axes)
    distance = 1
    while distance < total:
        route = [(i, i ^ distance) for i in range(total)]
        block = block + lax.ppermute(block, axes, route)
        distance *= 2
    return block


def xor_gather(block, axis, dim):
    count = lax.axis_size(axis)
    if not is_power_of_two(count):
        return lax.all_gather(block, axis, axis=dim, tiled=True), False
    distance = 1
    while distance < count:
        route = [(i, i ^ distance) for i in range(count)]
        block = jnp.concatenate([block, lax.ppermute(block, axis, route)], axis=dim)
        distance *= 2
    return block, True


def butterfly_scatter(block, axis):
    count = lax.axis_size(axis)
    if not is_power_of_two(count):
        return lax.psum_scatter(block, axis, scatter_dimension=0, tiled=True)
    me = lax.axis_index(axis)
    parts = block.reshape(count, -1, *block.shape[1:])
    distance = 1
    while distance < count:
        bit = (me // distance) % 2
        pairs = parts.reshape(parts.shape[0] // 2, 2, *parts.shape[1:])
        keep = lax.dynamic_index_in_dim(pairs, bit, axis=1, keepdims=False)
        give = lax.dynamic_index_in_dim(pairs, 1 - bit, axis=1, keepdims=False)
        route = [(i, i ^ distance) for i in range(count)]
        parts = keep + lax.ppermute(give, axis, route)
        distance *= 2
    return parts.reshape(-1, *block.shape[1:])


def group_reach(grouped, offsets):
    pieces = []
    for offset in offsets:
        if offset == 0:
            pieces.append(grouped)
        else:
            pieces.append(shifted(grouped, "leaf", -offset))
    return jnp.concatenate(pieces, axis=0)


def chol_solve_kernel(gram_ref, residue_ref, chol_ref, block_ref):
    left = gram_ref[...]
    size = left.shape[0]
    rows = lax.broadcasted_iota(jnp.int32, left.shape, 0)
    cols = lax.broadcasted_iota(jnp.int32, left.shape, 1)
    row_ids = lax.broadcasted_iota(jnp.int32, (size, 1), 0)
    col_ids = lax.broadcasted_iota(jnp.int32, (1, size), 1)
    low = jnp.zeros_like(left)
    for step in range(size):
        column = jnp.sum(jnp.where(cols == step, left, 0.0), axis=1, keepdims=True)
        row = jnp.sum(jnp.where(rows == step, left, 0.0), axis=0, keepdims=True)
        pivot = jnp.sum(jnp.where(row_ids == step, column, 0.0), axis=0, keepdims=True)
        root = jnp.sqrt(pivot)
        low_column = jnp.where(row_ids >= step, column / root, 0.0)
        low_row = jnp.where(col_ids >= step, row / root, 0.0)
        low = jnp.where(cols == step, low_column, low)
        left = left - low_column * low_row
    chol_ref[...] = low
    block = residue_ref[...]
    for step in range(size):
        low_column = jnp.sum(jnp.where(cols == step, low, 0.0), axis=1, keepdims=True)
        diagonal = jnp.sum(jnp.where(row_ids == step, low_column, 0.0), axis=0, keepdims=True)
        solved = jnp.sum(jnp.where(row_ids == step, block, 0.0), axis=0, keepdims=True) / diagonal
        block = jnp.where(
            row_ids == step, solved, jnp.where(row_ids > step, block - low_column * solved, block)
        )
    block_ref[...] = block


def chol_solve(gram_matrix, residue):
    size, width = residue.shape
    return pl.pallas_call(
        chol_solve_kernel,
        out_shape=(
            jax.ShapeDtypeStruct((size, size), jnp.float32),
            jax.ShapeDtypeStruct((size, width), jnp.float32),
        ),
        in_specs=[pl.BlockSpec(memory_space=pltpu.VMEM)] * 2,
        out_specs=(pl.BlockSpec(memory_space=pltpu.VMEM), pl.BlockSpec(memory_space=pltpu.VMEM)),
        cost_estimate=pl.CostEstimate(
            flops=4 * size * size * (size + width), bytes_accessed=8 * size * (size + width), transcendentals=size
        ),
    )(gram_matrix, residue)


def on_device(
    vectors, sigma_point, leaf_basis, near_blocks, near_list, coupling, far_list, far_rank, krylov
):
    highest = lax.Precision.HIGHEST
    local_count, rank_width, leaf_size = leaf_basis.shape
    vec_count = vectors.shape[0]
    near_count = near_list.shape[1]
    slot_count = far_list.shape[1]
    coef_count = lax.axis_size("coef")
    leaf_count = lax.axis_size("leaf")
    group_size = local_count * coef_count
    reach_groups = min(8, leaf_count // 4)
    total_points = local_count * leaf_size * coef_count * leaf_count
    sigma_val = sigma_point[0]
    powers = jnp.stack([jnp.ones((), jnp.float32), sigma_val, sigma_val * sigma_val])
    rounded = vectors.astype(jnp.bfloat16)
    by_cluster = rounded.reshape(vec_count, local_count, leaf_size)
    coarse = jnp.einsum(
        "cki,vci->cvk", leaf_basis, by_cluster, preferred_element_type=jnp.float32
    ).astype(jnp.bfloat16)
    own_rows = coarse.reshape(1, local_count, vec_count * rank_width)
    by_leaf, leaf_xor = xor_gather(own_rows, "leaf", 0)
    window, coef_xor = xor_gather(by_leaf, "coef", 1)
    flat_rows = window.reshape(-1, vec_count * rank_width)
    source_group = far_list // group_size
    source_holder = (far_list % group_size) // local_count
    if leaf_xor:
        source_group = source_group ^ lax.axis_index("leaf")
    if coef_xor:
        source_holder = source_holder ^ lax.axis_index("coef")
    local_ids = (
        source_group * group_size + source_holder * local_count + far_list % local_count
    ).reshape(-1)
    sources = flat_rows.at[local_ids].get(mode="promise_in_bounds").reshape(
        group_size, slot_count, vec_count, rank_width
    )
    lane_ids = jnp.arange(rank_width, dtype=jnp.int32)
    keep_mask = lane_ids[None, None, :] < far_rank[:, :, None]
    sources = jnp.where(keep_mask[:, :, None, :], sources, jnp.zeros((), jnp.bfloat16))
    couple = coupling.reshape(3, group_size, slot_count, rank_width, rank_width)
    far_terms = jnp.einsum("jcfkl,cfvl->jcfvk", couple, sources, preferred_element_type=jnp.float32)
    combined = jnp.tensordot(powers, far_terms, 1) * keep_mask[:, :, None, :].astype(jnp.float32)
    partial_far = jnp.sum(combined, axis=1).reshape(group_size, vec_count * rank_width)
    far_hat = butterfly_scatter(partial_far, "coef")
    far_round = far_hat.astype(jnp.bfloat16).reshape(local_count, vec_count, rank_width)
    far_part = jnp.einsum("cki,cvk->vci", leaf_basis, far_round, preferred_element_type=jnp.float32)
    extended = extended_2(rounded, ((("leaf", "coef"), 1),), local_count * leaf_size)
    extended = extended.reshape(vec_count, 3 * local_count, leaf_size)
    device_pos = lax.axis_index("leaf") * coef_count + lax.axis_index("coef")
    near_ids = (near_list - (device_pos - 1) * local_count).reshape(-1)
    near_src = extended.at[:, near_ids].get(mode="promise_in_bounds").reshape(
        vec_count, local_count, near_count, leaf_size
    )
    near_terms = jnp.einsum(
        "jcnil,vcnl->jvci", near_blocks, near_src, preferred_element_type=jnp.float32
    )
    near_part = jnp.tensordot(powers, near_terms, 1)
    applied = (far_part + near_part).reshape(vec_count, local_count * leaf_size)
    basis_count = krylov.shape[0]
    both_axes = ("leaf", "coef")
    proj_part = jnp.dot(krylov, applied.T, precision=highest)
    self_part = jnp.dot(applied, applied.T, precision=highest)
    summed = butterfly_sum(jnp.concatenate([proj_part, self_part], axis=0), both_axes)
    coeffs = summed[:basis_count]
    outer = summed[basis_count:]
    residue = applied - jnp.dot(coeffs.T, krylov, precision=highest)
    short_gram = (outer - jnp.dot(coeffs.T, coeffs, precision=highest)) / total_points
    eye = jnp.eye(vec_count, dtype=jnp.bool_)
    short_diag = jnp.sum(jnp.where(eye, short_gram, 0.0), axis=0)
    outer_diag = jnp.sum(jnp.where(eye, outer, 0.0), axis=0)
    kept = short_diag * (64 * total_points) >= outer_diag
    def exact_gram():
        part = jnp.dot(residue, residue.T, precision=highest)
        return butterfly_sum(part, both_axes) / total_points
    gram_matrix = lax.cond(jnp.all(kept), lambda: short_gram, exact_gram)
    chol_factor, new_block = chol_solve(gram_matrix, residue)
    return (new_block, coeffs, chol_factor)


def solution(mesh):
    in_specs = (
        P(None, ("leaf", "coef")),
        P(),
        P(("leaf", "coef"), None, None),
        P(None, ("leaf", "coef"), None, None, None),
        P(("leaf", "coef"), None),
        P(None, "leaf", "coef", None),
        P("leaf", "coef"),
        P("leaf", "coef"),
        P(None, ("leaf", "coef")),
    )
    out_specs = (P(None, ("leaf", "coef")), P(), P())
    return jax.shard_map(
        on_device, mesh=mesh, in_specs=in_specs, out_specs=out_specs, check_vma=False
    )
```

```python
import jax
import jax.numpy as jnp
from jax import lax
from jax.experimental import pallas as pl
from jax.experimental.pallas import tpu as pltpu
from jax.sharding import PartitionSpec as P


def shifted(block, axis, distance):
    devices = range(lax.axis_size(axis))
    route = [(i - distance, i) for i in devices if i - distance in devices]
    return lax.ppermute(block, axis, route)


def extended_2(block, sides, width):
    for axis, dim in sides:
        count = lax.axis_size(axis)
        forward = [(i, i + 1) for i in range(count - 1)]
        backward = [(target, source) for source, target in forward]
        low = lax.ppermute(
            lax.slice_in_dim(block, block.shape[dim] - width, None, axis=dim), axis, forward
        )
        high = lax.ppermute(lax.slice_in_dim(block, 0, width, axis=dim), axis, backward)
        block = jnp.concatenate([low, block, high], axis=dim)
    return block


def is_power_of_two(count):
    return count > 0 and count & (count - 1) == 0


def butterfly_sum(block, axes):
    total = 1
    for axis in axes:
        total *= lax.axis_size(axis)
    if not is_power_of_two(total):
        return lax.psum(block, axes)
    distance = 1
    while distance < total:
        route = [(i, i ^ distance) for i in range(total)]
        block = block + lax.ppermute(block, axes, route)
        distance *= 2
    return block


def xor_gather(block, axis, dim):
    count = lax.axis_size(axis)
    if not is_power_of_two(count):
        return lax.all_gather(block, axis, axis=dim, tiled=True), False
    distance = 1
    while distance < count:
        route = [(i, i ^ distance) for i in range(count)]
        block = jnp.concatenate([block, lax.ppermute(block, axis, route)], axis=dim)
        distance *= 2
    return block, True


def butterfly_scatter(block, axis):
    count = lax.axis_size(axis)
    if not is_power_of_two(count):
        return lax.psum_scatter(block, axis, scatter_dimension=0, tiled=True)
    me = lax.axis_index(axis)
    parts = block.reshape(count, -1, *block.shape[1:])
    distance = 1
    while distance < count:
        bit = (me // distance) % 2
        pairs = parts.reshape(parts.shape[0] // 2, 2, *parts.shape[1:])
        keep = lax.dynamic_index_in_dim(pairs, bit, axis=1, keepdims=False)
        give = lax.dynamic_index_in_dim(pairs, 1 - bit, axis=1, keepdims=False)
        route = [(i, i ^ distance) for i in range(count)]
        parts = keep + lax.ppermute(give, axis, route)
        distance *= 2
    return parts.reshape(-1, *block.shape[1:])


def paired_halo(block, axes):
    total = 1
    for axis in axes:
        total *= lax.axis_size(axis)
    me = lax.axis_index(axes[0])
    for axis in axes[1:]:
        me = me * lax.axis_size(axis) + lax.axis_index(axis)
    even_pairs = [(i, i ^ 1) for i in range(total) if (i ^ 1) < total]
    odd_pairs = [(i, i + 1) for i in range(1, total - 1, 2)] + [(i + 1, i) for i in range(1, total - 1, 2)]
    first = lax.ppermute(block, axes, even_pairs)
    second = lax.ppermute(block, axes, odd_pairs)
    is_even = me % 2 == 0
    low = jnp.where(is_even, second, first)
    high = jnp.where(is_even, first, second)
    return jnp.concatenate([low, block, high], axis=1)


def group_reach(grouped, offsets):
    pieces = []
    for offset in offsets:
        if offset == 0:
            pieces.append(grouped)
        else:
            pieces.append(shifted(grouped, "leaf", -offset))
    return jnp.concatenate(pieces, axis=0)


def chol_solve_kernel(gram_ref, residue_ref, chol_ref, block_ref):
    left = gram_ref[...]
    size = left.shape[0]
    rows = lax.broadcasted_iota(jnp.int32, left.shape, 0)
    cols = lax.broadcasted_iota(jnp.int32, left.shape, 1)
    row_ids = lax.broadcasted_iota(jnp.int32, (size, 1), 0)
    col_ids = lax.broadcasted_iota(jnp.int32, (1, size), 1)
    low = jnp.zeros_like(left)
    for step in range(size):
        column = jnp.sum(jnp.where(cols == step, left, 0.0), axis=1, keepdims=True)
        row = jnp.sum(jnp.where(rows == step, left, 0.0), axis=0, keepdims=True)
        pivot = jnp.sum(jnp.where(row_ids == step, column, 0.0), axis=0, keepdims=True)
        root = jnp.sqrt(pivot)
        low_column = jnp.where(row_ids >= step, column / root, 0.0)
        low_row = jnp.where(col_ids >= step, row / root, 0.0)
        low = jnp.where(cols == step, low_column, low)
        left = left - low_column * low_row
    chol_ref[...] = low
    block = residue_ref[...]
    for step in range(size):
        low_column = jnp.sum(jnp.where(cols == step, low, 0.0), axis=1, keepdims=True)
        diagonal = jnp.sum(jnp.where(row_ids == step, low_column, 0.0), axis=0, keepdims=True)
        solved = jnp.sum(jnp.where(row_ids == step, block, 0.0), axis=0, keepdims=True) / diagonal
        block = jnp.where(
            row_ids == step, solved, jnp.where(row_ids > step, block - low_column * solved, block)
        )
    block_ref[...] = block


def chol_solve(gram_matrix, residue):
    size, width = residue.shape
    return pl.pallas_call(
        chol_solve_kernel,
        out_shape=(
            jax.ShapeDtypeStruct((size, size), jnp.float32),
            jax.ShapeDtypeStruct((size, width), jnp.float32),
        ),
        in_specs=[pl.BlockSpec(memory_space=pltpu.VMEM)] * 2,
        out_specs=(pl.BlockSpec(memory_space=pltpu.VMEM), pl.BlockSpec(memory_space=pltpu.VMEM)),
        cost_estimate=pl.CostEstimate(
            flops=4 * size * size * (size + width), bytes_accessed=8 * size * (size + width), transcendentals=size
        ),
    )(gram_matrix, residue)


def on_device(
    vectors, sigma_point, leaf_basis, near_blocks, near_list, coupling, far_list, far_rank, krylov
):
    highest = lax.Precision.HIGHEST
    local_count, rank_width, leaf_size = leaf_basis.shape
    vec_count = vectors.shape[0]
    near_count = near_list.shape[1]
    slot_count = far_list.shape[1]
    coef_count = lax.axis_size("coef")
    leaf_count = lax.axis_size("leaf")
    group_size = local_count * coef_count
    reach_groups = min(8, leaf_count // 4)
    total_points = local_count * leaf_size * coef_count * leaf_count
    sigma_val = sigma_point[0]
    powers = jnp.stack([jnp.ones((), jnp.float32), sigma_val, sigma_val * sigma_val])
    rounded = vectors.astype(jnp.bfloat16)
    by_cluster = rounded.reshape(vec_count, local_count, leaf_size)
    coarse = jnp.einsum(
        "cki,vci->cvk", leaf_basis, by_cluster, preferred_element_type=jnp.float32
    ).astype(jnp.bfloat16)
    own_rows = coarse.reshape(1, local_count, vec_count * rank_width)
    by_leaf, leaf_xor = xor_gather(own_rows, "leaf", 0)
    window, coef_xor = xor_gather(by_leaf, "coef", 1)
    flat_rows = window.reshape(-1, vec_count * rank_width)
    source_group = far_list // group_size
    source_holder = (far_list % group_size) // local_count
    if leaf_xor:
        source_group = source_group ^ lax.axis_index("leaf")
    if coef_xor:
        source_holder = source_holder ^ lax.axis_index("coef")
    local_ids = (
        source_group * group_size + source_holder * local_count + far_list % local_count
    ).reshape(-1)
    sources = flat_rows.at[local_ids].get(mode="promise_in_bounds").reshape(
        group_size, slot_count, vec_count, rank_width
    )
    lane_ids = jnp.arange(rank_width, dtype=jnp.int32)
    keep_mask = lane_ids[None, None, :] < far_rank[:, :, None]
    sources = jnp.where(keep_mask[:, :, None, :], sources, jnp.zeros((), jnp.bfloat16))
    couple = coupling.reshape(3, group_size, slot_count, rank_width, rank_width)
    far_terms = jnp.einsum("jcfkl,cfvl->jcfvk", couple, sources, preferred_element_type=jnp.float32)
    combined = jnp.tensordot(powers, far_terms, 1) * keep_mask[:, :, None, :].astype(jnp.float32)
    partial_far = jnp.sum(combined, axis=1).reshape(group_size, vec_count * rank_width)
    far_hat = butterfly_scatter(partial_far, "coef")
    far_round = far_hat.astype(jnp.bfloat16).reshape(local_count, vec_count, rank_width)
    far_part = jnp.einsum("cki,cvk->vci", leaf_basis, far_round, preferred_element_type=jnp.float32)
    extended = paired_halo(rounded, ("leaf", "coef"))
    extended = extended.reshape(vec_count, 3 * local_count, leaf_size)
    device_pos = lax.axis_index("leaf") * coef_count + lax.axis_index("coef")
    near_ids = (near_list - (device_pos - 1) * local_count).reshape(-1)
    near_src = extended.at[:, near_ids].get(mode="promise_in_bounds").reshape(
        vec_count, local_count, near_count, leaf_size
    )
    near_terms = jnp.einsum(
        "jcnil,vcnl->jvci", near_blocks, near_src, preferred_element_type=jnp.float32
    )
    near_part = jnp.tensordot(powers, near_terms, 1)
    applied = (far_part + near_part).reshape(vec_count, local_count * leaf_size)
    basis_count = krylov.shape[0]
    both_axes = ("leaf", "coef")
    proj_part = jnp.dot(krylov, applied.T, precision=highest)
    self_part = jnp.dot(applied, applied.T, precision=highest)
    summed = butterfly_sum(jnp.concatenate([proj_part, self_part], axis=0), both_axes)
    coeffs = summed[:basis_count]
    outer = summed[basis_count:]
    residue = applied - jnp.dot(coeffs.T, krylov, precision=highest)
    short_gram = (outer - jnp.dot(coeffs.T, coeffs, precision=highest)) / total_points
    eye = jnp.eye(vec_count, dtype=jnp.bool_)
    short_diag = jnp.sum(jnp.where(eye, short_gram, 0.0), axis=0)
    outer_diag = jnp.sum(jnp.where(eye, outer, 0.0), axis=0)
    kept = short_diag * (64 * total_points) >= outer_diag
    def exact_gram():
        part = jnp.dot(residue, residue.T, precision=highest)
        return butterfly_sum(part, both_axes) / total_points
    gram_matrix = lax.cond(jnp.all(kept), lambda: short_gram, exact_gram)
    chol_factor, new_block = chol_solve(gram_matrix, residue)
    return (new_block, coeffs, chol_factor)


def solution(mesh):
    in_specs = (
        P(None, ("leaf", "coef")),
        P(),
        P(("leaf", "coef"), None, None),
        P(None, ("leaf", "coef"), None, None, None),
        P(("leaf", "coef"), None),
        P(None, "leaf", "coef", None),
        P("leaf", "coef"),
        P("leaf", "coef"),
        P(None, ("leaf", "coef")),
    )
    out_specs = (P(None, ("leaf", "coef")), P(), P())
    return jax.shard_map(
        on_device, mesh=mesh, in_specs=in_specs, out_specs=out_specs, check_vma=False
    )
```

```python
import jax
import jax.numpy as jnp
from jax import lax
from jax.experimental import pallas as pl
from jax.experimental.pallas import tpu as pltpu
from jax.sharding import PartitionSpec as P


def shifted(block, axis, distance):
    devices = range(lax.axis_size(axis))
    route = [(i - distance, i) for i in devices if i - distance in devices]
    return lax.ppermute(block, axis, route)


def extended_2(block, sides, width):
    for axis, dim in sides:
        count = lax.axis_size(axis)
        forward = [(i, i + 1) for i in range(count - 1)]
        backward = [(target, source) for source, target in forward]
        low = lax.ppermute(
            lax.slice_in_dim(block, block.shape[dim] - width, None, axis=dim), axis, forward
        )
        high = lax.ppermute(lax.slice_in_dim(block, 0, width, axis=dim), axis, backward)
        block = jnp.concatenate([low, block, high], axis=dim)
    return block


def is_power_of_two(count):
    return count > 0 and count & (count - 1) == 0


def butterfly_sum(block, axes):
    total = 1
    for axis in axes:
        total *= lax.axis_size(axis)
    if not is_power_of_two(total):
        return lax.psum(block, axes)
    distance = 1
    while distance < total:
        route = [(i, i ^ distance) for i in range(total)]
        block = block + lax.ppermute(block, axes, route)
        distance *= 2
    return block


def xor_gather(block, axis, dim):
    count = lax.axis_size(axis)
    if not is_power_of_two(count):
        return lax.all_gather(block, axis, axis=dim, tiled=True), False
    distance = 1
    while distance < count:
        route = [(i, i ^ distance) for i in range(count)]
        block = jnp.concatenate([block, lax.ppermute(block, axis, route)], axis=dim)
        distance *= 2
    return block, True


def butterfly_scatter(block, axis):
    count = lax.axis_size(axis)
    if not is_power_of_two(count):
        return lax.psum_scatter(block, axis, scatter_dimension=0, tiled=True)
    me = lax.axis_index(axis)
    parts = block
    distance = count // 2
    while distance >= 1:
        halves = parts.reshape(2, parts.shape[0] // 2, *parts.shape[1:])
        bit = (me // distance) % 2
        keep = lax.dynamic_index_in_dim(halves, bit, axis=0, keepdims=False)
        give = lax.dynamic_index_in_dim(halves, 1 - bit, axis=0, keepdims=False)
        route = [(i, i ^ distance) for i in range(count)]
        parts = keep + lax.ppermute(give, axis, route)
        distance //= 2
    return parts


def group_reach(grouped, offsets):
    pieces = []
    for offset in offsets:
        if offset == 0:
            pieces.append(grouped)
        else:
            pieces.append(shifted(grouped, "leaf", -offset))
    return jnp.concatenate(pieces, axis=0)


def chol_solve_kernel(gram_ref, residue_ref, chol_ref, block_ref):
    left = gram_ref[...]
    size = left.shape[0]
    rows = lax.broadcasted_iota(jnp.int32, left.shape, 0)
    cols = lax.broadcasted_iota(jnp.int32, left.shape, 1)
    row_ids = lax.broadcasted_iota(jnp.int32, (size, 1), 0)
    col_ids = lax.broadcasted_iota(jnp.int32, (1, size), 1)
    low = jnp.zeros_like(left)
    for step in range(size):
        column = jnp.sum(jnp.where(cols == step, left, 0.0), axis=1, keepdims=True)
        row = jnp.sum(jnp.where(rows == step, left, 0.0), axis=0, keepdims=True)
        pivot = jnp.sum(jnp.where(row_ids == step, column, 0.0), axis=0, keepdims=True)
        root = jnp.sqrt(pivot)
        low_column = jnp.where(row_ids >= step, column / root, 0.0)
        low_row = jnp.where(col_ids >= step, row / root, 0.0)
        low = jnp.where(cols == step, low_column, low)
        left = left - low_column * low_row
    chol_ref[...] = low
    block = residue_ref[...]
    for step in range(size):
        low_column = jnp.sum(jnp.where(cols == step, low, 0.0), axis=1, keepdims=True)
        diagonal = jnp.sum(jnp.where(row_ids == step, low_column, 0.0), axis=0, keepdims=True)
        solved = jnp.sum(jnp.where(row_ids == step, block, 0.0), axis=0, keepdims=True) / diagonal
        block = jnp.where(
            row_ids == step, solved, jnp.where(row_ids > step, block - low_column * solved, block)
        )
    block_ref[...] = block


def chol_solve(gram_matrix, residue):
    size, width = residue.shape
    return pl.pallas_call(
        chol_solve_kernel,
        out_shape=(
            jax.ShapeDtypeStruct((size, size), jnp.float32),
            jax.ShapeDtypeStruct((size, width), jnp.float32),
        ),
        in_specs=[pl.BlockSpec(memory_space=pltpu.VMEM)] * 2,
        out_specs=(pl.BlockSpec(memory_space=pltpu.VMEM), pl.BlockSpec(memory_space=pltpu.VMEM)),
        cost_estimate=pl.CostEstimate(
            flops=4 * size * size * (size + width), bytes_accessed=8 * size * (size + width), transcendentals=size
        ),
    )(gram_matrix, residue)


def on_device(
    vectors, sigma_point, leaf_basis, near_blocks, near_list, coupling, far_list, far_rank, krylov
):
    highest = lax.Precision.HIGHEST
    local_count, rank_width, leaf_size = leaf_basis.shape
    vec_count = vectors.shape[0]
    near_count = near_list.shape[1]
    slot_count = far_list.shape[1]
    coef_count = lax.axis_size("coef")
    leaf_count = lax.axis_size("leaf")
    group_size = local_count * coef_count
    reach_groups = min(8, leaf_count // 4)
    total_points = local_count * leaf_size * coef_count * leaf_count
    sigma_val = sigma_point[0]
    powers = jnp.stack([jnp.ones((), jnp.float32), sigma_val, sigma_val * sigma_val])
    rounded = vectors.astype(jnp.bfloat16)
    by_cluster = rounded.reshape(vec_count, local_count, leaf_size)
    coarse = jnp.einsum(
        "cki,vci->cvk", leaf_basis, by_cluster, preferred_element_type=jnp.float32
    ).astype(jnp.bfloat16)
    own_rows = coarse.reshape(1, local_count, vec_count * rank_width)
    by_leaf, leaf_xor = xor_gather(own_rows, "leaf", 0)
    window, coef_xor = xor_gather(by_leaf, "coef", 1)
    flat_rows = window.reshape(-1, vec_count * rank_width)
    source_group = far_list // group_size
    source_holder = (far_list % group_size) // local_count
    if leaf_xor:
        source_group = source_group ^ lax.axis_index("leaf")
    if coef_xor:
        source_holder = source_holder ^ lax.axis_index("coef")
    local_ids = (
        source_group * group_size + source_holder * local_count + far_list % local_count
    ).reshape(-1)
    sources = flat_rows.at[local_ids].get(mode="promise_in_bounds").reshape(
        group_size, slot_count, vec_count, rank_width
    )
    lane_ids = jnp.arange(rank_width, dtype=jnp.int32)
    keep_mask = lane_ids[None, None, :] < far_rank[:, :, None]
    sources = jnp.where(keep_mask[:, :, None, :], sources, jnp.zeros((), jnp.bfloat16))
    couple = coupling.reshape(3, group_size, slot_count, rank_width, rank_width)
    far_terms = jnp.einsum("jcfkl,cfvl->jcfvk", couple, sources, preferred_element_type=jnp.float32)
    combined = jnp.tensordot(powers, far_terms, 1) * keep_mask[:, :, None, :].astype(jnp.float32)
    partial_far = jnp.sum(combined, axis=1).reshape(group_size, vec_count * rank_width)
    far_hat = butterfly_scatter(partial_far, "coef")
    far_round = far_hat.astype(jnp.bfloat16).reshape(local_count, vec_count, rank_width)
    far_part = jnp.einsum("cki,cvk->vci", leaf_basis, far_round, preferred_element_type=jnp.float32)
    extended = extended_2(rounded, ((("leaf", "coef"), 1),), local_count * leaf_size)
    extended = extended.reshape(vec_count, 3 * local_count, leaf_size)
    device_pos = lax.axis_index("leaf") * coef_count + lax.axis_index("coef")
    near_ids = (near_list - (device_pos - 1) * local_count).reshape(-1)
    near_src = extended.at[:, near_ids].get(mode="promise_in_bounds").reshape(
        vec_count, local_count, near_count, leaf_size
    )
    near_terms = jnp.einsum(
        "jcnil,vcnl->jvci", near_blocks, near_src, preferred_element_type=jnp.float32
    )
    near_part = jnp.tensordot(powers, near_terms, 1)
    applied = (far_part + near_part).reshape(vec_count, local_count * leaf_size)
    basis_count = krylov.shape[0]
    both_axes = ("leaf", "coef")
    proj_part = jnp.dot(krylov, applied.T, precision=highest)
    self_part = jnp.dot(applied, applied.T, precision=highest)
    summed = butterfly_sum(jnp.concatenate([proj_part, self_part], axis=0), both_axes)
    coeffs = summed[:basis_count]
    outer = summed[basis_count:]
    residue = applied - jnp.dot(coeffs.T, krylov, precision=highest)
    short_gram = (outer - jnp.dot(coeffs.T, coeffs, precision=highest)) / total_points
    eye = jnp.eye(vec_count, dtype=jnp.bool_)
    short_diag = jnp.sum(jnp.where(eye, short_gram, 0.0), axis=0)
    outer_diag = jnp.sum(jnp.where(eye, outer, 0.0), axis=0)
    kept = short_diag * (64 * total_points) >= outer_diag
    def exact_gram():
        part = jnp.dot(residue, residue.T, precision=highest)
        return butterfly_sum(part, both_axes) / total_points
    gram_matrix = lax.cond(jnp.all(kept), lambda: short_gram, exact_gram)
    chol_factor, new_block = chol_solve(gram_matrix, residue)
    return (new_block, coeffs, chol_factor)


def solution(mesh):
    in_specs = (
        P(None, ("leaf", "coef")),
        P(),
        P(("leaf", "coef"), None, None),
        P(None, ("leaf", "coef"), None, None, None),
        P(("leaf", "coef"), None),
        P(None, "leaf", "coef", None),
        P("leaf", "coef"),
        P("leaf", "coef"),
        P(None, ("leaf", "coef")),
    )
    out_specs = (P(None, ("leaf", "coef")), P(), P())
    return jax.shard_map(
        on_device, mesh=mesh, in_specs=in_specs, out_specs=out_specs, check_vma=False
    )
```

```python
import jax
import jax.numpy as jnp
from jax import lax
from jax.experimental import pallas as pl
from jax.experimental.pallas import tpu as pltpu
from jax.sharding import PartitionSpec as P


def shifted(block, axis, distance):
    devices = range(lax.axis_size(axis))
    route = [(i - distance, i) for i in devices if i - distance in devices]
    return lax.ppermute(block, axis, route)


def extended_2(block, sides, width):
    for axis, dim in sides:
        count = lax.axis_size(axis)
        forward = [(i, i + 1) for i in range(count - 1)]
        backward = [(target, source) for source, target in forward]
        low = lax.ppermute(
            lax.slice_in_dim(block, block.shape[dim] - width, None, axis=dim), axis, forward
        )
        high = lax.ppermute(lax.slice_in_dim(block, 0, width, axis=dim), axis, backward)
        block = jnp.concatenate([low, block, high], axis=dim)
    return block


def is_power_of_two(count):
    return count > 0 and count & (count - 1) == 0


def butterfly_sum(block, axes):
    total = 1
    for axis in axes:
        total *= lax.axis_size(axis)
    if not is_power_of_two(total):
        return lax.psum(block, axes)
    distance = 1
    while distance < total:
        route = [(i, i ^ distance) for i in range(total)]
        block = block + lax.ppermute(block, axes, route)
        distance *= 2
    return block


def xor_gather(block, axis, dim):
    count = lax.axis_size(axis)
    if not is_power_of_two(count):
        return lax.all_gather(block, axis, axis=dim, tiled=True), False
    distance = 1
    while distance < count:
        route = [(i, i ^ distance) for i in range(count)]
        block = jnp.concatenate([block, lax.ppermute(block, axis, route)], axis=dim)
        distance *= 2
    return block, True


def butterfly_scatter(block, axis):
    count = lax.axis_size(axis)
    if not is_power_of_two(count):
        return lax.psum_scatter(block, axis, scatter_dimension=0, tiled=True)
    me = lax.axis_index(axis)
    parts = block
    distance = count // 2
    while distance >= 1:
        halves = parts.reshape(2, parts.shape[0] // 2, *parts.shape[1:])
        bit = (me // distance) % 2
        keep = lax.dynamic_index_in_dim(halves, bit, axis=0, keepdims=False)
        give = lax.dynamic_index_in_dim(halves, 1 - bit, axis=0, keepdims=False)
        route = [(i, i ^ distance) for i in range(count)]
        parts = keep + lax.ppermute(give, axis, route)
        distance //= 2
    return parts


def group_reach(grouped, offsets):
    pieces = []
    for offset in offsets:
        if offset == 0:
            pieces.append(grouped)
        else:
            pieces.append(shifted(grouped, "leaf", -offset))
    return jnp.concatenate(pieces, axis=0)


def chol_solve_kernel(gram_ref, residue_ref, chol_ref, block_ref):
    left = gram_ref[...]
    size = left.shape[0]
    rows = lax.broadcasted_iota(jnp.int32, left.shape, 0)
    cols = lax.broadcasted_iota(jnp.int32, left.shape, 1)
    row_ids = lax.broadcasted_iota(jnp.int32, (size, 1), 0)
    col_ids = lax.broadcasted_iota(jnp.int32, (1, size), 1)
    low = jnp.zeros_like(left)
    for step in range(size):
        column = jnp.sum(jnp.where(cols == step, left, 0.0), axis=1, keepdims=True)
        row = jnp.sum(jnp.where(rows == step, left, 0.0), axis=0, keepdims=True)
        pivot = jnp.sum(jnp.where(row_ids == step, column, 0.0), axis=0, keepdims=True)
        root = jnp.sqrt(pivot)
        low_column = jnp.where(row_ids >= step, column / root, 0.0)
        low_row = jnp.where(col_ids >= step, row / root, 0.0)
        low = jnp.where(cols == step, low_column, low)
        left = left - low_column * low_row
    chol_ref[...] = low
    block = residue_ref[...]
    for step in range(size):
        low_column = jnp.sum(jnp.where(cols == step, low, 0.0), axis=1, keepdims=True)
        diagonal = jnp.sum(jnp.where(row_ids == step, low_column, 0.0), axis=0, keepdims=True)
        solved = jnp.sum(jnp.where(row_ids == step, block, 0.0), axis=0, keepdims=True) / diagonal
        block = jnp.where(
            row_ids == step, solved, jnp.where(row_ids > step, block - low_column * solved, block)
        )
    block_ref[...] = block


def chol_solve(gram_matrix, residue):
    size, width = residue.shape
    return pl.pallas_call(
        chol_solve_kernel,
        out_shape=(
            jax.ShapeDtypeStruct((size, size), jnp.float32),
            jax.ShapeDtypeStruct((size, width), jnp.float32),
        ),
        in_specs=[pl.BlockSpec(memory_space=pltpu.VMEM)] * 2,
        out_specs=(pl.BlockSpec(memory_space=pltpu.VMEM), pl.BlockSpec(memory_space=pltpu.VMEM)),
        cost_estimate=pl.CostEstimate(
            flops=4 * size * size * (size + width), bytes_accessed=8 * size * (size + width), transcendentals=size
        ),
    )(gram_matrix, residue)


def on_device(
    vectors, sigma_point, leaf_basis, near_blocks, near_list, coupling, far_list, far_rank, krylov
):
    highest = lax.Precision.HIGHEST
    local_count, rank_width, leaf_size = leaf_basis.shape
    vec_count = vectors.shape[0]
    near_count = near_list.shape[1]
    slot_count = far_list.shape[1]
    coef_count = lax.axis_size("coef")
    leaf_count = lax.axis_size("leaf")
    group_size = local_count * coef_count
    reach_groups = min(8, leaf_count // 4)
    total_points = local_count * leaf_size * coef_count * leaf_count
    sigma_val = sigma_point[0]
    powers = jnp.stack([jnp.ones((), jnp.float32), sigma_val, sigma_val * sigma_val])
    rounded = vectors.astype(jnp.bfloat16)
    by_cluster = rounded.reshape(vec_count, local_count, leaf_size)
    coarse = jnp.einsum(
        "cki,vci->cvk", leaf_basis, by_cluster, preferred_element_type=jnp.float32
    ).astype(jnp.bfloat16)
    own_rows = coarse.reshape(1, local_count, vec_count * rank_width)
    by_leaf, leaf_xor = xor_gather(own_rows, "leaf", 0)
    window, coef_xor = xor_gather(by_leaf, "coef", 1)
    flat_rows = window.reshape(-1, vec_count * rank_width)
    source_group = far_list // group_size
    source_holder = (far_list % group_size) // local_count
    if leaf_xor:
        source_group = source_group ^ lax.axis_index("leaf")
    if coef_xor:
        source_holder = source_holder ^ lax.axis_index("coef")
    local_ids = (
        source_group * group_size + source_holder * local_count + far_list % local_count
    ).reshape(-1)
    sources = flat_rows.at[local_ids].get(mode="promise_in_bounds").reshape(
        group_size, slot_count, vec_count, rank_width
    )
    lane_ids = jnp.arange(rank_width, dtype=jnp.int32)
    keep_mask = lane_ids[None, None, :] < far_rank[:, :, None]
    sources = jnp.where(keep_mask[:, :, None, :], sources, jnp.zeros((), jnp.bfloat16))
    couple = coupling.reshape(3, group_size, slot_count, rank_width, rank_width)
    far_terms = jnp.einsum("cfvl,jcfkl->cfvjk", sources, couple, preferred_element_type=jnp.float32)
    weights = powers[None, None, None, :, None] * keep_mask[:, :, None, None, :].astype(jnp.float32)
    partial_far = jnp.sum(far_terms * weights, axis=(1, 3)).reshape(group_size, vec_count * rank_width)
    far_hat = butterfly_scatter(partial_far, "coef")
    far_round = far_hat.astype(jnp.bfloat16).reshape(local_count, vec_count, rank_width)
    far_part = jnp.einsum("cki,cvk->vci", leaf_basis, far_round, preferred_element_type=jnp.float32)
    extended = extended_2(rounded, ((("leaf", "coef"), 1),), local_count * leaf_size)
    extended = extended.reshape(vec_count, 3 * local_count, leaf_size)
    device_pos = lax.axis_index("leaf") * coef_count + lax.axis_index("coef")
    near_ids = (near_list - (device_pos - 1) * local_count).reshape(-1)
    near_src = extended.at[:, near_ids].get(mode="promise_in_bounds").reshape(
        vec_count, local_count, near_count, leaf_size
    )
    near_terms = jnp.einsum(
        "jcnil,vcnl->jvci", near_blocks, near_src, preferred_element_type=jnp.float32
    )
    near_part = jnp.tensordot(powers, near_terms, 1)
    applied = (far_part + near_part).reshape(vec_count, local_count * leaf_size)
    basis_count = krylov.shape[0]
    both_axes = ("leaf", "coef")
    proj_part = jnp.dot(krylov, applied.T, precision=highest)
    self_part = jnp.dot(applied, applied.T, precision=highest)
    summed = butterfly_sum(jnp.concatenate([proj_part, self_part], axis=0), both_axes)
    coeffs = summed[:basis_count]
    outer = summed[basis_count:]
    residue = applied - jnp.dot(coeffs.T, krylov, precision=highest)
    short_gram = (outer - jnp.dot(coeffs.T, coeffs, precision=highest)) / total_points
    eye = jnp.eye(vec_count, dtype=jnp.bool_)
    short_diag = jnp.sum(jnp.where(eye, short_gram, 0.0), axis=0)
    outer_diag = jnp.sum(jnp.where(eye, outer, 0.0), axis=0)
    kept = short_diag * (64 * total_points) >= outer_diag
    def exact_gram():
        part = jnp.dot(residue, residue.T, precision=highest)
        return butterfly_sum(part, both_axes) / total_points
    gram_matrix = lax.cond(jnp.all(kept), lambda: short_gram, exact_gram)
    chol_factor, new_block = chol_solve(gram_matrix, residue)
    return (new_block, coeffs, chol_factor)


def solution(mesh):
    in_specs = (
        P(None, ("leaf", "coef")),
        P(),
        P(("leaf", "coef"), None, None),
        P(None, ("leaf", "coef"), None, None, None),
        P(("leaf", "coef"), None),
        P(None, "leaf", "coef", None),
        P("leaf", "coef"),
        P("leaf", "coef"),
        P(None, ("leaf", "coef")),
    )
    out_specs = (P(None, ("leaf", "coef")), P(), P())
    return jax.shard_map(
        on_device, mesh=mesh, in_specs=in_specs, out_specs=out_specs, check_vma=False
    )
```

```python
import jax
import jax.numpy as jnp
from jax import lax
from jax.experimental import pallas as pl
from jax.experimental.pallas import tpu as pltpu
from jax.sharding import PartitionSpec as P


def shifted(block, axis, distance):
    devices = range(lax.axis_size(axis))
    route = [(i - distance, i) for i in devices if i - distance in devices]
    return lax.ppermute(block, axis, route)


def extended_2(block, sides, width):
    for axis, dim in sides:
        count = lax.axis_size(axis)
        forward = [(i, i + 1) for i in range(count - 1)]
        backward = [(target, source) for source, target in forward]
        low = lax.ppermute(
            lax.slice_in_dim(block, block.shape[dim] - width, None, axis=dim), axis, forward
        )
        high = lax.ppermute(lax.slice_in_dim(block, 0, width, axis=dim), axis, backward)
        block = jnp.concatenate([low, block, high], axis=dim)
    return block


def is_power_of_two(count):
    return count > 0 and count & (count - 1) == 0


def butterfly_sum(block, axes):
    total = 1
    for axis in axes:
        total *= lax.axis_size(axis)
    if not is_power_of_two(total):
        return lax.psum(block, axes)
    distance = 1
    while distance < total:
        route = [(i, i ^ distance) for i in range(total)]
        block = block + lax.ppermute(block, axes, route)
        distance *= 2
    return block


def xor_gather(block, axis, dim):
    count = lax.axis_size(axis)
    if not is_power_of_two(count):
        return lax.all_gather(block, axis, axis=dim, tiled=True), False
    distance = 1
    while distance < count:
        route = [(i, i ^ distance) for i in range(count)]
        block = jnp.concatenate([block, lax.ppermute(block, axis, route)], axis=dim)
        distance *= 2
    return block, True


def butterfly_scatter(block, axis):
    count = lax.axis_size(axis)
    if not is_power_of_two(count):
        return lax.psum_scatter(block, axis, scatter_dimension=0, tiled=True)
    me = lax.axis_index(axis)
    parts = block
    distance = count // 2
    while distance >= 1:
        halves = parts.reshape(2, parts.shape[0] // 2, *parts.shape[1:])
        bit = (me // distance) % 2
        keep = lax.dynamic_index_in_dim(halves, bit, axis=0, keepdims=False)
        give = lax.dynamic_index_in_dim(halves, 1 - bit, axis=0, keepdims=False)
        route = [(i, i ^ distance) for i in range(count)]
        parts = keep + lax.ppermute(give, axis, route)
        distance //= 2
    return parts


def group_reach(grouped, offsets):
    pieces = []
    for offset in offsets:
        if offset == 0:
            pieces.append(grouped)
        else:
            pieces.append(shifted(grouped, "leaf", -offset))
    return jnp.concatenate(pieces, axis=0)


def chol_solve_kernel(gram_ref, residue_ref, chol_ref, block_ref):
    left = gram_ref[...]
    size = left.shape[0]
    rows = lax.broadcasted_iota(jnp.int32, left.shape, 0)
    cols = lax.broadcasted_iota(jnp.int32, left.shape, 1)
    row_ids = lax.broadcasted_iota(jnp.int32, (size, 1), 0)
    col_ids = lax.broadcasted_iota(jnp.int32, (1, size), 1)
    low = jnp.zeros_like(left)
    for step in range(size):
        column = jnp.sum(jnp.where(cols == step, left, 0.0), axis=1, keepdims=True)
        row = jnp.sum(jnp.where(rows == step, left, 0.0), axis=0, keepdims=True)
        pivot = jnp.sum(jnp.where(row_ids == step, column, 0.0), axis=0, keepdims=True)
        root = jnp.sqrt(pivot)
        low_column = jnp.where(row_ids >= step, column / root, 0.0)
        low_row = jnp.where(col_ids >= step, row / root, 0.0)
        low = jnp.where(cols == step, low_column, low)
        left = left - low_column * low_row
    chol_ref[...] = low
    block = residue_ref[...]
    for step in range(size):
        low_column = jnp.sum(jnp.where(cols == step, low, 0.0), axis=1, keepdims=True)
        diagonal = jnp.sum(jnp.where(row_ids == step, low_column, 0.0), axis=0, keepdims=True)
        solved = jnp.sum(jnp.where(row_ids == step, block, 0.0), axis=0, keepdims=True) / diagonal
        block = jnp.where(
            row_ids == step, solved, jnp.where(row_ids > step, block - low_column * solved, block)
        )
    block_ref[...] = block


def chol_solve(gram_matrix, residue):
    size, width = residue.shape
    return pl.pallas_call(
        chol_solve_kernel,
        out_shape=(
            jax.ShapeDtypeStruct((size, size), jnp.float32),
            jax.ShapeDtypeStruct((size, width), jnp.float32),
        ),
        in_specs=[pl.BlockSpec(memory_space=pltpu.VMEM)] * 2,
        out_specs=(pl.BlockSpec(memory_space=pltpu.VMEM), pl.BlockSpec(memory_space=pltpu.VMEM)),
        cost_estimate=pl.CostEstimate(
            flops=4 * size * size * (size + width), bytes_accessed=8 * size * (size + width), transcendentals=size
        ),
    )(gram_matrix, residue)


def on_device(
    vectors, sigma_point, leaf_basis, near_blocks, near_list, coupling, far_list, far_rank, krylov
):
    highest = lax.Precision.HIGHEST
    local_count, rank_width, leaf_size = leaf_basis.shape
    vec_count = vectors.shape[0]
    near_count = near_list.shape[1]
    slot_count = far_list.shape[1]
    coef_count = lax.axis_size("coef")
    leaf_count = lax.axis_size("leaf")
    group_size = local_count * coef_count
    reach_groups = min(8, leaf_count // 4)
    total_points = local_count * leaf_size * coef_count * leaf_count
    sigma_val = sigma_point[0]
    powers = jnp.stack([jnp.ones((), jnp.float32), sigma_val, sigma_val * sigma_val])
    rounded = vectors.astype(jnp.bfloat16)
    by_cluster = rounded.reshape(vec_count, local_count, leaf_size)
    coarse = jnp.einsum(
        "cki,vci->cvk", leaf_basis, by_cluster, preferred_element_type=jnp.float32
    ).astype(jnp.bfloat16)
    own_rows = coarse.reshape(1, local_count, vec_count * rank_width)
    by_leaf, leaf_xor = xor_gather(own_rows, "leaf", 0)
    window, coef_xor = xor_gather(by_leaf, "coef", 1)
    flat_rows = window.reshape(-1, vec_count * rank_width)
    source_group = far_list // group_size
    source_holder = (far_list % group_size) // local_count
    if leaf_xor:
        source_group = source_group ^ lax.axis_index("leaf")
    if coef_xor:
        source_holder = source_holder ^ lax.axis_index("coef")
    local_ids = (
        source_group * group_size + source_holder * local_count + far_list % local_count
    ).reshape(-1)
    sources = flat_rows.at[local_ids].get(mode="promise_in_bounds").reshape(
        group_size, slot_count, vec_count, rank_width
    )
    lane_ids = jnp.arange(rank_width, dtype=jnp.int32)
    keep_mask = lane_ids[None, None, :] < far_rank[:, :, None]
    sources = jnp.where(keep_mask[:, :, None, :], sources, jnp.zeros((), jnp.bfloat16))
    couple = coupling.reshape(3, group_size, slot_count, rank_width, rank_width)
    far_terms = jnp.einsum("cfvl,jcfkl->cfvjk", sources, couple, preferred_element_type=jnp.float32)
    weights = powers[None, None, None, :, None] * keep_mask[:, :, None, None, :].astype(jnp.float32)
    partial_far = jnp.sum(far_terms * weights, axis=(1, 3))
    far_hat = butterfly_scatter(partial_far, "coef")
    far_round = far_hat.astype(jnp.bfloat16).reshape(local_count, vec_count, rank_width)
    far_part = jnp.einsum("cki,cvk->vci", leaf_basis, far_round, preferred_element_type=jnp.float32)
    extended = extended_2(rounded, ((("leaf", "coef"), 1),), local_count * leaf_size)
    extended = extended.reshape(vec_count, 3 * local_count, leaf_size)
    device_pos = lax.axis_index("leaf") * coef_count + lax.axis_index("coef")
    near_ids = (near_list - (device_pos - 1) * local_count).reshape(-1)
    near_src = extended.at[:, near_ids].get(mode="promise_in_bounds").reshape(
        vec_count, local_count, near_count, leaf_size
    )
    near_terms = jnp.einsum(
        "jcnil,vcnl->jvci", near_blocks, near_src, preferred_element_type=jnp.float32
    )
    near_part = jnp.tensordot(powers, near_terms, 1)
    applied = (far_part + near_part).reshape(vec_count, local_count * leaf_size)
    basis_count = krylov.shape[0]
    both_axes = ("leaf", "coef")
    proj_part = jnp.dot(krylov, applied.T, precision=highest)
    self_part = jnp.dot(applied, applied.T, precision=highest)
    summed = butterfly_sum(jnp.concatenate([proj_part, self_part], axis=0), both_axes)
    coeffs = summed[:basis_count]
    outer = summed[basis_count:]
    residue = applied - jnp.dot(coeffs.T, krylov, precision=highest)
    short_gram = (outer - jnp.dot(coeffs.T, coeffs, precision=highest)) / total_points
    eye = jnp.eye(vec_count, dtype=jnp.bool_)
    short_diag = jnp.sum(jnp.where(eye, short_gram, 0.0), axis=0)
    outer_diag = jnp.sum(jnp.where(eye, outer, 0.0), axis=0)
    kept = short_diag * (64 * total_points) >= outer_diag
    def exact_gram():
        part = jnp.dot(residue, residue.T, precision=highest)
        return butterfly_sum(part, both_axes) / total_points
    gram_matrix = lax.cond(jnp.all(kept), lambda: short_gram, exact_gram)
    chol_factor, new_block = chol_solve(gram_matrix, residue)
    return (new_block, coeffs, chol_factor)


def solution(mesh):
    in_specs = (
        P(None, ("leaf", "coef")),
        P(),
        P(("leaf", "coef"), None, None),
        P(None, ("leaf", "coef"), None, None, None),
        P(("leaf", "coef"), None),
        P(None, "leaf", "coef", None),
        P("leaf", "coef"),
        P("leaf", "coef"),
        P(None, ("leaf", "coef")),
    )
    out_specs = (P(None, ("leaf", "coef")), P(), P())
    return jax.shard_map(
        on_device, mesh=mesh, in_specs=in_specs, out_specs=out_specs, check_vma=False
    )
```

```python
import functools

import jax
import jax.numpy as jnp
from jax import lax
from jax.experimental import pallas as pl
from jax.experimental.pallas import tpu as pltpu
from jax.sharding import PartitionSpec as P


def shifted(block, axis, distance):
    devices = range(lax.axis_size(axis))
    route = [(i - distance, i) for i in devices if i - distance in devices]
    return lax.ppermute(block, axis, route)


def extended_2(block, sides, width):
    for axis, dim in sides:
        count = lax.axis_size(axis)
        forward = [(i, i + 1) for i in range(count - 1)]
        backward = [(target, source) for source, target in forward]
        low = lax.ppermute(
            lax.slice_in_dim(block, block.shape[dim] - width, None, axis=dim), axis, forward
        )
        high = lax.ppermute(lax.slice_in_dim(block, 0, width, axis=dim), axis, backward)
        block = jnp.concatenate([low, block, high], axis=dim)
    return block


def is_power_of_two(count):
    return count > 0 and count & (count - 1) == 0


def butterfly_sum(block, axes):
    total = 1
    for axis in axes:
        total *= lax.axis_size(axis)
    if not is_power_of_two(total):
        return lax.psum(block, axes)
    distance = 1
    while distance < total:
        route = [(i, i ^ distance) for i in range(total)]
        block = block + lax.ppermute(block, axes, route)
        distance *= 2
    return block


def xor_gather(block, axis, dim):
    count = lax.axis_size(axis)
    if not is_power_of_two(count):
        return lax.all_gather(block, axis, axis=dim, tiled=True), False
    distance = 1
    while distance < count:
        route = [(i, i ^ distance) for i in range(count)]
        block = jnp.concatenate([block, lax.ppermute(block, axis, route)], axis=dim)
        distance *= 2
    return block, True


def butterfly_scatter(block, axis):
    count = lax.axis_size(axis)
    if not is_power_of_two(count):
        return lax.psum_scatter(block, axis, scatter_dimension=0, tiled=True)
    me = lax.axis_index(axis)
    parts = block
    distance = count // 2
    while distance >= 1:
        halves = parts.reshape(2, parts.shape[0] // 2, *parts.shape[1:])
        bit = (me // distance) % 2
        keep = lax.dynamic_index_in_dim(halves, bit, axis=0, keepdims=False)
        give = lax.dynamic_index_in_dim(halves, 1 - bit, axis=0, keepdims=False)
        route = [(i, i ^ distance) for i in range(count)]
        parts = keep + lax.ppermute(give, axis, route)
        distance //= 2
    return parts


def group_reach(grouped, offsets):
    pieces = []
    for offset in offsets:
        if offset == 0:
            pieces.append(grouped)
        else:
            pieces.append(shifted(grouped, "leaf", -offset))
    return jnp.concatenate(pieces, axis=0)


def cholesky_and_solve(left, block):
    size = left.shape[0]
    rows = lax.broadcasted_iota(jnp.int32, left.shape, 0)
    cols = lax.broadcasted_iota(jnp.int32, left.shape, 1)
    row_ids = lax.broadcasted_iota(jnp.int32, (size, 1), 0)
    col_ids = lax.broadcasted_iota(jnp.int32, (1, size), 1)
    low = jnp.zeros_like(left)
    for step in range(size):
        column = jnp.sum(jnp.where(cols == step, left, 0.0), axis=1, keepdims=True)
        row = jnp.sum(jnp.where(rows == step, left, 0.0), axis=0, keepdims=True)
        pivot = jnp.sum(jnp.where(row_ids == step, column, 0.0), axis=0, keepdims=True)
        root = jnp.sqrt(pivot)
        low_column = jnp.where(row_ids >= step, column / root, 0.0)
        low_row = jnp.where(col_ids >= step, row / root, 0.0)
        low = jnp.where(cols == step, low_column, low)
        left = left - low_column * low_row
    for step in range(size):
        low_column = jnp.sum(jnp.where(cols == step, low, 0.0), axis=1, keepdims=True)
        diagonal = jnp.sum(jnp.where(row_ids == step, low_column, 0.0), axis=0, keepdims=True)
        solved = jnp.sum(jnp.where(row_ids == step, block, 0.0), axis=0, keepdims=True) / diagonal
        block = jnp.where(
            row_ids == step, solved, jnp.where(row_ids > step, block - low_column * solved, block)
        )
    return low, block


def chol_solve_kernel(gram_ref, residue_ref, chol_ref, block_ref):
    low, block = cholesky_and_solve(gram_ref[...], residue_ref[...])
    chol_ref[...] = low
    block_ref[...] = block


def fast_tail_kernel(scale, coeffs_ref, outer_ref, applied_ref, krylov_ref, chol_ref, block_ref, flag_ref):
    highest = lax.Precision.HIGHEST
    coeffs_t = coeffs_ref[...]
    outer = outer_ref[...]
    residue = applied_ref[...] - jnp.dot(coeffs_t, krylov_ref[...], precision=highest)
    overlap = lax.dot_general(coeffs_t, coeffs_t, (((1,), (1,)), ((), ())), precision=highest)
    short = outer - overlap
    size = short.shape[0]
    rows = lax.broadcasted_iota(jnp.int32, short.shape, 0)
    cols = lax.broadcasted_iota(jnp.int32, short.shape, 1)
    on_diagonal = rows == cols
    short_diag = jnp.sum(jnp.where(on_diagonal, short, 0.0), axis=0, keepdims=True)
    outer_diag = jnp.sum(jnp.where(on_diagonal, outer, 0.0), axis=0, keepdims=True)
    failed = jnp.sum(jnp.where(short_diag * 64.0 >= outer_diag, 0.0, 1.0), axis=1, keepdims=True)
    flag_ref[...] = jnp.broadcast_to(failed, flag_ref.shape)
    low, block = cholesky_and_solve(short * scale, residue)
    chol_ref[...] = low
    block_ref[...] = block


def chol_solve(gram_matrix, residue):
    size, width = residue.shape
    return pl.pallas_call(
        chol_solve_kernel,
        out_shape=(
            jax.ShapeDtypeStruct((size, size), jnp.float32),
            jax.ShapeDtypeStruct((size, width), jnp.float32),
        ),
        in_specs=[pl.BlockSpec(memory_space=pltpu.VMEM)] * 2,
        out_specs=(pl.BlockSpec(memory_space=pltpu.VMEM), pl.BlockSpec(memory_space=pltpu.VMEM)),
        cost_estimate=pl.CostEstimate(
            flops=4 * size * size * (size + width), bytes_accessed=8 * size * (size + width), transcendentals=size
        ),
    )(gram_matrix, residue)


def fast_tail(coeffs_t, outer, applied, krylov, scale):
    size, width = applied.shape
    vmem = pl.BlockSpec(memory_space=pltpu.VMEM)
    return pl.pallas_call(
        functools.partial(fast_tail_kernel, scale),
        out_shape=(
            jax.ShapeDtypeStruct((size, size), jnp.float32),
            jax.ShapeDtypeStruct((size, width), jnp.float32),
            jax.ShapeDtypeStruct((8, 128), jnp.float32),
        ),
        in_specs=[vmem] * 4,
        out_specs=(vmem, vmem, vmem),
        cost_estimate=pl.CostEstimate(
            flops=4 * size * width * (size + krylov.shape[0]),
            bytes_accessed=4 * (krylov.size + 3 * applied.size),
            transcendentals=size,
        ),
    )(coeffs_t, outer, applied, krylov)


def on_device(
    vectors, sigma_point, leaf_basis, near_blocks, near_list, coupling, far_list, far_rank, krylov
):
    highest = lax.Precision.HIGHEST
    local_count, rank_width, leaf_size = leaf_basis.shape
    vec_count = vectors.shape[0]
    near_count = near_list.shape[1]
    slot_count = far_list.shape[1]
    coef_count = lax.axis_size("coef")
    leaf_count = lax.axis_size("leaf")
    group_size = local_count * coef_count
    reach_groups = min(8, leaf_count // 4)
    total_points = local_count * leaf_size * coef_count * leaf_count
    sigma_val = sigma_point[0]
    powers = jnp.stack([jnp.ones((), jnp.float32), sigma_val, sigma_val * sigma_val])
    rounded = vectors.astype(jnp.bfloat16)
    by_cluster = rounded.reshape(vec_count, local_count, leaf_size)
    coarse = jnp.einsum(
        "cki,vci->cvk", leaf_basis, by_cluster, preferred_element_type=jnp.float32
    ).astype(jnp.bfloat16)
    own_rows = coarse.reshape(1, local_count, vec_count * rank_width)
    by_leaf, leaf_xor = xor_gather(own_rows, "leaf", 0)
    window, coef_xor = xor_gather(by_leaf, "coef", 1)
    flat_rows = window.reshape(-1, vec_count * rank_width)
    source_group = far_list // group_size
    source_holder = (far_list % group_size) // local_count
    if leaf_xor:
        source_group = source_group ^ lax.axis_index("leaf")
    if coef_xor:
        source_holder = source_holder ^ lax.axis_index("coef")
    local_ids = (
        source_group * group_size + source_holder * local_count + far_list % local_count
    ).reshape(-1)
    sources = flat_rows.at[local_ids].get(mode="promise_in_bounds").reshape(
        group_size, slot_count, vec_count, rank_width
    )
    lane_ids = jnp.arange(rank_width, dtype=jnp.int32)
    keep_mask = lane_ids[None, None, :] < far_rank[:, :, None]
    sources = jnp.where(keep_mask[:, :, None, :], sources, jnp.zeros((), jnp.bfloat16))
    couple = coupling.reshape(3, group_size, slot_count, rank_width, rank_width)
    far_terms = jnp.einsum("cfvl,jcfkl->cfvjk", sources, couple, preferred_element_type=jnp.float32)
    weights = powers[None, None, None, :, None] * keep_mask[:, :, None, None, :].astype(jnp.float32)
    partial_far = jnp.sum(far_terms * weights, axis=(1, 3))
    far_hat = butterfly_scatter(partial_far, "coef")
    far_round = far_hat.astype(jnp.bfloat16).reshape(local_count, vec_count, rank_width)
    far_part = jnp.einsum("cki,cvk->vci", leaf_basis, far_round, preferred_element_type=jnp.float32)
    extended = extended_2(rounded, ((("leaf", "coef"), 1),), local_count * leaf_size)
    extended = extended.reshape(vec_count, 3 * local_count, leaf_size)
    device_pos = lax.axis_index("leaf") * coef_count + lax.axis_index("coef")
    near_ids = (near_list - (device_pos - 1) * local_count).reshape(-1)
    near_src = extended.at[:, near_ids].get(mode="promise_in_bounds").reshape(
        vec_count, local_count, near_count, leaf_size
    )
    near_terms = jnp.einsum(
        "jcnil,vcnl->jvci", near_blocks, near_src, preferred_element_type=jnp.float32
    )
    near_part = jnp.tensordot(powers, near_terms, 1)
    applied = (far_part + near_part).reshape(vec_count, local_count * leaf_size)
    basis_count = krylov.shape[0]
    both_axes = ("leaf", "coef")
    proj_part = jnp.dot(krylov, applied.T, precision=highest)
    self_part = jnp.dot(applied, applied.T, precision=highest)
    summed = butterfly_sum(jnp.concatenate([proj_part, self_part], axis=0), both_axes)
    coeffs = summed[:basis_count]
    outer = summed[basis_count:]
    chol_fast, block_fast, failed = fast_tail(
        coeffs.T, outer, applied, krylov, 1.0 / total_points
    )
    def exact_path():
        residue = applied - jnp.dot(coeffs.T, krylov, precision=highest)
        part = jnp.dot(residue, residue.T, precision=highest)
        return chol_solve(butterfly_sum(part, both_axes) / total_points, residue)
    chol_factor, new_block = lax.cond(
        failed[0, 0] > 0, exact_path, lambda: (chol_fast, block_fast)
    )
    return (new_block, coeffs, chol_factor)


def solution(mesh):
    in_specs = (
        P(None, ("leaf", "coef")),
        P(),
        P(("leaf", "coef"), None, None),
        P(None, ("leaf", "coef"), None, None, None),
        P(("leaf", "coef"), None),
        P(None, "leaf", "coef", None),
        P("leaf", "coef"),
        P("leaf", "coef"),
        P(None, ("leaf", "coef")),
    )
    out_specs = (P(None, ("leaf", "coef")), P(), P())
    return jax.shard_map(
        on_device, mesh=mesh, in_specs=in_specs, out_specs=out_specs, check_vma=False
    )
```

```python
import jax
import jax.numpy as jnp
from jax import lax
from jax.experimental import pallas as pl
from jax.experimental.pallas import tpu as pltpu
from jax.sharding import PartitionSpec as P


def shifted(block, axis, distance):
    devices = range(lax.axis_size(axis))
    route = [(i - distance, i) for i in devices if i - distance in devices]
    return lax.ppermute(block, axis, route)


def extended_2(block, sides, width):
    for axis, dim in sides:
        count = lax.axis_size(axis)
        forward = [(i, i + 1) for i in range(count - 1)]
        backward = [(target, source) for source, target in forward]
        low = lax.ppermute(
            lax.slice_in_dim(block, block.shape[dim] - width, None, axis=dim), axis, forward
        )
        high = lax.ppermute(lax.slice_in_dim(block, 0, width, axis=dim), axis, backward)
        block = jnp.concatenate([low, block, high], axis=dim)
    return block


def is_power_of_two(count):
    return count > 0 and count & (count - 1) == 0


def butterfly_sum(block, axes):
    total = 1
    for axis in axes:
        total *= lax.axis_size(axis)
    if not is_power_of_two(total):
        return lax.psum(block, axes)
    distance = 1
    while distance < total:
        route = [(i, i ^ distance) for i in range(total)]
        block = block + lax.ppermute(block, axes, route)
        distance *= 2
    return block


def xor_gather(block, axis, dim):
    count = lax.axis_size(axis)
    if not is_power_of_two(count):
        return lax.all_gather(block, axis, axis=dim, tiled=True), False
    distance = count // 2
    while distance >= 1:
        route = [(i, i ^ distance) for i in range(count)]
        block = jnp.concatenate([block, lax.ppermute(block, axis, route)], axis=dim)
        distance //= 2
    return block, True


def xor_position(difference, count):
    position = jnp.zeros_like(difference)
    distance, place = count // 2, 1
    while distance >= 1:
        position = position + ((difference // distance) % 2) * place
        distance //= 2
        place *= 2
    return position


def butterfly_scatter(block, axis):
    count = lax.axis_size(axis)
    if not is_power_of_two(count):
        return lax.psum_scatter(block, axis, scatter_dimension=0, tiled=True)
    me = lax.axis_index(axis)
    parts = block
    distance = count // 2
    while distance >= 1:
        halves = parts.reshape(2, parts.shape[0] // 2, *parts.shape[1:])
        bit = (me // distance) % 2
        keep = lax.dynamic_index_in_dim(halves, bit, axis=0, keepdims=False)
        give = lax.dynamic_index_in_dim(halves, 1 - bit, axis=0, keepdims=False)
        route = [(i, i ^ distance) for i in range(count)]
        parts = keep + lax.ppermute(give, axis, route)
        distance //= 2
    return parts


def group_reach(grouped, offsets):
    pieces = []
    for offset in offsets:
        if offset == 0:
            pieces.append(grouped)
        else:
            pieces.append(shifted(grouped, "leaf", -offset))
    return jnp.concatenate(pieces, axis=0)


def chol_solve_kernel(gram_ref, residue_ref, chol_ref, block_ref):
    left = gram_ref[...]
    size = left.shape[0]
    rows = lax.broadcasted_iota(jnp.int32, left.shape, 0)
    cols = lax.broadcasted_iota(jnp.int32, left.shape, 1)
    row_ids = lax.broadcasted_iota(jnp.int32, (size, 1), 0)
    col_ids = lax.broadcasted_iota(jnp.int32, (1, size), 1)
    low = jnp.zeros_like(left)
    for step in range(size):
        column = jnp.sum(jnp.where(cols == step, left, 0.0), axis=1, keepdims=True)
        row = jnp.sum(jnp.where(rows == step, left, 0.0), axis=0, keepdims=True)
        pivot = jnp.sum(jnp.where(row_ids == step, column, 0.0), axis=0, keepdims=True)
        root = jnp.sqrt(pivot)
        low_column = jnp.where(row_ids >= step, column / root, 0.0)
        low_row = jnp.where(col_ids >= step, row / root, 0.0)
        low = jnp.where(cols == step, low_column, low)
        left = left - low_column * low_row
    chol_ref[...] = low
    block = residue_ref[...]
    for step in range(size):
        low_column = jnp.sum(jnp.where(cols == step, low, 0.0), axis=1, keepdims=True)
        diagonal = jnp.sum(jnp.where(row_ids == step, low_column, 0.0), axis=0, keepdims=True)
        solved = jnp.sum(jnp.where(row_ids == step, block, 0.0), axis=0, keepdims=True) / diagonal
        block = jnp.where(
            row_ids == step, solved, jnp.where(row_ids > step, block - low_column * solved, block)
        )
    block_ref[...] = block


def chol_solve(gram_matrix, residue):
    size, width = residue.shape
    return pl.pallas_call(
        chol_solve_kernel,
        out_shape=(
            jax.ShapeDtypeStruct((size, size), jnp.float32),
            jax.ShapeDtypeStruct((size, width), jnp.float32),
        ),
        in_specs=[pl.BlockSpec(memory_space=pltpu.VMEM)] * 2,
        out_specs=(pl.BlockSpec(memory_space=pltpu.VMEM), pl.BlockSpec(memory_space=pltpu.VMEM)),
        cost_estimate=pl.CostEstimate(
            flops=4 * size * size * (size + width), bytes_accessed=8 * size * (size + width), transcendentals=size
        ),
    )(gram_matrix, residue)


def on_device(
    vectors, sigma_point, leaf_basis, near_blocks, near_list, coupling, far_list, far_rank, krylov
):
    highest = lax.Precision.HIGHEST
    local_count, rank_width, leaf_size = leaf_basis.shape
    vec_count = vectors.shape[0]
    near_count = near_list.shape[1]
    slot_count = far_list.shape[1]
    coef_count = lax.axis_size("coef")
    leaf_count = lax.axis_size("leaf")
    group_size = local_count * coef_count
    reach_groups = min(8, leaf_count // 4)
    total_points = local_count * leaf_size * coef_count * leaf_count
    sigma_val = sigma_point[0]
    powers = jnp.stack([jnp.ones((), jnp.float32), sigma_val, sigma_val * sigma_val])
    rounded = vectors.astype(jnp.bfloat16)
    by_cluster = rounded.reshape(vec_count, local_count, leaf_size)
    coarse = jnp.einsum(
        "cki,vci->cvk", leaf_basis, by_cluster, preferred_element_type=jnp.float32
    ).astype(jnp.bfloat16)
    own_rows = coarse.reshape(1, local_count, vec_count * rank_width)
    by_leaf, leaf_xor = xor_gather(own_rows, "leaf", 0)
    window, coef_xor = xor_gather(by_leaf, "coef", 1)
    flat_rows = window.reshape(-1, vec_count * rank_width)
    source_group = far_list // group_size
    source_holder = (far_list % group_size) // local_count
    if leaf_xor:
        source_group = xor_position(source_group ^ lax.axis_index("leaf"), leaf_count)
    if coef_xor:
        source_holder = xor_position(source_holder ^ lax.axis_index("coef"), coef_count)
    local_ids = (
        source_group * group_size + source_holder * local_count + far_list % local_count
    ).reshape(-1)
    sources = flat_rows.at[local_ids].get(mode="promise_in_bounds").reshape(
        group_size, slot_count, vec_count, rank_width
    )
    lane_ids = jnp.arange(rank_width, dtype=jnp.int32)
    keep_mask = lane_ids[None, None, :] < far_rank[:, :, None]
    sources = jnp.where(keep_mask[:, :, None, :], sources, jnp.zeros((), jnp.bfloat16))
    couple = coupling.reshape(3, group_size, slot_count, rank_width, rank_width)
    far_terms = jnp.einsum("cfvl,jcfkl->cfvjk", sources, couple, preferred_element_type=jnp.float32)
    weights = powers[None, None, None, :, None] * keep_mask[:, :, None, None, :].astype(jnp.float32)
    partial_far = jnp.sum(far_terms * weights, axis=(1, 3))
    far_hat = butterfly_scatter(partial_far, "coef")
    far_round = far_hat.astype(jnp.bfloat16).reshape(local_count, vec_count, rank_width)
    far_part = jnp.einsum("cki,cvk->vci", leaf_basis, far_round, preferred_element_type=jnp.float32)
    extended = extended_2(rounded, ((("leaf", "coef"), 1),), local_count * leaf_size)
    extended = extended.reshape(vec_count, 3 * local_count, leaf_size)
    device_pos = lax.axis_index("leaf") * coef_count + lax.axis_index("coef")
    near_ids = (near_list - (device_pos - 1) * local_count).reshape(-1)
    near_src = extended.at[:, near_ids].get(mode="promise_in_bounds").reshape(
        vec_count, local_count, near_count, leaf_size
    )
    near_terms = jnp.einsum(
        "jcnil,vcnl->jvci", near_blocks, near_src, preferred_element_type=jnp.float32
    )
    near_part = jnp.tensordot(powers, near_terms, 1)
    applied = (far_part + near_part).reshape(vec_count, local_count * leaf_size)
    basis_count = krylov.shape[0]
    both_axes = ("leaf", "coef")
    proj_part = jnp.dot(krylov, applied.T, precision=highest)
    self_part = jnp.dot(applied, applied.T, precision=highest)
    summed = butterfly_sum(jnp.concatenate([proj_part, self_part], axis=0), both_axes)
    coeffs = summed[:basis_count]
    outer = summed[basis_count:]
    residue = applied - jnp.dot(coeffs.T, krylov, precision=highest)
    short_gram = (outer - jnp.dot(coeffs.T, coeffs, precision=highest)) / total_points
    eye = jnp.eye(vec_count, dtype=jnp.bool_)
    short_diag = jnp.sum(jnp.where(eye, short_gram, 0.0), axis=0)
    outer_diag = jnp.sum(jnp.where(eye, outer, 0.0), axis=0)
    kept = short_diag * (64 * total_points) >= outer_diag
    def exact_gram():
        part = jnp.dot(residue, residue.T, precision=highest)
        return butterfly_sum(part, both_axes) / total_points
    gram_matrix = lax.cond(jnp.all(kept), lambda: short_gram, exact_gram)
    chol_factor, new_block = chol_solve(gram_matrix, residue)
    return (new_block, coeffs, chol_factor)


def solution(mesh):
    in_specs = (
        P(None, ("leaf", "coef")),
        P(),
        P(("leaf", "coef"), None, None),
        P(None, ("leaf", "coef"), None, None, None),
        P(("leaf", "coef"), None),
        P(None, "leaf", "coef", None),
        P("leaf", "coef"),
        P("leaf", "coef"),
        P(None, ("leaf", "coef")),
    )
    out_specs = (P(None, ("leaf", "coef")), P(), P())
    return jax.shard_map(
        on_device, mesh=mesh, in_specs=in_specs, out_specs=out_specs, check_vma=False
    )
```

```python
import jax
import jax.numpy as jnp
from jax import lax
from jax.experimental import pallas as pl
from jax.experimental.pallas import tpu as pltpu
from jax.sharding import PartitionSpec as P


def shifted(block, axis, distance):
    devices = range(lax.axis_size(axis))
    route = [(i - distance, i) for i in devices if i - distance in devices]
    return lax.ppermute(block, axis, route)


def extended_2(block, sides, width):
    for axis, dim in sides:
        count = lax.axis_size(axis)
        forward = [(i, i + 1) for i in range(count - 1)]
        backward = [(target, source) for source, target in forward]
        low = lax.ppermute(
            lax.slice_in_dim(block, block.shape[dim] - width, None, axis=dim), axis, forward
        )
        high = lax.ppermute(lax.slice_in_dim(block, 0, width, axis=dim), axis, backward)
        block = jnp.concatenate([low, block, high], axis=dim)
    return block


def is_power_of_two(count):
    return count > 0 and count & (count - 1) == 0


def butterfly_sum(block, axes):
    total = 1
    for axis in axes:
        total *= lax.axis_size(axis)
    if not is_power_of_two(total):
        return lax.psum(block, axes)
    distance = 1
    while distance < total:
        route = [(i, i ^ distance) for i in range(total)]
        block = block + lax.ppermute(block, axes, route)
        distance *= 2
    return block


def xor_gather(block, axis, dim, descending=False):
    count = lax.axis_size(axis)
    if not is_power_of_two(count):
        return lax.all_gather(block, axis, axis=dim, tiled=True), False
    distances = []
    distance = 1
    while distance < count:
        distances.append(distance)
        distance *= 2
    if descending:
        distances.reverse()
    for distance in distances:
        route = [(i, i ^ distance) for i in range(count)]
        block = jnp.concatenate([block, lax.ppermute(block, axis, route)], axis=dim)
    return block, True


def xor_position(difference, count):
    position = jnp.zeros_like(difference)
    distance, place = count // 2, 1
    while distance >= 1:
        position = position + ((difference // distance) % 2) * place
        distance //= 2
        place *= 2
    return position


def butterfly_scatter(block, axis):
    count = lax.axis_size(axis)
    if not is_power_of_two(count):
        return lax.psum_scatter(block, axis, scatter_dimension=0, tiled=True)
    me = lax.axis_index(axis)
    parts = block
    distance = count // 2
    while distance >= 1:
        halves = parts.reshape(2, parts.shape[0] // 2, *parts.shape[1:])
        bit = (me // distance) % 2
        keep = lax.dynamic_index_in_dim(halves, bit, axis=0, keepdims=False)
        give = lax.dynamic_index_in_dim(halves, 1 - bit, axis=0, keepdims=False)
        route = [(i, i ^ distance) for i in range(count)]
        parts = keep + lax.ppermute(give, axis, route)
        distance //= 2
    return parts


def group_reach(grouped, offsets):
    pieces = []
    for offset in offsets:
        if offset == 0:
            pieces.append(grouped)
        else:
            pieces.append(shifted(grouped, "leaf", -offset))
    return jnp.concatenate(pieces, axis=0)


def chol_solve_kernel(gram_ref, residue_ref, chol_ref, block_ref):
    left = gram_ref[...]
    size = left.shape[0]
    rows = lax.broadcasted_iota(jnp.int32, left.shape, 0)
    cols = lax.broadcasted_iota(jnp.int32, left.shape, 1)
    row_ids = lax.broadcasted_iota(jnp.int32, (size, 1), 0)
    col_ids = lax.broadcasted_iota(jnp.int32, (1, size), 1)
    low = jnp.zeros_like(left)
    for step in range(size):
        column = jnp.sum(jnp.where(cols == step, left, 0.0), axis=1, keepdims=True)
        row = jnp.sum(jnp.where(rows == step, left, 0.0), axis=0, keepdims=True)
        pivot = jnp.sum(jnp.where(row_ids == step, column, 0.0), axis=0, keepdims=True)
        root = jnp.sqrt(pivot)
        low_column = jnp.where(row_ids >= step, column / root, 0.0)
        low_row = jnp.where(col_ids >= step, row / root, 0.0)
        low = jnp.where(cols == step, low_column, low)
        left = left - low_column * low_row
    chol_ref[...] = low
    block = residue_ref[...]
    for step in range(size):
        low_column = jnp.sum(jnp.where(cols == step, low, 0.0), axis=1, keepdims=True)
        diagonal = jnp.sum(jnp.where(row_ids == step, low_column, 0.0), axis=0, keepdims=True)
        solved = jnp.sum(jnp.where(row_ids == step, block, 0.0), axis=0, keepdims=True) / diagonal
        block = jnp.where(
            row_ids == step, solved, jnp.where(row_ids > step, block - low_column * solved, block)
        )
    block_ref[...] = block


def chol_solve(gram_matrix, residue):
    size, width = residue.shape
    return pl.pallas_call(
        chol_solve_kernel,
        out_shape=(
            jax.ShapeDtypeStruct((size, size), jnp.float32),
            jax.ShapeDtypeStruct((size, width), jnp.float32),
        ),
        in_specs=[pl.BlockSpec(memory_space=pltpu.VMEM)] * 2,
        out_specs=(pl.BlockSpec(memory_space=pltpu.VMEM), pl.BlockSpec(memory_space=pltpu.VMEM)),
        cost_estimate=pl.CostEstimate(
            flops=4 * size * size * (size + width), bytes_accessed=8 * size * (size + width), transcendentals=size
        ),
    )(gram_matrix, residue)


def on_device(
    vectors, sigma_point, leaf_basis, near_blocks, near_list, coupling, far_list, far_rank, krylov
):
    highest = lax.Precision.HIGHEST
    local_count, rank_width, leaf_size = leaf_basis.shape
    vec_count = vectors.shape[0]
    near_count = near_list.shape[1]
    slot_count = far_list.shape[1]
    coef_count = lax.axis_size("coef")
    leaf_count = lax.axis_size("leaf")
    group_size = local_count * coef_count
    reach_groups = min(8, leaf_count // 4)
    total_points = local_count * leaf_size * coef_count * leaf_count
    sigma_val = sigma_point[0]
    powers = jnp.stack([jnp.ones((), jnp.float32), sigma_val, sigma_val * sigma_val])
    rounded = vectors.astype(jnp.bfloat16)
    by_cluster = rounded.reshape(vec_count, local_count, leaf_size)
    coarse = jnp.einsum(
        "cki,vci->cvk", leaf_basis, by_cluster, preferred_element_type=jnp.float32
    ).astype(jnp.bfloat16)
    own_rows = coarse.reshape(1, local_count, vec_count * rank_width)
    by_leaf, leaf_xor = xor_gather(own_rows, "leaf", 0)
    window, coef_xor = xor_gather(by_leaf, "coef", 1, descending=True)
    flat_rows = window.reshape(-1, vec_count * rank_width)
    source_group = far_list // group_size
    source_holder = (far_list % group_size) // local_count
    if leaf_xor:
        source_group = source_group ^ lax.axis_index("leaf")
    if coef_xor:
        source_holder = xor_position(source_holder ^ lax.axis_index("coef"), coef_count)
    local_ids = (
        source_group * group_size + source_holder * local_count + far_list % local_count
    ).reshape(-1)
    sources = flat_rows.at[local_ids].get(mode="promise_in_bounds").reshape(
        group_size, slot_count, vec_count, rank_width
    )
    lane_ids = jnp.arange(rank_width, dtype=jnp.int32)
    keep_mask = lane_ids[None, None, :] < far_rank[:, :, None]
    sources = jnp.where(keep_mask[:, :, None, :], sources, jnp.zeros((), jnp.bfloat16))
    couple = coupling.reshape(3, group_size, slot_count, rank_width, rank_width)
    far_terms = jnp.einsum("cfvl,jcfkl->cfvjk", sources, couple, preferred_element_type=jnp.float32)
    weights = powers[None, None, None, :, None] * keep_mask[:, :, None, None, :].astype(jnp.float32)
    partial_far = jnp.sum(far_terms * weights, axis=(1, 3))
    far_hat = butterfly_scatter(partial_far, "coef")
    far_round = far_hat.astype(jnp.bfloat16).reshape(local_count, vec_count, rank_width)
    far_part = jnp.einsum("cki,cvk->vci", leaf_basis, far_round, preferred_element_type=jnp.float32)
    extended = extended_2(rounded, ((("leaf", "coef"), 1),), local_count * leaf_size)
    extended = extended.reshape(vec_count, 3 * local_count, leaf_size)
    device_pos = lax.axis_index("leaf") * coef_count + lax.axis_index("coef")
    near_ids = (near_list - (device_pos - 1) * local_count).reshape(-1)
    near_src = extended.at[:, near_ids].get(mode="promise_in_bounds").reshape(
        vec_count, local_count, near_count, leaf_size
    )
    near_terms = jnp.einsum(
        "jcnil,vcnl->jvci", near_blocks, near_src, preferred_element_type=jnp.float32
    )
    near_part = jnp.tensordot(powers, near_terms, 1)
    applied = (far_part + near_part).reshape(vec_count, local_count * leaf_size)
    basis_count = krylov.shape[0]
    both_axes = ("leaf", "coef")
    proj_part = jnp.dot(krylov, applied.T, precision=highest)
    self_part = jnp.dot(applied, applied.T, precision=highest)
    summed = butterfly_sum(jnp.concatenate([proj_part, self_part], axis=0), both_axes)
    coeffs = summed[:basis_count]
    outer = summed[basis_count:]
    residue = applied - jnp.dot(coeffs.T, krylov, precision=highest)
    short_gram = (outer - jnp.dot(coeffs.T, coeffs, precision=highest)) / total_points
    eye = jnp.eye(vec_count, dtype=jnp.bool_)
    short_diag = jnp.sum(jnp.where(eye, short_gram, 0.0), axis=0)
    outer_diag = jnp.sum(jnp.where(eye, outer, 0.0), axis=0)
    kept = short_diag * (64 * total_points) >= outer_diag
    def exact_gram():
        part = jnp.dot(residue, residue.T, precision=highest)
        return butterfly_sum(part, both_axes) / total_points
    gram_matrix = lax.cond(jnp.all(kept), lambda: short_gram, exact_gram)
    chol_factor, new_block = chol_solve(gram_matrix, residue)
    return (new_block, coeffs, chol_factor)


def solution(mesh):
    in_specs = (
        P(None, ("leaf", "coef")),
        P(),
        P(("leaf", "coef"), None, None),
        P(None, ("leaf", "coef"), None, None, None),
        P(("leaf", "coef"), None),
        P(None, "leaf", "coef", None),
        P("leaf", "coef"),
        P("leaf", "coef"),
        P(None, ("leaf", "coef")),
    )
    out_specs = (P(None, ("leaf", "coef")), P(), P())
    return jax.shard_map(
        on_device, mesh=mesh, in_specs=in_specs, out_specs=out_specs, check_vma=False
    )
```

```python
import jax
import jax.numpy as jnp
from jax import lax
from jax.experimental import pallas as pl
from jax.experimental.pallas import tpu as pltpu
from jax.sharding import PartitionSpec as P


def shifted(block, axis, distance):
    devices = range(lax.axis_size(axis))
    route = [(i - distance, i) for i in devices if i - distance in devices]
    return lax.ppermute(block, axis, route)


def extended_2(block, sides, width):
    for axis, dim in sides:
        count = lax.axis_size(axis)
        forward = [(i, i + 1) for i in range(count - 1)]
        backward = [(target, source) for source, target in forward]
        low = lax.ppermute(
            lax.slice_in_dim(block, block.shape[dim] - width, None, axis=dim), axis, forward
        )
        high = lax.ppermute(lax.slice_in_dim(block, 0, width, axis=dim), axis, backward)
        block = jnp.concatenate([low, block, high], axis=dim)
    return block


def is_power_of_two(count):
    return count > 0 and count & (count - 1) == 0


def butterfly_sum(block, axes):
    total = 1
    for axis in axes:
        total *= lax.axis_size(axis)
    if not is_power_of_two(total):
        return lax.psum(block, axes)
    distance = 1
    while distance < total:
        route = [(i, i ^ distance) for i in range(total)]
        block = block + lax.ppermute(block, axes, route)
        distance *= 2
    return block


def xor_gather(block, axis, dim, arrived=None):
    count = lax.axis_size(axis)
    if not is_power_of_two(count):
        return lax.all_gather(block, axis, axis=dim, tiled=True), False
    distance = 1
    while distance < count:
        route = [(i, i ^ distance) for i in range(count)]
        other = lax.ppermute(block, axis, route)
        if arrived is not None and not arrived:
            arrived.append(other)
        block = jnp.concatenate([block, other], axis=dim)
        distance *= 2
    return block, True


def butterfly_scatter(block, axis):
    count = lax.axis_size(axis)
    if not is_power_of_two(count):
        return lax.psum_scatter(block, axis, scatter_dimension=0, tiled=True)
    me = lax.axis_index(axis)
    parts = block
    distance = count // 2
    while distance >= 1:
        halves = parts.reshape(2, parts.shape[0] // 2, *parts.shape[1:])
        bit = (me // distance) % 2
        keep = lax.dynamic_index_in_dim(halves, bit, axis=0, keepdims=False)
        give = lax.dynamic_index_in_dim(halves, 1 - bit, axis=0, keepdims=False)
        route = [(i, i ^ distance) for i in range(count)]
        parts = keep + lax.ppermute(give, axis, route)
        distance //= 2
    return parts


def group_reach(grouped, offsets):
    pieces = []
    for offset in offsets:
        if offset == 0:
            pieces.append(grouped)
        else:
            pieces.append(shifted(grouped, "leaf", -offset))
    return jnp.concatenate(pieces, axis=0)


def chol_solve_kernel(gram_ref, residue_ref, chol_ref, block_ref):
    left = gram_ref[...]
    size = left.shape[0]
    rows = lax.broadcasted_iota(jnp.int32, left.shape, 0)
    cols = lax.broadcasted_iota(jnp.int32, left.shape, 1)
    row_ids = lax.broadcasted_iota(jnp.int32, (size, 1), 0)
    col_ids = lax.broadcasted_iota(jnp.int32, (1, size), 1)
    low = jnp.zeros_like(left)
    for step in range(size):
        column = jnp.sum(jnp.where(cols == step, left, 0.0), axis=1, keepdims=True)
        row = jnp.sum(jnp.where(rows == step, left, 0.0), axis=0, keepdims=True)
        pivot = jnp.sum(jnp.where(row_ids == step, column, 0.0), axis=0, keepdims=True)
        root = jnp.sqrt(pivot)
        low_column = jnp.where(row_ids >= step, column / root, 0.0)
        low_row = jnp.where(col_ids >= step, row / root, 0.0)
        low = jnp.where(cols == step, low_column, low)
        left = left - low_column * low_row
    chol_ref[...] = low
    block = residue_ref[...]
    for step in range(size):
        low_column = jnp.sum(jnp.where(cols == step, low, 0.0), axis=1, keepdims=True)
        diagonal = jnp.sum(jnp.where(row_ids == step, low_column, 0.0), axis=0, keepdims=True)
        solved = jnp.sum(jnp.where(row_ids == step, block, 0.0), axis=0, keepdims=True) / diagonal
        block = jnp.where(
            row_ids == step, solved, jnp.where(row_ids > step, block - low_column * solved, block)
        )
    block_ref[...] = block


def chol_solve(gram_matrix, residue):
    size, width = residue.shape
    return pl.pallas_call(
        chol_solve_kernel,
        out_shape=(
            jax.ShapeDtypeStruct((size, size), jnp.float32),
            jax.ShapeDtypeStruct((size, width), jnp.float32),
        ),
        in_specs=[pl.BlockSpec(memory_space=pltpu.VMEM)] * 2,
        out_specs=(pl.BlockSpec(memory_space=pltpu.VMEM), pl.BlockSpec(memory_space=pltpu.VMEM)),
        cost_estimate=pl.CostEstimate(
            flops=4 * size * size * (size + width), bytes_accessed=8 * size * (size + width), transcendentals=size
        ),
    )(gram_matrix, residue)


def on_device(
    vectors, sigma_point, leaf_basis, near_blocks, near_list, coupling, far_list, far_rank, krylov
):
    highest = lax.Precision.HIGHEST
    local_count, rank_width, leaf_size = leaf_basis.shape
    vec_count = vectors.shape[0]
    near_count = near_list.shape[1]
    slot_count = far_list.shape[1]
    coef_count = lax.axis_size("coef")
    leaf_count = lax.axis_size("leaf")
    group_size = local_count * coef_count
    reach_groups = min(8, leaf_count // 4)
    total_points = local_count * leaf_size * coef_count * leaf_count
    sigma_val = sigma_point[0]
    powers = jnp.stack([jnp.ones((), jnp.float32), sigma_val, sigma_val * sigma_val])
    rounded = vectors.astype(jnp.bfloat16)
    by_cluster = rounded.reshape(vec_count, local_count, leaf_size)
    coarse = jnp.einsum(
        "cki,vci->cvk", leaf_basis, by_cluster, preferred_element_type=jnp.float32
    ).astype(jnp.bfloat16)
    own_rows = coarse.reshape(1, local_count, vec_count * rank_width)
    arrived = []
    by_leaf, leaf_xor = xor_gather(own_rows, "leaf", 0, arrived)
    if arrived:
        later = (arrived[0][0, 0, 0] * 0).astype(jnp.int32)
        far_list = far_list + later
        far_rank = far_rank + later
        near_list = near_list + later
    window, coef_xor = xor_gather(by_leaf, "coef", 1)
    flat_rows = window.reshape(-1, vec_count * rank_width)
    source_group = far_list // group_size
    source_holder = (far_list % group_size) // local_count
    if leaf_xor:
        source_group = source_group ^ lax.axis_index("leaf")
    if coef_xor:
        source_holder = source_holder ^ lax.axis_index("coef")
    local_ids = (
        source_group * group_size + source_holder * local_count + far_list % local_count
    ).reshape(-1)
    sources = flat_rows.at[local_ids].get(mode="promise_in_bounds").reshape(
        group_size, slot_count, vec_count, rank_width
    )
    lane_ids = jnp.arange(rank_width, dtype=jnp.int32)
    keep_mask = lane_ids[None, None, :] < far_rank[:, :, None]
    sources = jnp.where(keep_mask[:, :, None, :], sources, jnp.zeros((), jnp.bfloat16))
    couple = coupling.reshape(3, group_size, slot_count, rank_width, rank_width)
    far_terms = jnp.einsum("cfvl,jcfkl->cfvjk", sources, couple, preferred_element_type=jnp.float32)
    weights = powers[None, None, None, :, None] * keep_mask[:, :, None, None, :].astype(jnp.float32)
    partial_far = jnp.sum(far_terms * weights, axis=(1, 3))
    far_hat = butterfly_scatter(partial_far, "coef")
    far_round = far_hat.astype(jnp.bfloat16).reshape(local_count, vec_count, rank_width)
    far_part = jnp.einsum("cki,cvk->vci", leaf_basis, far_round, preferred_element_type=jnp.float32)
    extended = extended_2(rounded, ((("leaf", "coef"), 1),), local_count * leaf_size)
    extended = extended.reshape(vec_count, 3 * local_count, leaf_size)
    device_pos = lax.axis_index("leaf") * coef_count + lax.axis_index("coef")
    near_ids = (near_list - (device_pos - 1) * local_count).reshape(-1)
    near_src = extended.at[:, near_ids].get(mode="promise_in_bounds").reshape(
        vec_count, local_count, near_count, leaf_size
    )
    near_terms = jnp.einsum(
        "jcnil,vcnl->jvci", near_blocks, near_src, preferred_element_type=jnp.float32
    )
    near_part = jnp.tensordot(powers, near_terms, 1)
    applied = (far_part + near_part).reshape(vec_count, local_count * leaf_size)
    basis_count = krylov.shape[0]
    both_axes = ("leaf", "coef")
    proj_part = jnp.dot(krylov, applied.T, precision=highest)
    self_part = jnp.dot(applied, applied.T, precision=highest)
    summed = butterfly_sum(jnp.concatenate([proj_part, self_part], axis=0), both_axes)
    coeffs = summed[:basis_count]
    outer = summed[basis_count:]
    residue = applied - jnp.dot(coeffs.T, krylov, precision=highest)
    short_gram = (outer - jnp.dot(coeffs.T, coeffs, precision=highest)) / total_points
    eye = jnp.eye(vec_count, dtype=jnp.bool_)
    short_diag = jnp.sum(jnp.where(eye, short_gram, 0.0), axis=0)
    outer_diag = jnp.sum(jnp.where(eye, outer, 0.0), axis=0)
    kept = short_diag * (64 * total_points) >= outer_diag
    def exact_gram():
        part = jnp.dot(residue, residue.T, precision=highest)
        return butterfly_sum(part, both_axes) / total_points
    gram_matrix = lax.cond(jnp.all(kept), lambda: short_gram, exact_gram)
    chol_factor, new_block = chol_solve(gram_matrix, residue)
    return (new_block, coeffs, chol_factor)


def solution(mesh):
    in_specs = (
        P(None, ("leaf", "coef")),
        P(),
        P(("leaf", "coef"), None, None),
        P(None, ("leaf", "coef"), None, None, None),
        P(("leaf", "coef"), None),
        P(None, "leaf", "coef", None),
        P("leaf", "coef"),
        P("leaf", "coef"),
        P(None, ("leaf", "coef")),
    )
    out_specs = (P(None, ("leaf", "coef")), P(), P())
    return jax.shard_map(
        on_device, mesh=mesh, in_specs=in_specs, out_specs=out_specs, check_vma=False
    )
```

```python
import jax
import jax.numpy as jnp
from jax import lax
from jax.experimental import pallas as pl
from jax.experimental.pallas import tpu as pltpu
from jax.sharding import PartitionSpec as P


def shifted(block, axis, distance):
    devices = range(lax.axis_size(axis))
    route = [(i - distance, i) for i in devices if i - distance in devices]
    return lax.ppermute(block, axis, route)


def extended_2(block, sides, width):
    for axis, dim in sides:
        count = lax.axis_size(axis)
        forward = [(i, i + 1) for i in range(count - 1)]
        backward = [(target, source) for source, target in forward]
        low = lax.ppermute(
            lax.slice_in_dim(block, block.shape[dim] - width, None, axis=dim), axis, forward
        )
        high = lax.ppermute(lax.slice_in_dim(block, 0, width, axis=dim), axis, backward)
        block = jnp.concatenate([low, block, high], axis=dim)
    return block


def is_power_of_two(count):
    return count > 0 and count & (count - 1) == 0


def butterfly_sum(block, axes):
    total = 1
    for axis in axes:
        total *= lax.axis_size(axis)
    if not is_power_of_two(total):
        return lax.psum(block, axes)
    distance = 1
    while distance < total:
        route = [(i, i ^ distance) for i in range(total)]
        block = block + lax.ppermute(block, axes, route)
        distance *= 2
    return block


def xor_gather(block, axis, dim):
    count = lax.axis_size(axis)
    if not is_power_of_two(count):
        return lax.all_gather(block, axis, axis=dim, tiled=True), False
    distance = 1
    while distance < count:
        route = [(i, i ^ distance) for i in range(count)]
        block = jnp.concatenate([block, lax.ppermute(block, axis, route)], axis=dim)
        distance *= 2
    return block, True


def butterfly_scatter(block, axis):
    count = lax.axis_size(axis)
    if not is_power_of_two(count):
        return lax.psum_scatter(block, axis, scatter_dimension=0, tiled=True)
    me = lax.axis_index(axis)
    parts = block
    distance = count // 2
    while distance >= 1:
        halves = parts.reshape(2, parts.shape[0] // 2, *parts.shape[1:])
        bit = (me // distance) % 2
        keep = lax.dynamic_index_in_dim(halves, bit, axis=0, keepdims=False)
        give = lax.dynamic_index_in_dim(halves, 1 - bit, axis=0, keepdims=False)
        route = [(i, i ^ distance) for i in range(count)]
        parts = keep + lax.ppermute(give, axis, route)
        distance //= 2
    return parts


def group_reach(grouped, offsets):
    pieces = []
    for offset in offsets:
        if offset == 0:
            pieces.append(grouped)
        else:
            pieces.append(shifted(grouped, "leaf", -offset))
    return jnp.concatenate(pieces, axis=0)


def chol_solve_kernel(gram_ref, residue_ref, chol_ref, block_ref):
    left = gram_ref[...]
    size = left.shape[0]
    rows = lax.broadcasted_iota(jnp.int32, left.shape, 0)
    cols = lax.broadcasted_iota(jnp.int32, left.shape, 1)
    row_ids = lax.broadcasted_iota(jnp.int32, (size, 1), 0)
    col_ids = lax.broadcasted_iota(jnp.int32, (1, size), 1)
    low = jnp.zeros_like(left)
    for step in range(size):
        column = jnp.sum(jnp.where(cols == step, left, 0.0), axis=1, keepdims=True)
        row = jnp.sum(jnp.where(rows == step, left, 0.0), axis=0, keepdims=True)
        pivot = jnp.sum(jnp.where(row_ids == step, column, 0.0), axis=0, keepdims=True)
        root = jnp.sqrt(pivot)
        low_column = jnp.where(row_ids >= step, column / root, 0.0)
        low_row = jnp.where(col_ids >= step, row / root, 0.0)
        low = jnp.where(cols == step, low_column, low)
        left = left - low_column * low_row
    chol_ref[...] = low
    block = residue_ref[...]
    for step in range(size):
        low_column = jnp.sum(jnp.where(cols == step, low, 0.0), axis=1, keepdims=True)
        diagonal = jnp.sum(jnp.where(row_ids == step, low_column, 0.0), axis=0, keepdims=True)
        solved = jnp.sum(jnp.where(row_ids == step, block, 0.0), axis=0, keepdims=True) / diagonal
        block = jnp.where(
            row_ids == step, solved, jnp.where(row_ids > step, block - low_column * solved, block)
        )
    block_ref[...] = block


def chol_solve(gram_matrix, residue):
    size, width = residue.shape
    return pl.pallas_call(
        chol_solve_kernel,
        out_shape=(
            jax.ShapeDtypeStruct((size, size), jnp.float32),
            jax.ShapeDtypeStruct((size, width), jnp.float32),
        ),
        in_specs=[pl.BlockSpec(memory_space=pltpu.VMEM)] * 2,
        out_specs=(pl.BlockSpec(memory_space=pltpu.VMEM), pl.BlockSpec(memory_space=pltpu.VMEM)),
        cost_estimate=pl.CostEstimate(
            flops=4 * size * size * (size + width), bytes_accessed=8 * size * (size + width), transcendentals=size
        ),
    )(gram_matrix, residue)


def on_device(
    vectors, sigma_point, leaf_basis, near_blocks, near_list, coupling, far_list, far_rank, krylov
):
    highest = lax.Precision.HIGHEST
    local_count, rank_width, leaf_size = leaf_basis.shape
    vec_count = vectors.shape[0]
    near_count = near_list.shape[1]
    slot_count = far_list.shape[1]
    coef_count = lax.axis_size("coef")
    leaf_count = lax.axis_size("leaf")
    group_size = local_count * coef_count
    reach_groups = min(8, leaf_count // 4)
    total_points = local_count * leaf_size * coef_count * leaf_count
    sigma_val = sigma_point[0]
    powers = jnp.stack([jnp.ones((), jnp.float32), sigma_val, sigma_val * sigma_val])
    rounded = vectors.astype(jnp.bfloat16)
    by_cluster = rounded.reshape(vec_count, local_count, leaf_size)
    coarse = jnp.einsum(
        "cki,vci->cvk", leaf_basis, by_cluster, preferred_element_type=jnp.float32
    ).astype(jnp.bfloat16)
    own_rows = coarse.reshape(1, local_count, vec_count * rank_width)
    by_leaf, leaf_xor = xor_gather(own_rows, "leaf", 0)
    window, coef_xor = xor_gather(by_leaf, "coef", 1)
    flat_rows = window.reshape(-1, vec_count * rank_width)
    source_group = far_list // group_size
    source_holder = (far_list % group_size) // local_count
    if leaf_xor:
        source_group = source_group ^ lax.axis_index("leaf")
    if coef_xor:
        source_holder = source_holder ^ lax.axis_index("coef")
    local_ids = (
        source_group * group_size + source_holder * local_count + far_list % local_count
    ).reshape(-1)
    sources = flat_rows.at[local_ids].get(mode="promise_in_bounds").reshape(
        group_size, slot_count, vec_count, rank_width
    )
    lane_ids = jnp.arange(rank_width, dtype=jnp.int32)
    keep_mask = lane_ids[None, None, :] < far_rank[:, :, None]
    sources = jnp.where(keep_mask[:, :, None, :], sources, jnp.zeros((), jnp.bfloat16))
    lane_width = 128
    halves = lane_width // rank_width
    tiles = rank_width // halves
    lane_half = jnp.arange(lane_width, dtype=jnp.int32) // rank_width
    spread = jnp.where(
        (lane_half[:, None] == jnp.arange(halves, dtype=jnp.int32)[None, :])[None, None, :, :, None],
        jnp.tile(jnp.swapaxes(sources, 2, 3), (1, 1, halves, 1))[:, :, :, None, :],
        jnp.zeros((), jnp.bfloat16),
    ).reshape(group_size, slot_count, lane_width, halves * vec_count)
    spread = jnp.broadcast_to(spread[None], (3, *spread.shape))
    couple = coupling.reshape(3, group_size, slot_count, tiles, lane_width)
    far_terms = jnp.einsum("jcfhL,jcfLw->jcfhw", couple, spread, preferred_element_type=jnp.float32)
    far_terms = far_terms.reshape(3, group_size, slot_count, tiles, halves, vec_count)
    weights = powers[:, None, None, None, None, None] * keep_mask.reshape(
        1, group_size, slot_count, tiles, halves, 1
    ).astype(jnp.float32)
    partial_far = jnp.transpose(
        jnp.sum(far_terms * weights, axis=(0, 2)), (0, 3, 1, 2)
    ).reshape(group_size, vec_count, rank_width)
    far_hat = butterfly_scatter(partial_far, "coef")
    far_round = far_hat.astype(jnp.bfloat16).reshape(local_count, vec_count, rank_width)
    far_part = jnp.einsum("cki,cvk->vci", leaf_basis, far_round, preferred_element_type=jnp.float32)
    extended = extended_2(rounded, ((("leaf", "coef"), 1),), local_count * leaf_size)
    extended = extended.reshape(vec_count, 3 * local_count, leaf_size)
    device_pos = lax.axis_index("leaf") * coef_count + lax.axis_index("coef")
    near_ids = (near_list - (device_pos - 1) * local_count).reshape(-1)
    near_src = extended.at[:, near_ids].get(mode="promise_in_bounds").reshape(
        vec_count, local_count, near_count, leaf_size
    )
    near_terms = jnp.einsum(
        "jcnil,vcnl->jvci", near_blocks, near_src, preferred_element_type=jnp.float32
    )
    near_part = jnp.tensordot(powers, near_terms, 1)
    applied = (far_part + near_part).reshape(vec_count, local_count * leaf_size)
    basis_count = krylov.shape[0]
    both_axes = ("leaf", "coef")
    proj_part = jnp.dot(krylov, applied.T, precision=highest)
    self_part = jnp.dot(applied, applied.T, precision=highest)
    summed = butterfly_sum(jnp.concatenate([proj_part, self_part], axis=0), both_axes)
    coeffs = summed[:basis_count]
    outer = summed[basis_count:]
    residue = applied - jnp.dot(coeffs.T, krylov, precision=highest)
    short_gram = (outer - jnp.dot(coeffs.T, coeffs, precision=highest)) / total_points
    eye = jnp.eye(vec_count, dtype=jnp.bool_)
    short_diag = jnp.sum(jnp.where(eye, short_gram, 0.0), axis=0)
    outer_diag = jnp.sum(jnp.where(eye, outer, 0.0), axis=0)
    kept = short_diag * (64 * total_points) >= outer_diag
    def exact_gram():
        part = jnp.dot(residue, residue.T, precision=highest)
        return butterfly_sum(part, both_axes) / total_points
    gram_matrix = lax.cond(jnp.all(kept), lambda: short_gram, exact_gram)
    chol_factor, new_block = chol_solve(gram_matrix, residue)
    return (new_block, coeffs, chol_factor)


def solution(mesh):
    in_specs = (
        P(None, ("leaf", "coef")),
        P(),
        P(("leaf", "coef"), None, None),
        P(None, ("leaf", "coef"), None, None, None),
        P(("leaf", "coef"), None),
        P(None, "leaf", "coef", None),
        P("leaf", "coef"),
        P("leaf", "coef"),
        P(None, ("leaf", "coef")),
    )
    out_specs = (P(None, ("leaf", "coef")), P(), P())
    return jax.shard_map(
        on_device, mesh=mesh, in_specs=in_specs, out_specs=out_specs, check_vma=False
    )
```

```python
import jax
import jax.numpy as jnp
from jax import lax
from jax.experimental import pallas as pl
from jax.experimental.pallas import tpu as pltpu
from jax.sharding import PartitionSpec as P


def shifted(block, axis, distance):
    devices = range(lax.axis_size(axis))
    route = [(i - distance, i) for i in devices if i - distance in devices]
    return lax.ppermute(block, axis, route)


def extended_2(block, sides, width):
    for axis, dim in sides:
        count = lax.axis_size(axis)
        forward = [(i, i + 1) for i in range(count - 1)]
        backward = [(target, source) for source, target in forward]
        low = lax.ppermute(
            lax.slice_in_dim(block, block.shape[dim] - width, None, axis=dim), axis, forward
        )
        high = lax.ppermute(lax.slice_in_dim(block, 0, width, axis=dim), axis, backward)
        block = jnp.concatenate([low, block, high], axis=dim)
    return block


def is_power_of_two(count):
    return count > 0 and count & (count - 1) == 0


def butterfly_sum(block, axes):
    total = 1
    for axis in axes:
        total *= lax.axis_size(axis)
    if not is_power_of_two(total):
        return lax.psum(block, axes)
    distance = 1
    while distance < total:
        route = [(i, i ^ distance) for i in range(total)]
        block = block + lax.ppermute(block, axes, route)
        distance *= 2
    return block


def xor_gather(block, axis, dim):
    count = lax.axis_size(axis)
    if not is_power_of_two(count):
        return lax.all_gather(block, axis, axis=dim, tiled=True), False
    distance = 1
    while distance < count:
        route = [(i, i ^ distance) for i in range(count)]
        block = jnp.concatenate([block, lax.ppermute(block, axis, route)], axis=dim)
        distance *= 2
    return block, True


def butterfly_scatter(block, axis):
    count = lax.axis_size(axis)
    if not is_power_of_two(count):
        return lax.psum_scatter(block, axis, scatter_dimension=0, tiled=True)
    me = lax.axis_index(axis)
    parts = block
    distance = count // 2
    while distance >= 1:
        halves = parts.reshape(2, parts.shape[0] // 2, *parts.shape[1:])
        bit = (me // distance) % 2
        keep = lax.dynamic_index_in_dim(halves, bit, axis=0, keepdims=False)
        give = lax.dynamic_index_in_dim(halves, 1 - bit, axis=0, keepdims=False)
        route = [(i, i ^ distance) for i in range(count)]
        parts = keep + lax.ppermute(give, axis, route)
        distance //= 2
    return parts


def group_reach(grouped, offsets):
    pieces = []
    for offset in offsets:
        if offset == 0:
            pieces.append(grouped)
        else:
            pieces.append(shifted(grouped, "leaf", -offset))
    return jnp.concatenate(pieces, axis=0)


def chol_solve_kernel(gram_ref, residue_ref, chol_ref, block_ref):
    left = gram_ref[...]
    size = left.shape[0]
    rows = lax.broadcasted_iota(jnp.int32, left.shape, 0)
    cols = lax.broadcasted_iota(jnp.int32, left.shape, 1)
    row_ids = lax.broadcasted_iota(jnp.int32, (size, 1), 0)
    col_ids = lax.broadcasted_iota(jnp.int32, (1, size), 1)
    low = jnp.zeros_like(left)
    for step in range(size):
        column = jnp.sum(jnp.where(cols == step, left, 0.0), axis=1, keepdims=True)
        row = jnp.sum(jnp.where(rows == step, left, 0.0), axis=0, keepdims=True)
        pivot = jnp.sum(jnp.where(row_ids == step, column, 0.0), axis=0, keepdims=True)
        root = jnp.sqrt(pivot)
        low_column = jnp.where(row_ids >= step, column / root, 0.0)
        low_row = jnp.where(col_ids >= step, row / root, 0.0)
        low = jnp.where(cols == step, low_column, low)
        left = left - low_column * low_row
    chol_ref[...] = low
    block = residue_ref[...]
    for step in range(size):
        low_column = jnp.sum(jnp.where(cols == step, low, 0.0), axis=1, keepdims=True)
        diagonal = jnp.sum(jnp.where(row_ids == step, low_column, 0.0), axis=0, keepdims=True)
        solved = jnp.sum(jnp.where(row_ids == step, block, 0.0), axis=0, keepdims=True) / diagonal
        block = jnp.where(
            row_ids == step, solved, jnp.where(row_ids > step, block - low_column * solved, block)
        )
    block_ref[...] = block


def chol_solve(gram_matrix, residue):
    size, width = residue.shape
    return pl.pallas_call(
        chol_solve_kernel,
        out_shape=(
            jax.ShapeDtypeStruct((size, size), jnp.float32),
            jax.ShapeDtypeStruct((size, width), jnp.float32),
        ),
        in_specs=[pl.BlockSpec(memory_space=pltpu.VMEM)] * 2,
        out_specs=(pl.BlockSpec(memory_space=pltpu.VMEM), pl.BlockSpec(memory_space=pltpu.VMEM)),
        cost_estimate=pl.CostEstimate(
            flops=4 * size * size * (size + width), bytes_accessed=8 * size * (size + width), transcendentals=size
        ),
    )(gram_matrix, residue)


def on_device(
    vectors, sigma_point, leaf_basis, near_blocks, near_list, coupling, far_list, far_rank, krylov
):
    highest = lax.Precision.HIGHEST
    local_count, rank_width, leaf_size = leaf_basis.shape
    vec_count = vectors.shape[0]
    near_count = near_list.shape[1]
    slot_count = far_list.shape[1]
    coef_count = lax.axis_size("coef")
    leaf_count = lax.axis_size("leaf")
    group_size = local_count * coef_count
    reach_groups = min(8, leaf_count // 4)
    total_points = local_count * leaf_size * coef_count * leaf_count
    sigma_val = sigma_point[0]
    powers = jnp.stack([jnp.ones((), jnp.float32), sigma_val, sigma_val * sigma_val])
    rounded = vectors.astype(jnp.bfloat16)
    by_cluster = rounded.reshape(vec_count, local_count, leaf_size)
    coarse = jnp.einsum(
        "cki,vci->cvk", leaf_basis, by_cluster, preferred_element_type=jnp.float32
    ).astype(jnp.bfloat16)
    own_rows = coarse.reshape(1, local_count, vec_count * rank_width)
    by_leaf, leaf_xor = xor_gather(own_rows, "leaf", 0)
    window, coef_xor = xor_gather(by_leaf, "coef", 1)
    flat_rows = window.reshape(-1, vec_count * rank_width)
    source_group = far_list // group_size
    source_holder = (far_list % group_size) // local_count
    if leaf_xor:
        source_group = source_group ^ lax.axis_index("leaf")
    if coef_xor:
        source_holder = source_holder ^ lax.axis_index("coef")
    local_ids = (
        source_group * group_size + source_holder * local_count + far_list % local_count
    ).reshape(-1)
    sources = flat_rows.at[local_ids].get(mode="promise_in_bounds").reshape(
        group_size, slot_count, vec_count, rank_width
    )
    lane_ids = jnp.arange(rank_width, dtype=jnp.int32)
    keep_mask = lane_ids[None, None, :] < far_rank[:, :, None]
    sources = jnp.where(keep_mask[:, :, None, :], sources, jnp.zeros((), jnp.bfloat16))
    couple = coupling.reshape(3, group_size, slot_count, rank_width, rank_width)
    far_terms = jnp.einsum("cfvl,jcfkl->cfvjk", sources, couple, preferred_element_type=jnp.float32)
    weights = powers[None, None, None, :, None] * keep_mask[:, :, None, None, :].astype(jnp.float32)
    partial_far = jnp.sum(far_terms * weights, axis=(1, 3))
    far_hat = butterfly_scatter(partial_far, "coef")
    far_round = far_hat.astype(jnp.bfloat16).reshape(local_count, vec_count, rank_width)
    far_part = jnp.einsum("cki,cvk->vci", leaf_basis, far_round, preferred_element_type=jnp.float32)
    extended = extended_2(rounded, ((("leaf", "coef"), 1),), local_count * leaf_size)
    extended = extended.reshape(vec_count, 3 * local_count, leaf_size)
    device_pos = lax.axis_index("leaf") * coef_count + lax.axis_index("coef")
    near_ids = (near_list - (device_pos - 1) * local_count).reshape(-1)
    near_src = extended.at[:, near_ids].get(mode="promise_in_bounds").reshape(
        vec_count, local_count, near_count, leaf_size
    )
    near_terms = jnp.einsum(
        "jcnil,vcnl->jvci", near_blocks, near_src, preferred_element_type=jnp.float32
    )
    near_part = jnp.tensordot(powers, near_terms, 1)
    applied = (far_part + near_part).reshape(vec_count, local_count * leaf_size)
    basis_count = krylov.shape[0]
    both_axes = ("leaf", "coef")
    proj_part = jnp.dot(krylov, applied.T, precision=highest)
    self_part = jnp.dot(applied, applied.T, precision=highest)
    summed = butterfly_sum(jnp.concatenate([proj_part, self_part], axis=0), both_axes)
    coeffs = summed[:basis_count]
    outer = summed[basis_count:]
    residue = applied - jnp.dot(coeffs.T, krylov, precision=highest)
    short_gram = (outer - jnp.dot(coeffs.T, coeffs, precision=highest)) / total_points
    eye = jnp.eye(vec_count, dtype=jnp.bool_)
    outer_diag = jnp.sum(jnp.where(eye, outer, 0.0), axis=0)
    kept = (outer_diag - jnp.sum(coeffs * coeffs, axis=0)) * 64 >= outer_diag
    def exact_gram():
        part = jnp.dot(residue, residue.T, precision=highest)
        return butterfly_sum(part, both_axes) / total_points
    gram_matrix = lax.cond(jnp.all(kept), lambda: short_gram, exact_gram)
    chol_factor, new_block = chol_solve(gram_matrix, residue)
    return (new_block, coeffs, chol_factor)


def solution(mesh):
    in_specs = (
        P(None, ("leaf", "coef")),
        P(),
        P(("leaf", "coef"), None, None),
        P(None, ("leaf", "coef"), None, None, None),
        P(("leaf", "coef"), None),
        P(None, "leaf", "coef", None),
        P("leaf", "coef"),
        P("leaf", "coef"),
        P(None, ("leaf", "coef")),
    )
    out_specs = (P(None, ("leaf", "coef")), P(), P())
    return jax.shard_map(
        on_device, mesh=mesh, in_specs=in_specs, out_specs=out_specs, check_vma=False
    )
```

```python
import jax
import jax.numpy as jnp
from jax import lax
from jax.experimental import pallas as pl
from jax.experimental.pallas import tpu as pltpu
from jax.sharding import PartitionSpec as P


def shifted(block, axis, distance):
    devices = range(lax.axis_size(axis))
    route = [(i - distance, i) for i in devices if i - distance in devices]
    return lax.ppermute(block, axis, route)


def extended_2(block, sides, width):
    for axis, dim in sides:
        count = lax.axis_size(axis)
        forward = [(i, i + 1) for i in range(count - 1)]
        backward = [(target, source) for source, target in forward]
        low = lax.ppermute(
            lax.slice_in_dim(block, block.shape[dim] - width, None, axis=dim), axis, forward
        )
        high = lax.ppermute(lax.slice_in_dim(block, 0, width, axis=dim), axis, backward)
        block = jnp.concatenate([low, block, high], axis=dim)
    return block


def is_power_of_two(count):
    return count > 0 and count & (count - 1) == 0


def butterfly_sum(block, axes):
    total = 1
    for axis in axes:
        total *= lax.axis_size(axis)
    if not is_power_of_two(total):
        return lax.psum(block, axes)
    distance = 1
    while distance < total:
        route = [(i, i ^ distance) for i in range(total)]
        block = block + lax.ppermute(block, axes, route)
        distance *= 2
    return block


def xor_gather(block, axis, dim):
    count = lax.axis_size(axis)
    if not is_power_of_two(count):
        return lax.all_gather(block, axis, axis=dim, tiled=True), False
    distance = 1
    while distance < count:
        route = [(i, i ^ distance) for i in range(count)]
        block = jnp.concatenate([block, lax.ppermute(block, axis, route)], axis=dim)
        distance *= 2
    return block, True


def butterfly_scatter(block, axis):
    count = lax.axis_size(axis)
    if not is_power_of_two(count):
        return lax.psum_scatter(block, axis, scatter_dimension=0, tiled=True)
    me = lax.axis_index(axis)
    parts = block
    distance = count // 2
    while distance >= 1:
        halves = parts.reshape(2, parts.shape[0] // 2, *parts.shape[1:])
        bit = (me // distance) % 2
        keep = lax.dynamic_index_in_dim(halves, bit, axis=0, keepdims=False)
        give = lax.dynamic_index_in_dim(halves, 1 - bit, axis=0, keepdims=False)
        route = [(i, i ^ distance) for i in range(count)]
        parts = keep + lax.ppermute(give, axis, route)
        distance //= 2
    return parts


def group_reach(grouped, offsets):
    pieces = []
    for offset in offsets:
        if offset == 0:
            pieces.append(grouped)
        else:
            pieces.append(shifted(grouped, "leaf", -offset))
    return jnp.concatenate(pieces, axis=0)


def chol_solve_kernel(gram_ref, residue_ref, chol_ref, block_ref):
    left = gram_ref[...]
    size = left.shape[0]
    rows = lax.broadcasted_iota(jnp.int32, left.shape, 0)
    cols = lax.broadcasted_iota(jnp.int32, left.shape, 1)
    row_ids = lax.broadcasted_iota(jnp.int32, (size, 1), 0)
    col_ids = lax.broadcasted_iota(jnp.int32, (1, size), 1)
    low = jnp.zeros_like(left)
    for step in range(size):
        column = jnp.sum(jnp.where(cols == step, left, 0.0), axis=1, keepdims=True)
        row = jnp.sum(jnp.where(rows == step, left, 0.0), axis=0, keepdims=True)
        pivot = jnp.sum(jnp.where(row_ids == step, column, 0.0), axis=0, keepdims=True)
        root = jnp.sqrt(pivot)
        low_column = jnp.where(row_ids >= step, column / root, 0.0)
        low_row = jnp.where(col_ids >= step, row / root, 0.0)
        low = jnp.where(cols == step, low_column, low)
        left = left - low_column * low_row
    chol_ref[...] = low
    block = jnp.where(rows == cols, 1.0, 0.0)
    for step in range(size):
        low_column = jnp.sum(jnp.where(cols == step, low, 0.0), axis=1, keepdims=True)
        diagonal = jnp.sum(jnp.where(row_ids == step, low_column, 0.0), axis=0, keepdims=True)
        solved = jnp.sum(jnp.where(row_ids == step, block, 0.0), axis=0, keepdims=True) / diagonal
        block = jnp.where(
            row_ids == step, solved, jnp.where(row_ids > step, block - low_column * solved, block)
        )
    block_ref[...] = jnp.dot(block, residue_ref[...], precision=lax.Precision.HIGHEST)


def chol_solve(gram_matrix, residue):
    size, width = residue.shape
    return pl.pallas_call(
        chol_solve_kernel,
        out_shape=(
            jax.ShapeDtypeStruct((size, size), jnp.float32),
            jax.ShapeDtypeStruct((size, width), jnp.float32),
        ),
        in_specs=[pl.BlockSpec(memory_space=pltpu.VMEM)] * 2,
        out_specs=(pl.BlockSpec(memory_space=pltpu.VMEM), pl.BlockSpec(memory_space=pltpu.VMEM)),
        cost_estimate=pl.CostEstimate(
            flops=4 * size * size * (size + width), bytes_accessed=8 * size * (size + width), transcendentals=size
        ),
    )(gram_matrix, residue)


def on_device(
    vectors, sigma_point, leaf_basis, near_blocks, near_list, coupling, far_list, far_rank, krylov
):
    highest = lax.Precision.HIGHEST
    local_count, rank_width, leaf_size = leaf_basis.shape
    vec_count = vectors.shape[0]
    near_count = near_list.shape[1]
    slot_count = far_list.shape[1]
    coef_count = lax.axis_size("coef")
    leaf_count = lax.axis_size("leaf")
    group_size = local_count * coef_count
    reach_groups = min(8, leaf_count // 4)
    total_points = local_count * leaf_size * coef_count * leaf_count
    sigma_val = sigma_point[0]
    powers = jnp.stack([jnp.ones((), jnp.float32), sigma_val, sigma_val * sigma_val])
    rounded = vectors.astype(jnp.bfloat16)
    by_cluster = rounded.reshape(vec_count, local_count, leaf_size)
    coarse = jnp.einsum(
        "cki,vci->cvk", leaf_basis, by_cluster, preferred_element_type=jnp.float32
    ).astype(jnp.bfloat16)
    own_rows = coarse.reshape(1, local_count, vec_count * rank_width)
    by_leaf, leaf_xor = xor_gather(own_rows, "leaf", 0)
    window, coef_xor = xor_gather(by_leaf, "coef", 1)
    flat_rows = window.reshape(-1, vec_count * rank_width)
    source_group = far_list // group_size
    source_holder = (far_list % group_size) // local_count
    if leaf_xor:
        source_group = source_group ^ lax.axis_index("leaf")
    if coef_xor:
        source_holder = source_holder ^ lax.axis_index("coef")
    local_ids = (
        source_group * group_size + source_holder * local_count + far_list % local_count
    ).reshape(-1)
    sources = flat_rows.at[local_ids].get(mode="promise_in_bounds").reshape(
        group_size, slot_count, vec_count, rank_width
    )
    lane_ids = jnp.arange(rank_width, dtype=jnp.int32)
    keep_mask = lane_ids[None, None, :] < far_rank[:, :, None]
    sources = jnp.where(keep_mask[:, :, None, :], sources, jnp.zeros((), jnp.bfloat16))
    couple = coupling.reshape(3, group_size, slot_count, rank_width, rank_width)
    far_terms = jnp.einsum("cfvl,jcfkl->cfvjk", sources, couple, preferred_element_type=jnp.float32)
    weights = powers[None, None, None, :, None] * keep_mask[:, :, None, None, :].astype(jnp.float32)
    partial_far = jnp.sum(far_terms * weights, axis=(1, 3))
    far_hat = butterfly_scatter(partial_far, "coef")
    far_round = far_hat.astype(jnp.bfloat16).reshape(local_count, vec_count, rank_width)
    far_part = jnp.einsum("cki,cvk->vci", leaf_basis, far_round, preferred_element_type=jnp.float32)
    extended = extended_2(rounded, ((("leaf", "coef"), 1),), local_count * leaf_size)
    extended = extended.reshape(vec_count, 3 * local_count, leaf_size)
    device_pos = lax.axis_index("leaf") * coef_count + lax.axis_index("coef")
    near_ids = (near_list - (device_pos - 1) * local_count).reshape(-1)
    near_src = extended.at[:, near_ids].get(mode="promise_in_bounds").reshape(
        vec_count, local_count, near_count, leaf_size
    )
    near_terms = jnp.einsum(
        "jcnil,vcnl->jvci", near_blocks, near_src, preferred_element_type=jnp.float32
    )
    near_part = jnp.tensordot(powers, near_terms, 1)
    applied = (far_part + near_part).reshape(vec_count, local_count * leaf_size)
    basis_count = krylov.shape[0]
    both_axes = ("leaf", "coef")
    proj_part = jnp.dot(krylov, applied.T, precision=highest)
    self_part = jnp.dot(applied, applied.T, precision=highest)
    summed = butterfly_sum(jnp.concatenate([proj_part, self_part], axis=0), both_axes)
    coeffs = summed[:basis_count]
    outer = summed[basis_count:]
    residue = applied - jnp.dot(coeffs.T, krylov, precision=highest)
    short_gram = (outer - jnp.dot(coeffs.T, coeffs, precision=highest)) / total_points
    eye = jnp.eye(vec_count, dtype=jnp.bool_)
    short_diag = jnp.sum(jnp.where(eye, short_gram, 0.0), axis=0)
    outer_diag = jnp.sum(jnp.where(eye, outer, 0.0), axis=0)
    kept = short_diag * (64 * total_points) >= outer_diag
    def exact_gram():
        part = jnp.dot(residue, residue.T, precision=highest)
        return butterfly_sum(part, both_axes) / total_points
    gram_matrix = lax.cond(jnp.all(kept), lambda: short_gram, exact_gram)
    chol_factor, new_block = chol_solve(gram_matrix, residue)
    return (new_block, coeffs, chol_factor)


def solution(mesh):
    in_specs = (
        P(None, ("leaf", "coef")),
        P(),
        P(("leaf", "coef"), None, None),
        P(None, ("leaf", "coef"), None, None, None),
        P(("leaf", "coef"), None),
        P(None, "leaf", "coef", None),
        P("leaf", "coef"),
        P("leaf", "coef"),
        P(None, ("leaf", "coef")),
    )
    out_specs = (P(None, ("leaf", "coef")), P(), P())
    return jax.shard_map(
        on_device, mesh=mesh, in_specs=in_specs, out_specs=out_specs, check_vma=False
    )
```
